32 devices in a mesh: groups: 2 (over x), freq: 16 (over z, y, core).
Axes of the slice: x: 2, y: 2, z: 4, core: 2. Of those that a mesh axis runs over, the one named last changes fastest.
Arguments:
- encoder_input: bfloat16 [64, 2048], P(('groups', 'freq')), parts along dimension 0, may hold values from -6 to 6
- desired_responses: bfloat16 [64, 384, 512], P('groups', 'freq'), parts along dimension 0, may hold values from -6 to 6
- sample_index: int32 [64], P('groups'), parts along dimension 0, may hold values from 0 to 31, each once
- encoder_weight: bfloat16 [2048, 512], replicated, may hold values from -0.125 to 0.125
- decoder_weight: bfloat16 [512, 512], replicated, may hold values from -0.25 to 0.25
- frequency_amplitude: bfloat16 [384, 512], P('freq'), may hold values from -4 to 4
- spectral_filter_weight: float32 [2, 256], replicated, may hold values from -4 to 4
- output_weight: bfloat16 [512, 512], replicated, may hold values from -0.25 to 0.25
Outputs:
- grad_enc: float32 [4096, 512], P('groups'), parts along dimension 0
- grad_dec: float32 [1024, 512], P('groups'), parts along dimension 0
- grad_out: float32 [1024, 512], P('groups'), parts along dimension 0
- grad_filter: float32 [4, 256], P('groups'), parts along dimension 0
The draws below stay inside these ranges and needn't reach their ends.
There are 2 independent parts, one for each index of `groups`. The reference program is written for one: setup_inputs(seed, part) draws one part's arguments, and reference() takes and returns one part's arrays. A program takes and returns all parts, laid end to end along the dimension named above; an argument that names none is the same for every part. Nothing has to cross between parts.
Inputs may be any that keep to these rules, and one draw needn't show every extreme that they name: sample_index names each of the 32 samples once.
All inputs are finite; a program needn't handle non-finite values.
Results may differ from the reference program's by a relative error of at most 0.0065.
Values may be sent and summed in bfloat16 or wider, within the bound.
No kernel may reach another device: no remote copies, remote signals or barrier semaphores. Data moves between devices by JAX's collectives and lax.ppermute only.
A program may use at most 128 MiB of HBM per device.

```python
import math
import jax
import jax.numpy as jnp
from jax import lax

ANTENNA_COUNT = 256
LINK_COMPONENTS = 512
CODE = 512
ENC_IN = 2048
TONES_PER_CHIPSET = 24
BATCH_USERS = 32
SUBCARRIER_COUNT = 384
N_FREQ = 16


def strengthened(entries, stream_key, source, target, shards_of, factor):
    owner, partner = [(jnp.arange(entries.shape[position]) // (entries.shape[position] // shards_of)).reshape([-1 if axis == position else 1 for axis in range(entries.ndim)]) for position in (source, target)]
    chosen = jax.random.permutation(stream_key, shards_of)[partner]
    strong = (owner == chosen) | (owner == (partner + shards_of // 2) % shards_of)
    return jnp.where(strong, factor * entries, entries)


def block_levels(key, extent, shards, low, high):
    loudness = 1.0
    for axis_at, blocks in shards:
        draws = jax.random.uniform(jax.random.fold_in(jax.random.fold_in(key, 6), axis_at), (blocks,), jnp.float32, low / len(shards), high / len(shards))
        loudness = loudness * jnp.repeat(jnp.exp(draws), extent[axis_at] // blocks).reshape((-1,) + (1,) * (len(extent) - 1 - axis_at))
    return loudness


def scatter_about(rng, shape, spread, reach, shards=(), kind=jnp.bfloat16):
    result = jax.random.normal(rng, shape, jnp.float32) * spread
    if len(shards) > 0:
        result = block_levels(rng, shape, shards, -0.22, 0.18) * result
    return jnp.clip(result, min=-reach, max=reach).astype(kind)


def bell_draw_with(key, dims, deviation, bound, cuts, heavy, kind=jnp.bfloat16):
    array = deviation * jax.random.normal(key, dims, jnp.float32)
    if cuts:
        array = array * block_levels(key, dims, cuts, -0.22, 0.18)
    return jnp.clip(strengthened(array, jax.random.fold_in(key, 3), *heavy), -bound, bound).astype(kind)


def setup_inputs(seed: int = 0, part: int = 0) -> dict:
    splits = jax.random.split(jax.random.key(seed), 9)
    part_keys = jax.random.split(jax.random.fold_in(splits[8], part), 9)
    encoder_input = scatter_about(part_keys[0], (BATCH_USERS, ENC_IN), 1.0, 6.0, ((0, 16),))
    desired_responses = bell_draw_with(part_keys[1], (BATCH_USERS, SUBCARRIER_COUNT, LINK_COMPONENTS), 1.0, 6.0, ((1, 16),), (1, 0, 16, 2.0))
    sample_index = jax.random.permutation(part_keys[2], BATCH_USERS).astype(jnp.int32)
    encoder_weight = scatter_about(splits[3], (ENC_IN, CODE), ENC_IN ** -0.5, 0.125)
    decoder_weight = scatter_about(splits[4], (CODE, LINK_COMPONENTS), CODE ** -0.5, 0.25)
    frequency_amplitude = scatter_about(splits[5], (SUBCARRIER_COUNT, LINK_COMPONENTS), 1.0, 4.0, ((0, 16),))
    spectral_filter_weight = scatter_about(splits[6], (2, ANTENNA_COUNT), 1.0, 4.0, (), jnp.float32)
    output_weight = scatter_about(splits[7], (LINK_COMPONENTS, LINK_COMPONENTS), LINK_COMPONENTS ** -0.5, 0.25)
    return dict(encoder_input=encoder_input, desired_responses=desired_responses, sample_index=sample_index, encoder_weight=encoder_weight, decoder_weight=decoder_weight, frequency_amplitude=frequency_amplitude, spectral_filter_weight=spectral_filter_weight, output_weight=output_weight)


def rotation_tables(antennas):
    indices = jnp.arange(antennas, dtype=jnp.int32)
    products_mod = indices[:, None] * indices[None, :] % antennas
    angle_table = products_mod.astype(jnp.float32) * (2.0 * math.pi / antennas)
    cosine_table = jnp.cos(angle_table) / math.sqrt(antennas)
    sine_table = jnp.sin(angle_table) / math.sqrt(antennas)
    forward_transform = jnp.concatenate([jnp.concatenate([cosine_table, -sine_table], 1), jnp.concatenate([sine_table, cosine_table], 1)], 0)
    inverse_transform = jnp.concatenate([jnp.concatenate([cosine_table, sine_table], 1), jnp.concatenate([-sine_table, cosine_table], 1)], 0)
    return (forward_transform.astype(jnp.bfloat16), inverse_transform.astype(jnp.bfloat16))

def decode_rows(mixed_in, wanted_lines, output_weight, spectral_filter_weight, forward_transform, inverse_transform, loss_scale):
    filter_re = spectral_filter_weight[0]
    filter_im = spectral_filter_weight[1]
    spectrum = jnp.dot(mixed_in, forward_transform, preferred_element_type=jnp.float32)
    half_width = spectrum.shape[1] // 2
    spec_re = spectrum[:, :half_width]
    spec_im = spectrum[:, half_width:]
    filtered = jnp.concatenate([spec_re * filter_re - spec_im * filter_im, spec_re * filter_im + spec_im * filter_re], 1).astype(jnp.bfloat16)
    mixed_back = jnp.dot(filtered, inverse_transform, preferred_element_type=jnp.float32)
    hidden = (mixed_in.astype(jnp.float32) + jax.nn.gelu(mixed_back)).astype(jnp.bfloat16)
    rebuilt = hidden.astype(jnp.float32) + jnp.dot(hidden, output_weight, preferred_element_type=jnp.float32)
    residual = loss_scale * (rebuilt - wanted_lines.astype(jnp.float32))
    residual_half = residual.astype(jnp.bfloat16)
    grad_out = lax.dot_general(hidden, residual_half, (((0,), (0,)), ((), ())), preferred_element_type=jnp.float32)
    grad_hidden = residual + lax.dot_general(residual_half, output_weight, (((1,), (1,)), ((), ())), preferred_element_type=jnp.float32)
    grad_mixed = jax.vjp(jax.nn.gelu, mixed_back)[1](grad_hidden)[0].astype(jnp.bfloat16)
    grad_filtered = lax.dot_general(grad_mixed, inverse_transform, (((1,), (1,)), ((), ())), preferred_element_type=jnp.float32)
    grad_re = grad_filtered[:, :half_width]
    grad_im = grad_filtered[:, half_width:]
    grad_filter = jnp.stack([lax.optimization_barrier(jnp.sum(grad_re * spec_re + grad_im * spec_im, 0)), lax.optimization_barrier(jnp.sum(grad_im * spec_re - grad_re * spec_im, 0))])
    grad_spec = jnp.concatenate([grad_re * filter_re + grad_im * filter_im, grad_im * filter_re - grad_re * filter_im], 1).astype(jnp.bfloat16)
    derivative_entering = grad_hidden + lax.dot_general(grad_spec, forward_transform, (((1,), (1,)), ((), ())), preferred_element_type=jnp.float32)
    return (derivative_entering, grad_out, grad_filter)

def encoder_grads(inputs_rows, codewords, latent_sums, decoder_weight):
    latent_half = latent_sums.astype(jnp.bfloat16)
    grad_dec = lax.dot_general(codewords, latent_half, (((0,), (0,)), ((), ())), preferred_element_type=jnp.float32)
    grad_codes = lax.dot_general(latent_half, decoder_weight, (((1,), (1,)), ((), ())), preferred_element_type=jnp.float32)
    grad_pre = (grad_codes * (1.0 - jnp.square(codewords.astype(jnp.float32)))).astype(jnp.bfloat16)
    grad_enc = lax.dot_general(inputs_rows, grad_pre, (((0,), (0,)), ((), ())), preferred_element_type=jnp.float32)
    return (grad_enc, grad_dec)

def reference(encoder_input, desired_responses, sample_index, encoder_weight, decoder_weight, frequency_amplitude, spectral_filter_weight, output_weight):
    forward_transform, inverse_transform = rotation_tables(ANTENNA_COUNT)
    loss_scale = 1.0 / math.sqrt(BATCH_USERS * SUBCARRIER_COUNT)
    codewords = jnp.tanh(jnp.dot(encoder_input, encoder_weight, preferred_element_type=jnp.float32)).astype(jnp.bfloat16)
    inverse_ids = jnp.zeros((BATCH_USERS,), jnp.int32).at[sample_index].set(jnp.arange(BATCH_USERS, dtype=jnp.int32))
    latent = jnp.dot(codewords[inverse_ids], decoder_weight, preferred_element_type=jnp.float32)

    def scan_step(totals, segment_number):
        leading_position = (segment_number * TONES_PER_CHIPSET).astype(jnp.int32)
        wanted_lines = lax.dynamic_slice_in_dim(desired_responses, leading_position, TONES_PER_CHIPSET, 1).reshape(-1, LINK_COMPONENTS)
        amplitude_piece = lax.dynamic_slice_in_dim(frequency_amplitude, leading_position, TONES_PER_CHIPSET, 0).astype(jnp.float32)
        mixed_in = (latent[:, None, :] * amplitude_piece[None]).astype(jnp.bfloat16).reshape(-1, LINK_COMPONENTS)
        derivative_entering, grad_out, grad_filter = decode_rows(mixed_in, wanted_lines, output_weight, spectral_filter_weight, forward_transform, inverse_transform, loss_scale)
        derivative_bottleneck = jnp.einsum('orm,rm->om', derivative_entering.reshape(BATCH_USERS, TONES_PER_CHIPSET, LINK_COMPONENTS), amplitude_piece)
        return ((totals[0] + grad_out, totals[1] + grad_filter, totals[2] + derivative_bottleneck), None)
    empty_sum_buffers = (jnp.zeros((LINK_COMPONENTS, LINK_COMPONENTS), jnp.float32), jnp.zeros((2, ANTENNA_COUNT), jnp.float32), jnp.zeros((BATCH_USERS, LINK_COMPONENTS), jnp.float32))
    sums_out, _ = lax.scan(scan_step, empty_sum_buffers, jnp.arange(N_FREQ, dtype=jnp.int32))
    grad_out, grad_filter, derivative_bottleneck = sums_out
    grad_enc, grad_dec = encoder_grads(encoder_input, codewords, derivative_bottleneck[sample_index], decoder_weight)
    return (grad_enc, grad_dec, grad_out, grad_filter)
```

```python
import math

import jax
import jax.numpy as jnp
from jax import lax
from jax.sharding import PartitionSpec as P


def rotation_tables(antennas):
    indices = jnp.arange(antennas, dtype=jnp.int32)
    products_mod = indices[:, None] * indices[None, :] % antennas
    angle_table = products_mod.astype(jnp.float32) * (2.0 * math.pi / antennas)
    cosine_table = jnp.cos(angle_table) / math.sqrt(antennas)
    sine_table = jnp.sin(angle_table) / math.sqrt(antennas)
    forward_transform = jnp.concatenate(
        [
            jnp.concatenate([cosine_table, -sine_table], 1),
            jnp.concatenate([sine_table, cosine_table], 1),
        ],
        0,
    )
    inverse_transform = jnp.concatenate(
        [
            jnp.concatenate([cosine_table, sine_table], 1),
            jnp.concatenate([-sine_table, cosine_table], 1),
        ],
        0,
    )
    return (forward_transform.astype(jnp.bfloat16), inverse_transform.astype(jnp.bfloat16))


def decode_rows(
    mixed_in,
    wanted_lines,
    output_weight,
    spectral_filter_weight,
    forward_transform,
    inverse_transform,
    loss_scale,
):
    filter_re = spectral_filter_weight[0]
    filter_im = spectral_filter_weight[1]
    spectrum = jnp.dot(mixed_in, forward_transform, preferred_element_type=jnp.float32)
    half_width = spectrum.shape[1] // 2
    spec_re = spectrum[:, :half_width]
    spec_im = spectrum[:, half_width:]
    filtered = jnp.concatenate(
        [spec_re * filter_re - spec_im * filter_im, spec_re * filter_im + spec_im * filter_re], 1
    ).astype(jnp.bfloat16)
    mixed_back = jnp.dot(filtered, inverse_transform, preferred_element_type=jnp.float32)
    hidden = (mixed_in.astype(jnp.float32) + jax.nn.gelu(mixed_back)).astype(jnp.bfloat16)
    rebuilt = hidden.astype(jnp.float32) + jnp.dot(
        hidden, output_weight, preferred_element_type=jnp.float32
    )
    residual = loss_scale * (rebuilt - wanted_lines.astype(jnp.float32))
    residual_half = residual.astype(jnp.bfloat16)
    grad_out = lax.dot_general(
        hidden, residual_half, (((0,), (0,)), ((), ())), preferred_element_type=jnp.float32
    )
    grad_hidden = residual + lax.dot_general(
        residual_half, output_weight, (((1,), (1,)), ((), ())), preferred_element_type=jnp.float32
    )
    grad_mixed = jax.vjp(jax.nn.gelu, mixed_back)[1](grad_hidden)[0].astype(jnp.bfloat16)
    grad_filtered = lax.dot_general(
        grad_mixed, inverse_transform, (((1,), (1,)), ((), ())), preferred_element_type=jnp.float32
    )
    grad_re = grad_filtered[:, :half_width]
    grad_im = grad_filtered[:, half_width:]
    grad_filter = jnp.stack(
        [
            jnp.sum(grad_re * spec_re + grad_im * spec_im, 0),
            jnp.sum(grad_im * spec_re - grad_re * spec_im, 0),
        ]
    )
    grad_spec = jnp.concatenate(
        [grad_re * filter_re + grad_im * filter_im, grad_im * filter_re - grad_re * filter_im], 1
    ).astype(jnp.bfloat16)
    derivative_entering = grad_hidden + lax.dot_general(
        grad_spec, forward_transform, (((1,), (1,)), ((), ())), preferred_element_type=jnp.float32
    )
    return (derivative_entering, grad_out, grad_filter)


def encoder_grads(inputs_rows, codewords, latent_sums, decoder_weight):
    latent_half = latent_sums.astype(jnp.bfloat16)
    grad_dec = lax.dot_general(
        codewords, latent_half, (((0,), (0,)), ((), ())), preferred_element_type=jnp.float32
    )
    grad_codes = lax.dot_general(
        latent_half, decoder_weight, (((1,), (1,)), ((), ())), preferred_element_type=jnp.float32
    )
    grad_pre = (grad_codes * (1.0 - jnp.square(codewords.astype(jnp.float32)))).astype(jnp.bfloat16)
    grad_enc = lax.dot_general(
        inputs_rows, grad_pre, (((0,), (0,)), ((), ())), preferred_element_type=jnp.float32
    )
    return (grad_enc, grad_dec)


def local(
    encoder_input,
    desired_responses,
    sample_index,
    encoder_weight,
    decoder_weight,
    frequency_amplitude,
    spectral_filter_weight,
    output_weight,
):
    samples = sample_index.shape[0]
    sub_dev = desired_responses.shape[1]
    width = desired_responses.shape[2]
    forward_transform, inverse_transform = rotation_tables(width // 2)
    loss_scale = 1.0 / math.sqrt(samples * sub_dev * lax.axis_size("freq"))
    all_inputs = lax.all_gather(encoder_input, "freq", axis=0, tiled=True)
    codes = jnp.tanh(
        jnp.dot(all_inputs, encoder_weight, preferred_element_type=jnp.float32)
    ).astype(jnp.bfloat16)
    inverse_ids = (
        jnp.zeros((samples,), jnp.int32).at[sample_index].set(jnp.arange(samples, dtype=jnp.int32))
    )
    latent = jnp.dot(codes[inverse_ids], decoder_weight, preferred_element_type=jnp.float32)
    gain_row_values = frequency_amplitude.astype(jnp.float32)
    mixed_in = (latent[:, None, :] * gain_row_values[None]).astype(jnp.bfloat16).reshape(-1, width)
    wanted_lines = desired_responses.reshape(-1, width)
    derivative_entering, grad_out, grad_filter = decode_rows(
        mixed_in,
        wanted_lines,
        output_weight,
        spectral_filter_weight,
        forward_transform,
        inverse_transform,
        loss_scale,
    )
    derivative_bottleneck = jnp.einsum(
        "orm,rm->om", derivative_entering.reshape(samples, sub_dev, width), gain_row_values
    )
    derivative_bottleneck, grad_out, grad_filter = lax.psum(
        (derivative_bottleneck, grad_out, grad_filter), "freq"
    )
    grad_enc, grad_dec = encoder_grads(
        all_inputs, codes, derivative_bottleneck[sample_index], decoder_weight
    )
    return (grad_enc, grad_dec, grad_out, grad_filter)


def solution(mesh):
    return jax.shard_map(
        local,
        mesh=mesh,
        in_specs=(
            P(("groups", "freq"), None),
            P("groups", "freq", None),
            P("groups"),
            P(),
            P(),
            P("freq", None),
            P(),
            P(),
        ),
        out_specs=(P("groups", None), P("groups", None), P("groups", None), P("groups", None)),
        check_vma=False,
    )
```

```python
import math

import jax
import jax.numpy as jnp
from jax import lax
from jax.sharding import PartitionSpec as P


def rotation_tables(antennas):
    indices = jnp.arange(antennas, dtype=jnp.int32)
    products_mod = indices[:, None] * indices[None, :] % antennas
    angle_table = products_mod.astype(jnp.float32) * (2.0 * math.pi / antennas)
    cosine_table = jnp.cos(angle_table) / math.sqrt(antennas)
    sine_table = jnp.sin(angle_table) / math.sqrt(antennas)
    forward_transform = jnp.concatenate(
        [
            jnp.concatenate([cosine_table, -sine_table], 1),
            jnp.concatenate([sine_table, cosine_table], 1),
        ],
        0,
    )
    inverse_transform = jnp.concatenate(
        [
            jnp.concatenate([cosine_table, sine_table], 1),
            jnp.concatenate([-sine_table, cosine_table], 1),
        ],
        0,
    )
    return (forward_transform.astype(jnp.bfloat16), inverse_transform.astype(jnp.bfloat16))


def decode_rows(
    mixed_in,
    wanted_lines,
    output_weight,
    spectral_filter_weight,
    forward_transform,
    inverse_transform,
    loss_scale,
):
    filter_re = spectral_filter_weight[0]
    filter_im = spectral_filter_weight[1]
    spectrum = jnp.dot(mixed_in, forward_transform, preferred_element_type=jnp.float32)
    half_width = spectrum.shape[1] // 2
    spec_re = spectrum[:, :half_width]
    spec_im = spectrum[:, half_width:]
    filtered = jnp.concatenate(
        [spec_re * filter_re - spec_im * filter_im, spec_re * filter_im + spec_im * filter_re], 1
    ).astype(jnp.bfloat16)
    mixed_back = jnp.dot(filtered, inverse_transform, preferred_element_type=jnp.float32)
    hidden = (mixed_in.astype(jnp.float32) + jax.nn.gelu(mixed_back)).astype(jnp.bfloat16)
    rebuilt = hidden.astype(jnp.float32) + jnp.dot(
        hidden, output_weight, preferred_element_type=jnp.float32
    )
    residual = loss_scale * (rebuilt - wanted_lines.astype(jnp.float32))
    residual_half = residual.astype(jnp.bfloat16)
    grad_out = lax.dot_general(
        hidden, residual_half, (((0,), (0,)), ((), ())), preferred_element_type=jnp.float32
    )
    grad_hidden = residual + lax.dot_general(
        residual_half, output_weight, (((1,), (1,)), ((), ())), preferred_element_type=jnp.float32
    )
    grad_mixed = jax.vjp(jax.nn.gelu, mixed_back)[1](grad_hidden)[0].astype(jnp.bfloat16)
    grad_filtered = lax.dot_general(
        grad_mixed, inverse_transform, (((1,), (1,)), ((), ())), preferred_element_type=jnp.float32
    )
    grad_re = grad_filtered[:, :half_width]
    grad_im = grad_filtered[:, half_width:]
    grad_filter = jnp.stack(
        [
            jnp.sum(grad_re * spec_re + grad_im * spec_im, 0),
            jnp.sum(grad_im * spec_re - grad_re * spec_im, 0),
        ]
    )
    grad_spec = jnp.concatenate(
        [grad_re * filter_re + grad_im * filter_im, grad_im * filter_re - grad_re * filter_im], 1
    ).astype(jnp.bfloat16)
    derivative_entering = grad_hidden + lax.dot_general(
        grad_spec, forward_transform, (((1,), (1,)), ((), ())), preferred_element_type=jnp.float32
    )
    return (derivative_entering, grad_out, grad_filter)


def encoder_grads(inputs_rows, codewords, latent_sums, decoder_weight):
    latent_half = latent_sums.astype(jnp.bfloat16)
    grad_dec = lax.dot_general(
        codewords, latent_half, (((0,), (0,)), ((), ())), preferred_element_type=jnp.float32
    )
    grad_codes = lax.dot_general(
        latent_half, decoder_weight, (((1,), (1,)), ((), ())), preferred_element_type=jnp.float32
    )
    grad_pre = (grad_codes * (1.0 - jnp.square(codewords.astype(jnp.float32)))).astype(jnp.bfloat16)
    grad_enc = lax.dot_general(
        inputs_rows, grad_pre, (((0,), (0,)), ((), ())), preferred_element_type=jnp.float32
    )
    return (grad_enc, grad_dec)


def _exchange_pairs(count, distance):
    return [(i, i ^ distance) for i in range(count)]


def _is_power_of_two(count):
    return count > 0 and count & (count - 1) == 0


def gather_rows(block, axis_name):
    count = lax.axis_size(axis_name)
    if not _is_power_of_two(count):
        return lax.all_gather(block, axis_name, axis=0, tiled=True)
    position = lax.axis_index(axis_name)
    distance = 1
    while distance < count:
        other = lax.ppermute(block, axis_name, _exchange_pairs(count, distance))
        lower = (position // distance) % 2 == 0
        block = jnp.where(
            lower, jnp.concatenate([block, other], 0), jnp.concatenate([other, block], 0)
        )
        distance *= 2
    return block


def sum_whole(values, axis_name):
    count = lax.axis_size(axis_name)
    if not _is_power_of_two(count):
        return lax.psum(values, axis_name)
    distance = 1
    while distance < count:
        values = values + lax.ppermute(values, axis_name, _exchange_pairs(count, distance))
        distance *= 2
    return values


def sum_halving(values, axis_name):
    count = lax.axis_size(axis_name)
    if not _is_power_of_two(count) or values.shape[0] % count != 0:
        return lax.psum(values, axis_name)
    position = lax.axis_index(axis_name)
    distance = 1
    while distance < count:
        half = values.shape[0] // 2
        lower = (position // distance) % 2 == 0
        keep = jnp.where(lower, values[:half], values[half:])
        send = jnp.where(lower, values[half:], values[:half])
        values = keep + lax.ppermute(send, axis_name, _exchange_pairs(count, distance))
        distance *= 2
    distance = count // 2
    while distance >= 1:
        other = lax.ppermute(values, axis_name, _exchange_pairs(count, distance))
        lower = (position // distance) % 2 == 0
        values = jnp.where(
            lower, jnp.concatenate([values, other], 0), jnp.concatenate([other, values], 0)
        )
        distance //= 2
    return values


def local(
    encoder_input,
    desired_responses,
    sample_index,
    encoder_weight,
    decoder_weight,
    frequency_amplitude,
    spectral_filter_weight,
    output_weight,
):
    samples = sample_index.shape[0]
    sub_dev = desired_responses.shape[1]
    width = desired_responses.shape[2]
    forward_transform, inverse_transform = rotation_tables(width // 2)
    loss_scale = 1.0 / math.sqrt(samples * sub_dev * lax.axis_size("freq"))
    all_inputs = gather_rows(encoder_input, "freq")
    codes = jnp.tanh(
        jnp.dot(all_inputs, encoder_weight, preferred_element_type=jnp.float32)
    ).astype(jnp.bfloat16)
    inverse_ids = (
        jnp.zeros((samples,), jnp.int32).at[sample_index].set(jnp.arange(samples, dtype=jnp.int32))
    )
    latent = jnp.dot(codes[inverse_ids], decoder_weight, preferred_element_type=jnp.float32)
    gain_row_values = frequency_amplitude.astype(jnp.float32)
    mixed_in = (latent[:, None, :] * gain_row_values[None]).astype(jnp.bfloat16).reshape(-1, width)
    wanted_lines = desired_responses.reshape(-1, width)
    derivative_entering, grad_out, grad_filter = decode_rows(
        mixed_in,
        wanted_lines,
        output_weight,
        spectral_filter_weight,
        forward_transform,
        inverse_transform,
        loss_scale,
    )
    derivative_bottleneck = jnp.einsum(
        "orm,rm->om", derivative_entering.reshape(samples, sub_dev, width), gain_row_values
    )
    grad_out = sum_halving(grad_out, "freq")
    packed = sum_whole(
        jnp.concatenate([derivative_bottleneck, grad_filter.reshape(1, -1)], 0), "freq"
    )
    derivative_bottleneck = packed[:samples]
    grad_filter = packed[samples:].reshape(grad_filter.shape)
    grad_enc, grad_dec = encoder_grads(
        all_inputs, codes, derivative_bottleneck[sample_index], decoder_weight
    )
    return (grad_enc, grad_dec, grad_out, grad_filter)


def solution(mesh):
    return jax.shard_map(
        local,
        mesh=mesh,
        in_specs=(
            P(("groups", "freq"), None),
            P("groups", "freq", None),
            P("groups"),
            P(),
            P(),
            P("freq", None),
            P(),
            P(),
        ),
        out_specs=(P("groups", None), P("groups", None), P("groups", None), P("groups", None)),
        check_vma=False,
    )
```

```python
import math

import jax
import jax.numpy as jnp
from jax import lax
from jax.sharding import PartitionSpec as P


def rotation_tables(antennas):
    indices = jnp.arange(antennas, dtype=jnp.int32)
    products_mod = indices[:, None] * indices[None, :] % antennas
    angle_table = products_mod.astype(jnp.float32) * (2.0 * math.pi / antennas)
    cosine_table = jnp.cos(angle_table) / math.sqrt(antennas)
    sine_table = jnp.sin(angle_table) / math.sqrt(antennas)
    forward_transform = jnp.concatenate(
        [
            jnp.concatenate([cosine_table, -sine_table], 1),
            jnp.concatenate([sine_table, cosine_table], 1),
        ],
        0,
    )
    inverse_transform = jnp.concatenate(
        [
            jnp.concatenate([cosine_table, sine_table], 1),
            jnp.concatenate([-sine_table, cosine_table], 1),
        ],
        0,
    )
    return (forward_transform.astype(jnp.bfloat16), inverse_transform.astype(jnp.bfloat16))


def decode_rows(
    mixed_in,
    wanted_lines,
    output_weight,
    spectral_filter_weight,
    forward_transform,
    inverse_transform,
    loss_scale,
):
    filter_re = spectral_filter_weight[0]
    filter_im = spectral_filter_weight[1]
    spectrum = jnp.dot(mixed_in, forward_transform, preferred_element_type=jnp.float32)
    half_width = spectrum.shape[1] // 2
    spec_re = spectrum[:, :half_width]
    spec_im = spectrum[:, half_width:]
    filtered = jnp.concatenate(
        [spec_re * filter_re - spec_im * filter_im, spec_re * filter_im + spec_im * filter_re], 1
    ).astype(jnp.bfloat16)
    mixed_back = jnp.dot(filtered, inverse_transform, preferred_element_type=jnp.float32)
    hidden = (mixed_in.astype(jnp.float32) + jax.nn.gelu(mixed_back)).astype(jnp.bfloat16)
    rebuilt = hidden.astype(jnp.float32) + jnp.dot(
        hidden, output_weight, preferred_element_type=jnp.float32
    )
    residual = loss_scale * (rebuilt - wanted_lines.astype(jnp.float32))
    residual_half = residual.astype(jnp.bfloat16)
    grad_out = lax.dot_general(
        hidden, residual_half, (((0,), (0,)), ((), ())), preferred_element_type=jnp.float32
    )
    grad_hidden = residual + lax.dot_general(
        residual_half, output_weight, (((1,), (1,)), ((), ())), preferred_element_type=jnp.float32
    )
    grad_mixed = jax.vjp(jax.nn.gelu, mixed_back)[1](grad_hidden)[0].astype(jnp.bfloat16)
    grad_filtered = lax.dot_general(
        grad_mixed, inverse_transform, (((1,), (1,)), ((), ())), preferred_element_type=jnp.float32
    )
    grad_re = grad_filtered[:, :half_width]
    grad_im = grad_filtered[:, half_width:]
    grad_filter = jnp.stack(
        [
            jnp.sum(grad_re * spec_re + grad_im * spec_im, 0),
            jnp.sum(grad_im * spec_re - grad_re * spec_im, 0),
        ]
    )
    grad_spec = jnp.concatenate(
        [grad_re * filter_re + grad_im * filter_im, grad_im * filter_re - grad_re * filter_im], 1
    ).astype(jnp.bfloat16)
    derivative_entering = grad_hidden + lax.dot_general(
        grad_spec, forward_transform, (((1,), (1,)), ((), ())), preferred_element_type=jnp.float32
    )
    return (derivative_entering, grad_out, grad_filter)


def encoder_grads(inputs_rows, codewords, latent_sums, decoder_weight):
    latent_half = latent_sums.astype(jnp.bfloat16)
    grad_dec = lax.dot_general(
        codewords, latent_half, (((0,), (0,)), ((), ())), preferred_element_type=jnp.float32
    )
    grad_codes = lax.dot_general(
        latent_half, decoder_weight, (((1,), (1,)), ((), ())), preferred_element_type=jnp.float32
    )
    grad_pre = (grad_codes * (1.0 - jnp.square(codewords.astype(jnp.float32)))).astype(jnp.bfloat16)
    grad_enc = lax.dot_general(
        inputs_rows, grad_pre, (((0,), (0,)), ((), ())), preferred_element_type=jnp.float32
    )
    return (grad_enc, grad_dec)


def _exchange_pairs(count, distance):
    return [(i, i ^ distance) for i in range(count)]


def _is_power_of_two(count):
    return count > 0 and count & (count - 1) == 0


def gather_rows(block, axis_name):
    count = lax.axis_size(axis_name)
    if not _is_power_of_two(count):
        return lax.all_gather(block, axis_name, axis=0, tiled=True)
    position = lax.axis_index(axis_name)
    distance = 1
    while distance < count:
        other = lax.ppermute(block, axis_name, _exchange_pairs(count, distance))
        lower = (position // distance) % 2 == 0
        block = jnp.where(
            lower, jnp.concatenate([block, other], 0), jnp.concatenate([other, block], 0)
        )
        distance *= 2
    return block


def sum_whole(values, axis_name):
    count = lax.axis_size(axis_name)
    if not _is_power_of_two(count):
        return lax.psum(values, axis_name)
    distance = 1
    while distance < count:
        values = values + lax.ppermute(values, axis_name, _exchange_pairs(count, distance))
        distance *= 2
    return values


def sum_halving(values, axis_name):
    count = lax.axis_size(axis_name)
    if not _is_power_of_two(count) or values.shape[0] % count != 0:
        return lax.psum(values, axis_name)
    position = lax.axis_index(axis_name)
    distance = 1
    while distance < count:
        half = values.shape[0] // 2
        lower = (position // distance) % 2 == 0
        keep = jnp.where(lower, values[:half], values[half:])
        send = jnp.where(lower, values[half:], values[:half])
        values = keep + lax.ppermute(send, axis_name, _exchange_pairs(count, distance))
        distance *= 2
    distance = count // 2
    while distance >= 1:
        other = lax.ppermute(values, axis_name, _exchange_pairs(count, distance))
        lower = (position // distance) % 2 == 0
        values = jnp.where(
            lower, jnp.concatenate([values, other], 0), jnp.concatenate([other, values], 0)
        )
        distance //= 2
    return values


def local(
    encoder_input,
    desired_responses,
    sample_index,
    encoder_weight,
    decoder_weight,
    frequency_amplitude,
    spectral_filter_weight,
    output_weight,
):
    samples = sample_index.shape[0]
    sub_dev = desired_responses.shape[1]
    width = desired_responses.shape[2]
    forward_transform, inverse_transform = rotation_tables(width // 2)
    loss_scale = 1.0 / math.sqrt(samples * sub_dev * lax.axis_size("freq"))
    all_inputs = gather_rows(encoder_input, "freq")
    codes = jnp.tanh(
        jnp.dot(all_inputs, encoder_weight, preferred_element_type=jnp.float32)
    ).astype(jnp.bfloat16)
    inverse_ids = (
        jnp.zeros((samples,), jnp.int32).at[sample_index].set(jnp.arange(samples, dtype=jnp.int32))
    )
    latent = jnp.dot(codes[inverse_ids], decoder_weight, preferred_element_type=jnp.float32)
    gain_row_values = frequency_amplitude.astype(jnp.float32)
    mixed_in = (latent[:, None, :] * gain_row_values[None]).astype(jnp.bfloat16).reshape(-1, width)
    wanted_lines = desired_responses.reshape(-1, width)
    derivative_entering, grad_out, grad_filter = decode_rows(
        mixed_in,
        wanted_lines,
        output_weight,
        spectral_filter_weight,
        forward_transform,
        inverse_transform,
        loss_scale,
    )
    derivative_bottleneck = jnp.einsum(
        "orm,rm->om", derivative_entering.reshape(samples, sub_dev, width), gain_row_values
    )
    count = lax.axis_size("freq")
    packed_rows = samples + 1 + grad_out.shape[0]
    padding = -packed_rows % count
    packed = jnp.concatenate(
        [
            derivative_bottleneck,
            grad_filter.reshape(1, -1),
            grad_out,
            jnp.zeros((padding, width), jnp.float32),
        ],
        0,
    )
    packed = sum_halving(packed, "freq")
    derivative_bottleneck = packed[:samples]
    grad_filter = packed[samples].reshape(grad_filter.shape)
    grad_out = packed[samples + 1 : packed_rows]
    grad_enc, grad_dec = encoder_grads(
        all_inputs, codes, derivative_bottleneck[sample_index], decoder_weight
    )
    return (grad_enc, grad_dec, grad_out, grad_filter)


def solution(mesh):
    return jax.shard_map(
        local,
        mesh=mesh,
        in_specs=(
            P(("groups", "freq"), None),
            P("groups", "freq", None),
            P("groups"),
            P(),
            P(),
            P("freq", None),
            P(),
            P(),
        ),
        out_specs=(P("groups", None), P("groups", None), P("groups", None), P("groups", None)),
        check_vma=False,
    )
```

```python
import math

import jax
import jax.numpy as jnp
from jax import lax
from jax.sharding import PartitionSpec as P


def rotation_tables(antennas):
    indices = jnp.arange(antennas, dtype=jnp.int32)
    products_mod = indices[:, None] * indices[None, :] % antennas
    angle_table = products_mod.astype(jnp.float32) * (2.0 * math.pi / antennas)
    cosine_table = jnp.cos(angle_table) / math.sqrt(antennas)
    sine_table = jnp.sin(angle_table) / math.sqrt(antennas)
    forward_transform = jnp.concatenate(
        [
            jnp.concatenate([cosine_table, -sine_table], 1),
            jnp.concatenate([sine_table, cosine_table], 1),
        ],
        0,
    )
    inverse_transform = jnp.concatenate(
        [
            jnp.concatenate([cosine_table, sine_table], 1),
            jnp.concatenate([-sine_table, cosine_table], 1),
        ],
        0,
    )
    return (forward_transform.astype(jnp.bfloat16), inverse_transform.astype(jnp.bfloat16))


def decode_rows(
    mixed_in,
    wanted_lines,
    output_weight,
    spectral_filter_weight,
    forward_transform,
    inverse_transform,
    loss_scale,
):
    filter_re = spectral_filter_weight[0]
    filter_im = spectral_filter_weight[1]
    spectrum = jnp.dot(mixed_in, forward_transform, preferred_element_type=jnp.float32)
    half_width = spectrum.shape[1] // 2
    spec_re = spectrum[:, :half_width]
    spec_im = spectrum[:, half_width:]
    filtered = jnp.concatenate(
        [spec_re * filter_re - spec_im * filter_im, spec_re * filter_im + spec_im * filter_re], 1
    ).astype(jnp.bfloat16)
    mixed_back = jnp.dot(filtered, inverse_transform, preferred_element_type=jnp.float32)
    hidden = (mixed_in.astype(jnp.float32) + jax.nn.gelu(mixed_back)).astype(jnp.bfloat16)
    rebuilt = hidden.astype(jnp.float32) + jnp.dot(
        hidden, output_weight, preferred_element_type=jnp.float32
    )
    residual = loss_scale * (rebuilt - wanted_lines.astype(jnp.float32))
    residual_half = residual.astype(jnp.bfloat16)
    grad_out = lax.dot_general(
        hidden, residual_half, (((0,), (0,)), ((), ())), preferred_element_type=jnp.float32
    )
    grad_hidden = residual + lax.dot_general(
        residual_half, output_weight, (((1,), (1,)), ((), ())), preferred_element_type=jnp.float32
    )
    grad_mixed = jax.vjp(jax.nn.gelu, mixed_back)[1](grad_hidden)[0].astype(jnp.bfloat16)
    grad_filtered = lax.dot_general(
        grad_mixed, inverse_transform, (((1,), (1,)), ((), ())), preferred_element_type=jnp.float32
    )
    grad_re = grad_filtered[:, :half_width]
    grad_im = grad_filtered[:, half_width:]
    grad_filter = jnp.stack(
        [
            jnp.sum(grad_re * spec_re + grad_im * spec_im, 0),
            jnp.sum(grad_im * spec_re - grad_re * spec_im, 0),
        ]
    )
    grad_spec = jnp.concatenate(
        [grad_re * filter_re + grad_im * filter_im, grad_im * filter_re - grad_re * filter_im], 1
    ).astype(jnp.bfloat16)
    derivative_entering = grad_hidden + lax.dot_general(
        grad_spec, forward_transform, (((1,), (1,)), ((), ())), preferred_element_type=jnp.float32
    )
    return (derivative_entering, grad_out, grad_filter)


def encoder_grads(inputs_rows, codewords, latent_sums, decoder_weight):
    latent_half = latent_sums.astype(jnp.bfloat16)
    grad_dec = lax.dot_general(
        codewords, latent_half, (((0,), (0,)), ((), ())), preferred_element_type=jnp.float32
    )
    grad_codes = lax.dot_general(
        latent_half, decoder_weight, (((1,), (1,)), ((), ())), preferred_element_type=jnp.float32
    )
    grad_pre = (grad_codes * (1.0 - jnp.square(codewords.astype(jnp.float32)))).astype(jnp.bfloat16)
    grad_enc = lax.dot_general(
        inputs_rows, grad_pre, (((0,), (0,)), ((), ())), preferred_element_type=jnp.float32
    )
    return (grad_enc, grad_dec)


def _exchange_pairs(count, distance):
    return [(i, i ^ distance) for i in range(count)]


def _is_power_of_two(count):
    return count > 0 and count & (count - 1) == 0


def gather_rows(block, axis_name):
    count = lax.axis_size(axis_name)
    if not _is_power_of_two(count):
        return lax.all_gather(block, axis_name, axis=0, tiled=True)
    position = lax.axis_index(axis_name)
    distance = 1
    while distance < count:
        other = lax.ppermute(block, axis_name, _exchange_pairs(count, distance))
        lower = (position // distance) % 2 == 0
        block = jnp.where(
            lower, jnp.concatenate([block, other], 0), jnp.concatenate([other, block], 0)
        )
        distance *= 2
    return block


def sum_whole(values, axis_name):
    count = lax.axis_size(axis_name)
    if not _is_power_of_two(count):
        return lax.psum(values, axis_name)
    distance = 1
    while distance < count:
        values = values + lax.ppermute(values, axis_name, _exchange_pairs(count, distance))
        distance *= 2
    return values


def sum_halving(values, axis_name, wire=jnp.bfloat16):
    count = lax.axis_size(axis_name)
    if not _is_power_of_two(count) or values.shape[0] % count != 0:
        return lax.psum(values, axis_name)
    position = lax.axis_index(axis_name)
    distance = 1
    while distance < count:
        half = values.shape[0] // 2
        lower = (position // distance) % 2 == 0
        keep = jnp.where(lower, values[:half], values[half:])
        send = jnp.where(lower, values[half:], values[:half]).astype(wire)
        arrived = lax.ppermute(send, axis_name, _exchange_pairs(count, distance))
        values = keep + arrived.astype(keep.dtype)
        distance *= 2
    values = values.astype(wire)
    distance = count // 2
    while distance >= 1:
        other = lax.ppermute(values, axis_name, _exchange_pairs(count, distance))
        lower = (position // distance) % 2 == 0
        values = jnp.where(
            lower, jnp.concatenate([values, other], 0), jnp.concatenate([other, values], 0)
        )
        distance //= 2
    return values


def local(
    encoder_input,
    desired_responses,
    sample_index,
    encoder_weight,
    decoder_weight,
    frequency_amplitude,
    spectral_filter_weight,
    output_weight,
):
    samples = sample_index.shape[0]
    sub_dev = desired_responses.shape[1]
    width = desired_responses.shape[2]
    forward_transform, inverse_transform = rotation_tables(width // 2)
    loss_scale = 1.0 / math.sqrt(samples * sub_dev * lax.axis_size("freq"))
    all_inputs = gather_rows(encoder_input, "freq")
    codes = jnp.tanh(
        jnp.dot(all_inputs, encoder_weight, preferred_element_type=jnp.float32)
    ).astype(jnp.bfloat16)
    inverse_ids = (
        jnp.zeros((samples,), jnp.int32).at[sample_index].set(jnp.arange(samples, dtype=jnp.int32))
    )
    latent = jnp.dot(codes[inverse_ids], decoder_weight, preferred_element_type=jnp.float32)
    gain_row_values = frequency_amplitude.astype(jnp.float32)
    mixed_in = (latent[:, None, :] * gain_row_values[None]).astype(jnp.bfloat16).reshape(-1, width)
    wanted_lines = desired_responses.reshape(-1, width)
    derivative_entering, grad_out, grad_filter = decode_rows(
        mixed_in,
        wanted_lines,
        output_weight,
        spectral_filter_weight,
        forward_transform,
        inverse_transform,
        loss_scale,
    )
    derivative_bottleneck = jnp.einsum(
        "orm,rm->om", derivative_entering.reshape(samples, sub_dev, width), gain_row_values
    )
    count = lax.axis_size("freq")
    packed_rows = samples + 1 + grad_out.shape[0]
    padding = -packed_rows % count
    packed = jnp.concatenate(
        [
            derivative_bottleneck,
            grad_filter.reshape(1, -1),
            grad_out,
            jnp.zeros((padding, width), jnp.float32),
        ],
        0,
    )
    packed = sum_halving(packed, "freq").astype(jnp.float32)
    derivative_bottleneck = packed[:samples]
    grad_filter = packed[samples].reshape(grad_filter.shape)
    grad_out = packed[samples + 1 : packed_rows]
    grad_enc, grad_dec = encoder_grads(
        all_inputs, codes, derivative_bottleneck[sample_index], decoder_weight
    )
    return (grad_enc, grad_dec, grad_out, grad_filter)


def solution(mesh):
    return jax.shard_map(
        local,
        mesh=mesh,
        in_specs=(
            P(("groups", "freq"), None),
            P("groups", "freq", None),
            P("groups"),
            P(),
            P(),
            P("freq", None),
            P(),
            P(),
        ),
        out_specs=(P("groups", None), P("groups", None), P("groups", None), P("groups", None)),
        check_vma=False,
    )
```

```python
import math

import jax
import jax.numpy as jnp
from jax import lax
from jax.sharding import PartitionSpec as P


def rotation_tables(antennas):
    indices = jnp.arange(antennas, dtype=jnp.int32)
    products_mod = indices[:, None] * indices[None, :] % antennas
    angle_table = products_mod.astype(jnp.float32) * (2.0 * math.pi / antennas)
    cosine_table = jnp.cos(angle_table) / math.sqrt(antennas)
    sine_table = jnp.sin(angle_table) / math.sqrt(antennas)
    forward_transform = jnp.concatenate(
        [
            jnp.concatenate([cosine_table, -sine_table], 1),
            jnp.concatenate([sine_table, cosine_table], 1),
        ],
        0,
    )
    inverse_transform = jnp.concatenate(
        [
            jnp.concatenate([cosine_table, sine_table], 1),
            jnp.concatenate([-sine_table, cosine_table], 1),
        ],
        0,
    )
    return (forward_transform.astype(jnp.bfloat16), inverse_transform.astype(jnp.bfloat16))


def decode_rows(
    mixed_in,
    wanted_lines,
    output_weight,
    spectral_filter_weight,
    forward_transform,
    inverse_transform,
    loss_scale,
):
    filter_re = spectral_filter_weight[0]
    filter_im = spectral_filter_weight[1]
    spectrum = jnp.dot(mixed_in, forward_transform, preferred_element_type=jnp.float32)
    half_width = spectrum.shape[1] // 2
    spec_re = spectrum[:, :half_width]
    spec_im = spectrum[:, half_width:]
    filtered = jnp.concatenate(
        [spec_re * filter_re - spec_im * filter_im, spec_re * filter_im + spec_im * filter_re], 1
    ).astype(jnp.bfloat16)
    mixed_back = jnp.dot(filtered, inverse_transform, preferred_element_type=jnp.float32)
    hidden = (mixed_in.astype(jnp.float32) + jax.nn.gelu(mixed_back)).astype(jnp.bfloat16)
    rebuilt = hidden.astype(jnp.float32) + jnp.dot(
        hidden, output_weight, preferred_element_type=jnp.float32
    )
    residual = loss_scale * (rebuilt - wanted_lines.astype(jnp.float32))
    residual_half = residual.astype(jnp.bfloat16)
    grad_out = lax.dot_general(
        hidden, residual_half, (((0,), (0,)), ((), ())), preferred_element_type=jnp.float32
    )
    grad_hidden = residual + lax.dot_general(
        residual_half, output_weight, (((1,), (1,)), ((), ())), preferred_element_type=jnp.float32
    )
    grad_mixed = jax.vjp(jax.nn.gelu, mixed_back)[1](grad_hidden)[0].astype(jnp.bfloat16)
    grad_filtered = lax.dot_general(
        grad_mixed, inverse_transform, (((1,), (1,)), ((), ())), preferred_element_type=jnp.float32
    )
    grad_re = grad_filtered[:, :half_width]
    grad_im = grad_filtered[:, half_width:]
    grad_filter = jnp.stack(
        [
            jnp.sum(grad_re * spec_re + grad_im * spec_im, 0),
            jnp.sum(grad_im * spec_re - grad_re * spec_im, 0),
        ]
    )
    grad_spec = jnp.concatenate(
        [grad_re * filter_re + grad_im * filter_im, grad_im * filter_re - grad_re * filter_im], 1
    ).astype(jnp.bfloat16)
    derivative_entering = grad_hidden + lax.dot_general(
        grad_spec, forward_transform, (((1,), (1,)), ((), ())), preferred_element_type=jnp.float32
    )
    return (derivative_entering, grad_out, grad_filter)


def encoder_grads(inputs_rows, codewords, latent_sums, decoder_weight):
    latent_half = latent_sums.astype(jnp.bfloat16)
    grad_dec = lax.dot_general(
        codewords, latent_half, (((0,), (0,)), ((), ())), preferred_element_type=jnp.float32
    )
    grad_codes = lax.dot_general(
        latent_half, decoder_weight, (((1,), (1,)), ((), ())), preferred_element_type=jnp.float32
    )
    grad_pre = (grad_codes * (1.0 - jnp.square(codewords.astype(jnp.float32)))).astype(jnp.bfloat16)
    grad_enc = lax.dot_general(
        inputs_rows, grad_pre, (((0,), (0,)), ((), ())), preferred_element_type=jnp.float32
    )
    return (grad_enc, grad_dec)


def _exchange_pairs(count, distance):
    return [(i, i ^ distance) for i in range(count)]


def _is_power_of_two(count):
    return count > 0 and count & (count - 1) == 0


def gather_rows(block, axis_name):
    count = lax.axis_size(axis_name)
    if not _is_power_of_two(count):
        return lax.all_gather(block, axis_name, axis=0, tiled=True)
    position = lax.axis_index(axis_name)
    distance = 1
    while distance < count:
        other = lax.ppermute(block, axis_name, _exchange_pairs(count, distance))
        lower = (position // distance) % 2 == 0
        block = jnp.where(
            lower, jnp.concatenate([block, other], 0), jnp.concatenate([other, block], 0)
        )
        distance *= 2
    return block


def sum_whole(values, axis_name):
    count = lax.axis_size(axis_name)
    if not _is_power_of_two(count):
        return lax.psum(values, axis_name)
    distance = 1
    while distance < count:
        values = values + lax.ppermute(values, axis_name, _exchange_pairs(count, distance))
        distance *= 2
    return values


def sum_halving(values, axis_name, wire=jnp.bfloat16, halving_levels=2):
    count = lax.axis_size(axis_name)
    if not _is_power_of_two(count) or values.shape[0] % count != 0:
        return lax.psum(values, axis_name)
    position = lax.axis_index(axis_name)
    distance = 1
    while distance < count and distance < 2**halving_levels:
        half = values.shape[0] // 2
        lower = (position // distance) % 2 == 0
        keep = jnp.where(lower, values[:half], values[half:])
        send = jnp.where(lower, values[half:], values[:half]).astype(wire)
        arrived = lax.ppermute(send, axis_name, _exchange_pairs(count, distance))
        values = keep + arrived.astype(keep.dtype)
        distance *= 2
    top = distance
    values = values.astype(wire)
    while distance < count:
        arrived = lax.ppermute(values, axis_name, _exchange_pairs(count, distance))
        values = (values.astype(jnp.float32) + arrived.astype(jnp.float32)).astype(wire)
        distance *= 2
    distance = top // 2
    while distance >= 1:
        other = lax.ppermute(values, axis_name, _exchange_pairs(count, distance))
        lower = (position // distance) % 2 == 0
        values = jnp.where(
            lower, jnp.concatenate([values, other], 0), jnp.concatenate([other, values], 0)
        )
        distance //= 2
    return values


def local(
    encoder_input,
    desired_responses,
    sample_index,
    encoder_weight,
    decoder_weight,
    frequency_amplitude,
    spectral_filter_weight,
    output_weight,
):
    samples = sample_index.shape[0]
    sub_dev = desired_responses.shape[1]
    width = desired_responses.shape[2]
    forward_transform, inverse_transform = rotation_tables(width // 2)
    loss_scale = 1.0 / math.sqrt(samples * sub_dev * lax.axis_size("freq"))
    all_inputs = gather_rows(encoder_input, "freq")
    codes = jnp.tanh(
        jnp.dot(all_inputs, encoder_weight, preferred_element_type=jnp.float32)
    ).astype(jnp.bfloat16)
    inverse_ids = (
        jnp.zeros((samples,), jnp.int32).at[sample_index].set(jnp.arange(samples, dtype=jnp.int32))
    )
    latent = jnp.dot(codes[inverse_ids], decoder_weight, preferred_element_type=jnp.float32)
    gain_row_values = frequency_amplitude.astype(jnp.float32)
    mixed_in = (latent[:, None, :] * gain_row_values[None]).astype(jnp.bfloat16).reshape(-1, width)
    wanted_lines = desired_responses.reshape(-1, width)
    derivative_entering, grad_out, grad_filter = decode_rows(
        mixed_in,
        wanted_lines,
        output_weight,
        spectral_filter_weight,
        forward_transform,
        inverse_transform,
        loss_scale,
    )
    derivative_bottleneck = jnp.einsum(
        "orm,rm->om", derivative_entering.reshape(samples, sub_dev, width), gain_row_values
    )
    count = lax.axis_size("freq")
    packed_rows = samples + 1 + grad_out.shape[0]
    padding = -packed_rows % count
    packed = jnp.concatenate(
        [
            grad_out,
            derivative_bottleneck,
            grad_filter.reshape(1, -1),
            jnp.zeros((padding, width), jnp.float32),
        ],
        0,
    )
    packed = sum_halving(packed, "freq").astype(jnp.float32)
    rows_out = grad_out.shape[0]
    grad_out = packed[:rows_out]
    derivative_bottleneck = packed[rows_out : rows_out + samples]
    grad_filter = packed[rows_out + samples].reshape(grad_filter.shape)
    grad_enc, grad_dec = encoder_grads(
        all_inputs, codes, derivative_bottleneck[sample_index], decoder_weight
    )
    return (grad_enc, grad_dec, grad_out, grad_filter)


def solution(mesh):
    return jax.shard_map(
        local,
        mesh=mesh,
        in_specs=(
            P(("groups", "freq"), None),
            P("groups", "freq", None),
            P("groups"),
            P(),
            P(),
            P("freq", None),
            P(),
            P(),
        ),
        out_specs=(P("groups", None), P("groups", None), P("groups", None), P("groups", None)),
        check_vma=False,
    )
```

```python
import math

import jax
import jax.numpy as jnp
from jax import lax
from jax.sharding import PartitionSpec as P


def rotation_tables(antennas):
    indices = jnp.arange(antennas, dtype=jnp.int32)
    products_mod = indices[:, None] * indices[None, :] % antennas
    angle_table = products_mod.astype(jnp.float32) * (2.0 * math.pi / antennas)
    cosine_table = jnp.cos(angle_table) / math.sqrt(antennas)
    sine_table = jnp.sin(angle_table) / math.sqrt(antennas)
    forward_transform = jnp.concatenate(
        [
            jnp.concatenate([cosine_table, -sine_table], 1),
            jnp.concatenate([sine_table, cosine_table], 1),
        ],
        0,
    )
    inverse_transform = jnp.concatenate(
        [
            jnp.concatenate([cosine_table, sine_table], 1),
            jnp.concatenate([-sine_table, cosine_table], 1),
        ],
        0,
    )
    return (forward_transform.astype(jnp.bfloat16), inverse_transform.astype(jnp.bfloat16))


def decode_rows(
    mixed_in,
    wanted_lines,
    output_weight,
    spectral_filter_weight,
    forward_transform,
    inverse_transform,
    loss_scale,
):
    filter_re = spectral_filter_weight[0]
    filter_im = spectral_filter_weight[1]
    spectrum = jnp.dot(mixed_in, forward_transform, preferred_element_type=jnp.float32)
    half_width = spectrum.shape[1] // 2
    spec_re = spectrum[:, :half_width]
    spec_im = spectrum[:, half_width:]
    filtered = jnp.concatenate(
        [spec_re * filter_re - spec_im * filter_im, spec_re * filter_im + spec_im * filter_re], 1
    ).astype(jnp.bfloat16)
    mixed_back = jnp.dot(filtered, inverse_transform, preferred_element_type=jnp.float32)
    hidden = (mixed_in.astype(jnp.float32) + jax.nn.gelu(mixed_back)).astype(jnp.bfloat16)
    rebuilt = hidden.astype(jnp.float32) + jnp.dot(
        hidden, output_weight, preferred_element_type=jnp.float32
    )
    residual = loss_scale * (rebuilt - wanted_lines.astype(jnp.float32))
    residual_half = residual.astype(jnp.bfloat16)
    grad_out = lax.dot_general(
        hidden, residual_half, (((0,), (0,)), ((), ())), preferred_element_type=jnp.float32
    )
    grad_hidden = residual + lax.dot_general(
        residual_half, output_weight, (((1,), (1,)), ((), ())), preferred_element_type=jnp.float32
    )
    grad_mixed = jax.vjp(jax.nn.gelu, mixed_back)[1](grad_hidden)[0].astype(jnp.bfloat16)
    grad_filtered = lax.dot_general(
        grad_mixed, inverse_transform, (((1,), (1,)), ((), ())), preferred_element_type=jnp.float32
    )
    grad_re = grad_filtered[:, :half_width]
    grad_im = grad_filtered[:, half_width:]
    grad_filter = jnp.stack(
        [
            jnp.sum(grad_re * spec_re + grad_im * spec_im, 0),
            jnp.sum(grad_im * spec_re - grad_re * spec_im, 0),
        ]
    )
    grad_spec = jnp.concatenate(
        [grad_re * filter_re + grad_im * filter_im, grad_im * filter_re - grad_re * filter_im], 1
    ).astype(jnp.bfloat16)
    derivative_entering = grad_hidden + lax.dot_general(
        grad_spec, forward_transform, (((1,), (1,)), ((), ())), preferred_element_type=jnp.float32
    )
    return (derivative_entering, grad_out, grad_filter)


def encoder_grads(inputs_rows, codewords, latent_sums, decoder_weight):
    latent_half = latent_sums.astype(jnp.bfloat16)
    grad_dec = lax.dot_general(
        codewords, latent_half, (((0,), (0,)), ((), ())), preferred_element_type=jnp.float32
    )
    grad_codes = lax.dot_general(
        latent_half, decoder_weight, (((1,), (1,)), ((), ())), preferred_element_type=jnp.float32
    )
    grad_pre = (grad_codes * (1.0 - jnp.square(codewords.astype(jnp.float32)))).astype(jnp.bfloat16)
    grad_enc = lax.dot_general(
        inputs_rows, grad_pre, (((0,), (0,)), ((), ())), preferred_element_type=jnp.float32
    )
    return (grad_enc, grad_dec)


def _exchange_pairs(count, distance):
    return [(i, i ^ distance) for i in range(count)]


def _is_power_of_two(count):
    return count > 0 and count & (count - 1) == 0


def gather_rows(block, axis_name):
    count = lax.axis_size(axis_name)
    if not _is_power_of_two(count):
        return lax.all_gather(block, axis_name, axis=0, tiled=True)
    position = lax.axis_index(axis_name)
    distance = 1
    while distance < count:
        other = lax.ppermute(block, axis_name, _exchange_pairs(count, distance))
        lower = (position // distance) % 2 == 0
        block = jnp.where(
            lower, jnp.concatenate([block, other], 0), jnp.concatenate([other, block], 0)
        )
        distance *= 2
    return block


def sum_whole(values, axis_name):
    count = lax.axis_size(axis_name)
    if not _is_power_of_two(count):
        return lax.psum(values, axis_name)
    distance = 1
    while distance < count:
        values = values + lax.ppermute(values, axis_name, _exchange_pairs(count, distance))
        distance *= 2
    return values


def reduce_grads(grad_out, small, axis_name, wire=jnp.bfloat16, halving_levels=2):
    count = lax.axis_size(axis_name)
    parts = min(2**halving_levels, count)
    rows_out, width = grad_out.shape
    if not _is_power_of_two(count) or rows_out % parts != 0:
        return lax.psum(grad_out, axis_name), lax.psum(small, axis_name)
    chunk = rows_out // parts
    block = chunk + small.shape[0]
    block += -block % 16
    filler = jnp.zeros((block - chunk - small.shape[0], width), jnp.float32)
    values = jnp.concatenate(
        [
            piece
            for index in range(parts)
            for piece in (grad_out[index * chunk : (index + 1) * chunk], small, filler)
        ],
        0,
    )
    position = lax.axis_index(axis_name)
    distance = 1
    while distance < parts:
        half = values.shape[0] // 2
        lower = (position // distance) % 2 == 0
        keep = jnp.where(lower, values[:half], values[half:])
        send = jnp.where(lower, values[half:], values[:half]).astype(wire)
        arrived = lax.ppermute(send, axis_name, _exchange_pairs(count, distance))
        shared = (jnp.arange(half) % block >= chunk)[:, None]
        keep = jnp.where(shared, keep.astype(wire).astype(keep.dtype), keep)
        values = keep + arrived.astype(keep.dtype)
        distance *= 2
    values = values.astype(wire)
    while distance < count:
        arrived = lax.ppermute(values, axis_name, _exchange_pairs(count, distance))
        values = (values.astype(jnp.float32) + arrived.astype(jnp.float32)).astype(wire)
        distance *= 2
    small_total = values[chunk : chunk + small.shape[0]].astype(jnp.float32)
    distance = parts // 2
    while distance >= 1:
        other = lax.ppermute(values, axis_name, _exchange_pairs(count, distance))
        lower = (position // distance) % 2 == 0
        values = jnp.where(
            lower, jnp.concatenate([values, other], 0), jnp.concatenate([other, values], 0)
        )
        distance //= 2
    grad_total = values.reshape(parts, block, width)[:, :chunk].reshape(rows_out, width)
    return grad_total.astype(jnp.float32), small_total


def local(
    encoder_input,
    desired_responses,
    sample_index,
    encoder_weight,
    decoder_weight,
    frequency_amplitude,
    spectral_filter_weight,
    output_weight,
):
    samples = sample_index.shape[0]
    sub_dev = desired_responses.shape[1]
    width = desired_responses.shape[2]
    forward_transform, inverse_transform = rotation_tables(width // 2)
    loss_scale = 1.0 / math.sqrt(samples * sub_dev * lax.axis_size("freq"))
    all_inputs = gather_rows(encoder_input, "freq")
    codes = jnp.tanh(
        jnp.dot(all_inputs, encoder_weight, preferred_element_type=jnp.float32)
    ).astype(jnp.bfloat16)
    inverse_ids = (
        jnp.zeros((samples,), jnp.int32).at[sample_index].set(jnp.arange(samples, dtype=jnp.int32))
    )
    latent = jnp.dot(codes[inverse_ids], decoder_weight, preferred_element_type=jnp.float32)
    gain_row_values = frequency_amplitude.astype(jnp.float32)
    mixed_in = (latent[:, None, :] * gain_row_values[None]).astype(jnp.bfloat16).reshape(-1, width)
    wanted_lines = desired_responses.reshape(-1, width)
    derivative_entering, grad_out, grad_filter = decode_rows(
        mixed_in,
        wanted_lines,
        output_weight,
        spectral_filter_weight,
        forward_transform,
        inverse_transform,
        loss_scale,
    )
    derivative_bottleneck = jnp.einsum(
        "orm,rm->om", derivative_entering.reshape(samples, sub_dev, width), gain_row_values
    )
    grad_out, small = reduce_grads(
        grad_out,
        jnp.concatenate([derivative_bottleneck, grad_filter.reshape(1, -1)], 0),
        "freq",
    )
    derivative_bottleneck = small[:samples]
    grad_filter = small[samples].reshape(grad_filter.shape)
    grad_enc, grad_dec = encoder_grads(
        all_inputs, codes, derivative_bottleneck[sample_index], decoder_weight
    )
    return (grad_enc, grad_dec, grad_out, grad_filter)


def solution(mesh):
    return jax.shard_map(
        local,
        mesh=mesh,
        in_specs=(
            P(("groups", "freq"), None),
            P("groups", "freq", None),
            P("groups"),
            P(),
            P(),
            P("freq", None),
            P(),
            P(),
        ),
        out_specs=(P("groups", None), P("groups", None), P("groups", None), P("groups", None)),
        check_vma=False,
    )
```

```python
import math

import jax
import ml_dtypes
import numpy as np
import jax.numpy as jnp
from jax import lax
from jax.sharding import PartitionSpec as P


def rotation_tables(antennas):
    indices = np.arange(antennas, dtype=np.int32)
    products_mod = indices[:, None] * indices[None, :] % antennas
    angle_table = products_mod.astype(np.float32) * np.float32(2.0 * math.pi / antennas)
    cosine_table = np.cos(angle_table) / np.float32(math.sqrt(antennas))
    sine_table = np.sin(angle_table) / np.float32(math.sqrt(antennas))
    forward_transform = np.concatenate(
        [
            np.concatenate([cosine_table, -sine_table], 1),
            np.concatenate([sine_table, cosine_table], 1),
        ],
        0,
    )
    inverse_transform = np.concatenate(
        [
            np.concatenate([cosine_table, sine_table], 1),
            np.concatenate([-sine_table, cosine_table], 1),
        ],
        0,
    )
    return (
        jnp.asarray(forward_transform.astype(ml_dtypes.bfloat16)),
        jnp.asarray(inverse_transform.astype(ml_dtypes.bfloat16)),
    )


def decode_rows(
    mixed_in,
    wanted_lines,
    output_weight,
    spectral_filter_weight,
    forward_transform,
    inverse_transform,
    loss_scale,
):
    filter_re = spectral_filter_weight[0]
    filter_im = spectral_filter_weight[1]
    spectrum = jnp.dot(mixed_in, forward_transform, preferred_element_type=jnp.float32)
    half_width = spectrum.shape[1] // 2
    spec_re = spectrum[:, :half_width]
    spec_im = spectrum[:, half_width:]
    filtered = jnp.concatenate(
        [spec_re * filter_re - spec_im * filter_im, spec_re * filter_im + spec_im * filter_re], 1
    ).astype(jnp.bfloat16)
    mixed_back = jnp.dot(filtered, inverse_transform, preferred_element_type=jnp.float32)
    hidden = (mixed_in.astype(jnp.float32) + jax.nn.gelu(mixed_back)).astype(jnp.bfloat16)
    rebuilt = hidden.astype(jnp.float32) + jnp.dot(
        hidden, output_weight, preferred_element_type=jnp.float32
    )
    residual = loss_scale * (rebuilt - wanted_lines.astype(jnp.float32))
    residual_half = residual.astype(jnp.bfloat16)
    grad_out = lax.dot_general(
        hidden, residual_half, (((0,), (0,)), ((), ())), preferred_element_type=jnp.float32
    )
    grad_hidden = residual + lax.dot_general(
        residual_half, output_weight, (((1,), (1,)), ((), ())), preferred_element_type=jnp.float32
    )
    grad_mixed = jax.vjp(jax.nn.gelu, mixed_back)[1](grad_hidden)[0].astype(jnp.bfloat16)
    grad_filtered = lax.dot_general(
        grad_mixed, inverse_transform, (((1,), (1,)), ((), ())), preferred_element_type=jnp.float32
    )
    grad_re = grad_filtered[:, :half_width]
    grad_im = grad_filtered[:, half_width:]
    grad_filter = jnp.stack(
        [
            jnp.sum(grad_re * spec_re + grad_im * spec_im, 0),
            jnp.sum(grad_im * spec_re - grad_re * spec_im, 0),
        ]
    )
    grad_spec = jnp.concatenate(
        [grad_re * filter_re + grad_im * filter_im, grad_im * filter_re - grad_re * filter_im], 1
    ).astype(jnp.bfloat16)
    derivative_entering = grad_hidden + lax.dot_general(
        grad_spec, forward_transform, (((1,), (1,)), ((), ())), preferred_element_type=jnp.float32
    )
    return (derivative_entering, grad_out, grad_filter)


def encoder_grads(inputs_rows, codewords, latent_sums, decoder_weight):
    latent_half = latent_sums.astype(jnp.bfloat16)
    grad_dec = lax.dot_general(
        codewords, latent_half, (((0,), (0,)), ((), ())), preferred_element_type=jnp.float32
    )
    grad_codes = lax.dot_general(
        latent_half, decoder_weight, (((1,), (1,)), ((), ())), preferred_element_type=jnp.float32
    )
    grad_pre = (grad_codes * (1.0 - jnp.square(codewords.astype(jnp.float32)))).astype(jnp.bfloat16)
    grad_enc = lax.dot_general(
        inputs_rows, grad_pre, (((0,), (0,)), ((), ())), preferred_element_type=jnp.float32
    )
    return (grad_enc, grad_dec)


def _exchange_pairs(count, distance):
    return [(i, i ^ distance) for i in range(count)]


def _is_power_of_two(count):
    return count > 0 and count & (count - 1) == 0


def gather_rows(block, axis_name):
    count = lax.axis_size(axis_name)
    if not _is_power_of_two(count):
        return lax.all_gather(block, axis_name, axis=0, tiled=True)
    position = lax.axis_index(axis_name)
    distance = 1
    while distance < count:
        other = lax.ppermute(block, axis_name, _exchange_pairs(count, distance))
        lower = (position // distance) % 2 == 0
        block = jnp.where(
            lower, jnp.concatenate([block, other], 0), jnp.concatenate([other, block], 0)
        )
        distance *= 2
    return block


def sum_whole(values, axis_name):
    count = lax.axis_size(axis_name)
    if not _is_power_of_two(count):
        return lax.psum(values, axis_name)
    distance = 1
    while distance < count:
        values = values + lax.ppermute(values, axis_name, _exchange_pairs(count, distance))
        distance *= 2
    return values


def sum_halving(values, axis_name, wire=jnp.bfloat16, halving_levels=2):
    count = lax.axis_size(axis_name)
    if not _is_power_of_two(count) or values.shape[0] % count != 0:
        return lax.psum(values, axis_name)
    position = lax.axis_index(axis_name)
    distance = 1
    while distance < count and distance < 2**halving_levels:
        half = values.shape[0] // 2
        lower = (position // distance) % 2 == 0
        keep = jnp.where(lower, values[:half], values[half:])
        send = jnp.where(lower, values[half:], values[:half]).astype(wire)
        arrived = lax.ppermute(send, axis_name, _exchange_pairs(count, distance))
        values = keep + arrived.astype(keep.dtype)
        distance *= 2
    top = distance
    values = values.astype(wire)
    while distance < count:
        arrived = lax.ppermute(values, axis_name, _exchange_pairs(count, distance))
        values = (values.astype(jnp.float32) + arrived.astype(jnp.float32)).astype(wire)
        distance *= 2
    distance = top // 2
    while distance >= 1:
        other = lax.ppermute(values, axis_name, _exchange_pairs(count, distance))
        lower = (position // distance) % 2 == 0
        values = jnp.where(
            lower, jnp.concatenate([values, other], 0), jnp.concatenate([other, values], 0)
        )
        distance //= 2
    return values


def local(
    encoder_input,
    desired_responses,
    sample_index,
    encoder_weight,
    decoder_weight,
    frequency_amplitude,
    spectral_filter_weight,
    output_weight,
):
    samples = sample_index.shape[0]
    sub_dev = desired_responses.shape[1]
    width = desired_responses.shape[2]
    forward_transform, inverse_transform = rotation_tables(width // 2)
    loss_scale = 1.0 / math.sqrt(samples * sub_dev * lax.axis_size("freq"))
    all_inputs = gather_rows(encoder_input, "freq")
    codes = jnp.tanh(
        jnp.dot(all_inputs, encoder_weight, preferred_element_type=jnp.float32)
    ).astype(jnp.bfloat16)
    selection = (
        sample_index[None, :] == jnp.arange(samples, dtype=jnp.int32)[:, None]
    ).astype(jnp.bfloat16)
    codes_by_sample = jnp.dot(selection, codes, preferred_element_type=jnp.float32).astype(
        jnp.bfloat16
    )
    latent = jnp.dot(codes_by_sample, decoder_weight, preferred_element_type=jnp.float32)
    gain_row_values = frequency_amplitude.astype(jnp.float32)
    mixed_in = (latent[:, None, :] * gain_row_values[None]).astype(jnp.bfloat16).reshape(-1, width)
    wanted_lines = desired_responses.reshape(-1, width)
    derivative_entering, grad_out, grad_filter = decode_rows(
        mixed_in,
        wanted_lines,
        output_weight,
        spectral_filter_weight,
        forward_transform,
        inverse_transform,
        loss_scale,
    )
    derivative_bottleneck = jnp.einsum(
        "orm,rm->om", derivative_entering.reshape(samples, sub_dev, width), gain_row_values
    )
    count = lax.axis_size("freq")
    packed_rows = samples + 1 + grad_out.shape[0]
    padding = -packed_rows % count
    packed = jnp.concatenate(
        [
            grad_out,
            derivative_bottleneck,
            grad_filter.reshape(1, -1),
            jnp.zeros((padding, width), jnp.float32),
        ],
        0,
    )
    packed = sum_halving(packed, "freq")
    rows_out = grad_out.shape[0]
    grad_out = packed[:rows_out].astype(jnp.float32)
    derivative_bottleneck = packed[rows_out : rows_out + samples].astype(jnp.float32)
    grad_filter = packed[rows_out + samples].astype(jnp.float32).reshape(grad_filter.shape)
    grad_enc, grad_dec = encoder_grads(
        all_inputs, codes, derivative_bottleneck[sample_index], decoder_weight
    )
    return (grad_enc, grad_dec, grad_out, grad_filter)


def solution(mesh):
    return jax.shard_map(
        local,
        mesh=mesh,
        in_specs=(
            P(("groups", "freq"), None),
            P("groups", "freq", None),
            P("groups"),
            P(),
            P(),
            P("freq", None),
            P(),
            P(),
        ),
        out_specs=(P("groups", None), P("groups", None), P("groups", None), P("groups", None)),
        check_vma=False,
    )
```

```python
import functools
import math

import jax
import ml_dtypes
import numpy as np
import jax.numpy as jnp
from jax import lax
from jax.experimental import pallas as pl
from jax.experimental.pallas import tpu as pltpu
from jax.sharding import PartitionSpec as P


def rotation_tables(antennas):
    indices = np.arange(antennas, dtype=np.int32)
    products_mod = indices[:, None] * indices[None, :] % antennas
    angle_table = products_mod.astype(np.float32) * np.float32(2.0 * math.pi / antennas)
    cosine_table = np.cos(angle_table) / np.float32(math.sqrt(antennas))
    sine_table = np.sin(angle_table) / np.float32(math.sqrt(antennas))
    forward_transform = np.concatenate(
        [
            np.concatenate([cosine_table, -sine_table], 1),
            np.concatenate([sine_table, cosine_table], 1),
        ],
        0,
    )
    inverse_transform = np.concatenate(
        [
            np.concatenate([cosine_table, sine_table], 1),
            np.concatenate([-sine_table, cosine_table], 1),
        ],
        0,
    )
    return (
        jnp.asarray(forward_transform.astype(ml_dtypes.bfloat16)),
        jnp.asarray(inverse_transform.astype(ml_dtypes.bfloat16)),
    )


def decode_rows(
    mixed_in,
    wanted_lines,
    output_weight,
    spectral_filter_weight,
    forward_transform,
    inverse_transform,
    loss_scale,
):
    filter_re = spectral_filter_weight[0]
    filter_im = spectral_filter_weight[1]
    spectrum = jnp.dot(mixed_in, forward_transform, preferred_element_type=jnp.float32)
    half_width = spectrum.shape[1] // 2
    spec_re = spectrum[:, :half_width]
    spec_im = spectrum[:, half_width:]
    filtered = jnp.concatenate(
        [spec_re * filter_re - spec_im * filter_im, spec_re * filter_im + spec_im * filter_re], 1
    ).astype(jnp.bfloat16)
    mixed_back = jnp.dot(filtered, inverse_transform, preferred_element_type=jnp.float32)
    hidden = (mixed_in.astype(jnp.float32) + jax.nn.gelu(mixed_back)).astype(jnp.bfloat16)
    rebuilt = hidden.astype(jnp.float32) + jnp.dot(
        hidden, output_weight, preferred_element_type=jnp.float32
    )
    residual = loss_scale * (rebuilt - wanted_lines.astype(jnp.float32))
    residual_half = residual.astype(jnp.bfloat16)
    grad_out = lax.dot_general(
        hidden, residual_half, (((0,), (0,)), ((), ())), preferred_element_type=jnp.float32
    )
    grad_hidden = residual + lax.dot_general(
        residual_half, output_weight, (((1,), (1,)), ((), ())), preferred_element_type=jnp.float32
    )
    grad_mixed = jax.vjp(jax.nn.gelu, mixed_back)[1](grad_hidden)[0].astype(jnp.bfloat16)
    grad_filtered = lax.dot_general(
        grad_mixed, inverse_transform, (((1,), (1,)), ((), ())), preferred_element_type=jnp.float32
    )
    grad_re = grad_filtered[:, :half_width]
    grad_im = grad_filtered[:, half_width:]
    grad_filter = jnp.stack(
        [
            jnp.sum(grad_re * spec_re + grad_im * spec_im, 0),
            jnp.sum(grad_im * spec_re - grad_re * spec_im, 0),
        ]
    )
    grad_spec = jnp.concatenate(
        [grad_re * filter_re + grad_im * filter_im, grad_im * filter_re - grad_re * filter_im], 1
    ).astype(jnp.bfloat16)
    derivative_entering = grad_hidden + lax.dot_general(
        grad_spec, forward_transform, (((1,), (1,)), ((), ())), preferred_element_type=jnp.float32
    )
    return (derivative_entering, grad_out, grad_filter)


def encoder_grads(inputs_rows, codewords, latent_sums, decoder_weight):
    latent_half = latent_sums.astype(jnp.bfloat16)
    grad_dec = lax.dot_general(
        codewords, latent_half, (((0,), (0,)), ((), ())), preferred_element_type=jnp.float32
    )
    grad_codes = lax.dot_general(
        latent_half, decoder_weight, (((1,), (1,)), ((), ())), preferred_element_type=jnp.float32
    )
    grad_pre = (grad_codes * (1.0 - jnp.square(codewords.astype(jnp.float32)))).astype(jnp.bfloat16)
    grad_enc = lax.dot_general(
        inputs_rows, grad_pre, (((0,), (0,)), ((), ())), preferred_element_type=jnp.float32
    )
    return (grad_enc, grad_dec)


def _exchange_pairs(count, distance):
    return [(i, i ^ distance) for i in range(count)]


def _is_power_of_two(count):
    return count > 0 and count & (count - 1) == 0


def gather_rows(block, axis_name):
    count = lax.axis_size(axis_name)
    if not _is_power_of_two(count):
        return lax.all_gather(block, axis_name, axis=0, tiled=True)
    position = lax.axis_index(axis_name)
    distance = 1
    while distance < count:
        other = lax.ppermute(block, axis_name, _exchange_pairs(count, distance))
        lower = (position // distance) % 2 == 0
        block = jnp.where(
            lower, jnp.concatenate([block, other], 0), jnp.concatenate([other, block], 0)
        )
        distance *= 2
    return block


def sum_whole(values, axis_name):
    count = lax.axis_size(axis_name)
    if not _is_power_of_two(count):
        return lax.psum(values, axis_name)
    distance = 1
    while distance < count:
        values = values + lax.ppermute(values, axis_name, _exchange_pairs(count, distance))
        distance *= 2
    return values


def sum_halving(values, axis_name, wire=jnp.bfloat16, halving_levels=2):
    count = lax.axis_size(axis_name)
    if not _is_power_of_two(count) or values.shape[0] % count != 0:
        return lax.psum(values, axis_name)
    position = lax.axis_index(axis_name)
    distance = 1
    while distance < count and distance < 2**halving_levels:
        half = values.shape[0] // 2
        lower = (position // distance) % 2 == 0
        keep = jnp.where(lower, values[:half], values[half:])
        send = jnp.where(lower, values[half:], values[:half]).astype(wire)
        arrived = lax.ppermute(send, axis_name, _exchange_pairs(count, distance))
        values = keep + arrived.astype(keep.dtype)
        distance *= 2
    top = distance
    values = values.astype(wire)
    while distance < count:
        arrived = lax.ppermute(values, axis_name, _exchange_pairs(count, distance))
        values = (values.astype(jnp.float32) + arrived.astype(jnp.float32)).astype(wire)
        distance *= 2
    distance = top // 2
    while distance >= 1:
        other = lax.ppermute(values, axis_name, _exchange_pairs(count, distance))
        lower = (position // distance) % 2 == 0
        values = jnp.where(
            lower, jnp.concatenate([values, other], 0), jnp.concatenate([other, values], 0)
        )
        distance //= 2
    return values


def _encoder_tail_kernel(
    rows_out,
    samples,
    packed_ref,
    selection_ref,
    codes_ref,
    codes_t_ref,
    decoder_ref,
    inputs_t_ref,
    grad_enc_ref,
    grad_dec_ref,
    grad_out_ref,
    grad_filter_ref,
    grad_pre_ref,
):
    @pl.when(pl.program_id(0) == 0)
    def _():
        grad_out_ref[...] = packed_ref[pl.ds(0, rows_out), :].astype(jnp.float32)
        sums = packed_ref[pl.ds(rows_out, samples), :]
        latent_half = jnp.dot(
            selection_ref[...], sums, preferred_element_type=jnp.float32
        ).astype(jnp.bfloat16)
        grad_dec_ref[...] = jnp.dot(
            codes_t_ref[...], latent_half, preferred_element_type=jnp.float32
        )
        grad_codes = lax.dot_general(
            latent_half,
            decoder_ref[...],
            (((1,), (1,)), ((), ())),
            preferred_element_type=jnp.float32,
        )
        codes = codes_ref[...].astype(jnp.float32)
        grad_pre_ref[...] = (grad_codes * (1.0 - jnp.square(codes))).astype(jnp.bfloat16)
        filter_row = packed_ref[pl.ds(rows_out + samples, 1), :].astype(jnp.float32)
        half = filter_row.shape[1] // 2
        grad_filter_ref[pl.ds(0, 1), :] = filter_row[:, :half]
        grad_filter_ref[pl.ds(1, 1), :] = filter_row[:, half:]

    grad_enc_ref[...] = jnp.dot(
        inputs_t_ref[...], grad_pre_ref[...], preferred_element_type=jnp.float32
    )


def encoder_tail(packed, rows_out, samples, selection_t, codes, decoder_weight, inputs_rows):
    width = packed.shape[1]
    enc_in = inputs_rows.shape[1]
    code = codes.shape[1]
    steps = 4 if enc_in % (4 * 8) == 0 else 1
    tile = enc_in // steps
    whole = lambda shape: pl.BlockSpec(shape, lambda i: (0,) * len(shape))
    return pl.pallas_call(
        functools.partial(_encoder_tail_kernel, rows_out, samples),
        grid=(steps,),
        in_specs=[
            whole(packed.shape),
            whole(selection_t.shape),
            whole(codes.shape),
            whole((code, samples)),
            whole(decoder_weight.shape),
            pl.BlockSpec((tile, samples), lambda i: (i, 0)),
        ],
        out_specs=[
            pl.BlockSpec((tile, code), lambda i: (i, 0)),
            whole((code, width)),
            whole((rows_out, width)),
            whole((2, width // 2)),
        ],
        out_shape=[
            jax.ShapeDtypeStruct((enc_in, code), jnp.float32),
            jax.ShapeDtypeStruct((code, width), jnp.float32),
            jax.ShapeDtypeStruct((rows_out, width), jnp.float32),
            jax.ShapeDtypeStruct((2, width // 2), jnp.float32),
        ],
        scratch_shapes=[pltpu.VMEM((samples, code), jnp.bfloat16)],
        compiler_params=pltpu.CompilerParams(dimension_semantics=("arbitrary",)),
    )(packed, selection_t, codes, codes.T, decoder_weight, inputs_rows.T)


def local(
    encoder_input,
    desired_responses,
    sample_index,
    encoder_weight,
    decoder_weight,
    frequency_amplitude,
    spectral_filter_weight,
    output_weight,
):
    samples = sample_index.shape[0]
    sub_dev = desired_responses.shape[1]
    width = desired_responses.shape[2]
    forward_transform, inverse_transform = rotation_tables(width // 2)
    loss_scale = 1.0 / math.sqrt(samples * sub_dev * lax.axis_size("freq"))
    all_inputs = gather_rows(encoder_input, "freq")
    codes = jnp.tanh(
        jnp.dot(all_inputs, encoder_weight, preferred_element_type=jnp.float32)
    ).astype(jnp.bfloat16)
    selection = (
        sample_index[None, :] == jnp.arange(samples, dtype=jnp.int32)[:, None]
    ).astype(jnp.bfloat16)
    codes_by_sample = jnp.dot(selection, codes, preferred_element_type=jnp.float32).astype(
        jnp.bfloat16
    )
    latent = jnp.dot(codes_by_sample, decoder_weight, preferred_element_type=jnp.float32)
    gain_row_values = frequency_amplitude.astype(jnp.float32)
    mixed_in = (latent[:, None, :] * gain_row_values[None]).astype(jnp.bfloat16).reshape(-1, width)
    wanted_lines = desired_responses.reshape(-1, width)
    derivative_entering, grad_out, grad_filter = decode_rows(
        mixed_in,
        wanted_lines,
        output_weight,
        spectral_filter_weight,
        forward_transform,
        inverse_transform,
        loss_scale,
    )
    derivative_bottleneck = jnp.einsum(
        "orm,rm->om", derivative_entering.reshape(samples, sub_dev, width), gain_row_values
    )
    count = lax.axis_size("freq")
    packed_rows = samples + 1 + grad_out.shape[0]
    padding = -packed_rows % count
    packed = jnp.concatenate(
        [
            grad_out,
            derivative_bottleneck,
            grad_filter.reshape(1, -1),
            jnp.zeros((padding, width), jnp.float32),
        ],
        0,
    )
    packed = sum_halving(packed, "freq")
    selection_t = (
        sample_index[:, None] == jnp.arange(samples, dtype=jnp.int32)[None, :]
    ).astype(jnp.bfloat16)
    grad_enc, grad_dec, grad_out, grad_filter = encoder_tail(
        packed, grad_out.shape[0], samples, selection_t, codes, decoder_weight, all_inputs
    )
    return (grad_enc, grad_dec, grad_out, grad_filter)


def solution(mesh):
    return jax.shard_map(
        local,
        mesh=mesh,
        in_specs=(
            P(("groups", "freq"), None),
            P("groups", "freq", None),
            P("groups"),
            P(),
            P(),
            P("freq", None),
            P(),
            P(),
        ),
        out_specs=(P("groups", None), P("groups", None), P("groups", None), P("groups", None)),
        check_vma=False,
    )
```

```python
import functools
import math

import jax
import ml_dtypes
import numpy as np
import jax.numpy as jnp
from jax import lax
from jax.experimental import pallas as pl
from jax.experimental.pallas import tpu as pltpu
from jax.sharding import PartitionSpec as P


def rotation_tables(antennas):
    indices = np.arange(antennas, dtype=np.int32)
    products_mod = indices[:, None] * indices[None, :] % antennas
    angle_table = products_mod.astype(np.float32) * np.float32(2.0 * math.pi / antennas)
    cosine_table = np.cos(angle_table) / np.float32(math.sqrt(antennas))
    sine_table = np.sin(angle_table) / np.float32(math.sqrt(antennas))
    forward_transform = np.concatenate(
        [
            np.concatenate([cosine_table, -sine_table], 1),
            np.concatenate([sine_table, cosine_table], 1),
        ],
        0,
    )
    inverse_transform = np.concatenate(
        [
            np.concatenate([cosine_table, sine_table], 1),
            np.concatenate([-sine_table, cosine_table], 1),
        ],
        0,
    )
    return (
        jnp.asarray(forward_transform.astype(ml_dtypes.bfloat16)),
        jnp.asarray(inverse_transform.astype(ml_dtypes.bfloat16)),
    )


def decode_rows(
    mixed_in,
    wanted_lines,
    output_weight,
    spectral_filter_weight,
    forward_transform,
    inverse_transform,
    loss_scale,
):
    filter_re = spectral_filter_weight[0]
    filter_im = spectral_filter_weight[1]
    spectrum = jnp.dot(mixed_in, forward_transform, preferred_element_type=jnp.float32)
    half_width = spectrum.shape[1] // 2
    spec_re = spectrum[:, :half_width]
    spec_im = spectrum[:, half_width:]
    filtered = jnp.concatenate(
        [spec_re * filter_re - spec_im * filter_im, spec_re * filter_im + spec_im * filter_re], 1
    ).astype(jnp.bfloat16)
    mixed_back = jnp.dot(filtered, inverse_transform, preferred_element_type=jnp.float32)
    hidden = (mixed_in.astype(jnp.float32) + jax.nn.gelu(mixed_back)).astype(jnp.bfloat16)
    rebuilt = hidden.astype(jnp.float32) + jnp.dot(
        hidden, output_weight, preferred_element_type=jnp.float32
    )
    residual = loss_scale * (rebuilt - wanted_lines.astype(jnp.float32))
    residual_half = residual.astype(jnp.bfloat16)
    grad_out = lax.dot_general(
        hidden, residual_half, (((0,), (0,)), ((), ())), preferred_element_type=jnp.float32
    )
    grad_hidden = residual + lax.dot_general(
        residual_half, output_weight, (((1,), (1,)), ((), ())), preferred_element_type=jnp.float32
    )
    grad_mixed = jax.vjp(jax.nn.gelu, mixed_back)[1](grad_hidden)[0].astype(jnp.bfloat16)
    grad_filtered = lax.dot_general(
        grad_mixed, inverse_transform, (((1,), (1,)), ((), ())), preferred_element_type=jnp.float32
    )
    grad_re = grad_filtered[:, :half_width]
    grad_im = grad_filtered[:, half_width:]
    grad_filter = jnp.stack(
        [
            jnp.sum(grad_re * spec_re + grad_im * spec_im, 0),
            jnp.sum(grad_im * spec_re - grad_re * spec_im, 0),
        ]
    )
    grad_spec = jnp.concatenate(
        [grad_re * filter_re + grad_im * filter_im, grad_im * filter_re - grad_re * filter_im], 1
    ).astype(jnp.bfloat16)
    derivative_entering = grad_hidden + lax.dot_general(
        grad_spec, forward_transform, (((1,), (1,)), ((), ())), preferred_element_type=jnp.float32
    )
    return (derivative_entering, grad_out, grad_filter)


def encoder_grads(inputs_rows, codewords, latent_sums, decoder_weight):
    latent_half = latent_sums.astype(jnp.bfloat16)
    grad_dec = lax.dot_general(
        codewords, latent_half, (((0,), (0,)), ((), ())), preferred_element_type=jnp.float32
    )
    grad_codes = lax.dot_general(
        latent_half, decoder_weight, (((1,), (1,)), ((), ())), preferred_element_type=jnp.float32
    )
    grad_pre = (grad_codes * (1.0 - jnp.square(codewords.astype(jnp.float32)))).astype(jnp.bfloat16)
    grad_enc = lax.dot_general(
        inputs_rows, grad_pre, (((0,), (0,)), ((), ())), preferred_element_type=jnp.float32
    )
    return (grad_enc, grad_dec)


def _exchange_pairs(count, distance):
    return [(i, i ^ distance) for i in range(count)]


def _is_power_of_two(count):
    return count > 0 and count & (count - 1) == 0


def gather_rows(block, axis_name):
    count = lax.axis_size(axis_name)
    if not _is_power_of_two(count):
        return lax.all_gather(block, axis_name, axis=0, tiled=True)
    position = lax.axis_index(axis_name)
    distance = 1
    while distance < count:
        other = lax.ppermute(block, axis_name, _exchange_pairs(count, distance))
        lower = (position // distance) % 2 == 0
        block = jnp.where(
            lower, jnp.concatenate([block, other], 0), jnp.concatenate([other, block], 0)
        )
        distance *= 2
    return block


def sum_whole(values, axis_name):
    count = lax.axis_size(axis_name)
    if not _is_power_of_two(count):
        return lax.psum(values, axis_name)
    distance = 1
    while distance < count:
        values = values + lax.ppermute(values, axis_name, _exchange_pairs(count, distance))
        distance *= 2
    return values


def sum_halving(values, axis_name, wire=jnp.bfloat16, halving_levels=2):
    count = lax.axis_size(axis_name)
    if not _is_power_of_two(count) or values.shape[0] % count != 0:
        return lax.psum(values, axis_name)
    position = lax.axis_index(axis_name)
    distance = 1
    while distance < count and distance < 2**halving_levels:
        half = values.shape[0] // 2
        lower = (position // distance) % 2 == 0
        keep = jnp.where(lower, values[:half], values[half:])
        send = jnp.where(lower, values[half:], values[:half]).astype(wire)
        arrived = lax.ppermute(send, axis_name, _exchange_pairs(count, distance))
        values = keep + arrived.astype(keep.dtype)
        distance *= 2
    top = distance
    values = values.astype(wire)
    while distance < count:
        arrived = lax.ppermute(values, axis_name, _exchange_pairs(count, distance))
        values = (values.astype(jnp.float32) + arrived.astype(jnp.float32)).astype(wire)
        distance *= 2
    distance = top // 2
    while distance >= 1:
        other = lax.ppermute(values, axis_name, _exchange_pairs(count, distance))
        lower = (position // distance) % 2 == 0
        values = jnp.where(
            lower, jnp.concatenate([values, other], 0), jnp.concatenate([other, values], 0)
        )
        distance //= 2
    return values


_TRANSPOSED_RIGHT = (((1,), (1,)), ((), ()))


def _decoder_kernel(
    loss_scale,
    latent_ref,
    amplitude_ref,
    wanted_ref,
    filter_ref,
    forward_ref,
    inverse_ref,
    output_weight_ref,
    bottleneck_ref,
    grad_out_ref,
    grad_filter_ref,
):
    block_samples, width = latent_ref.shape
    tones = amplitude_ref.shape[0]
    half_width = width // 2
    amplitude = amplitude_ref[...].astype(jnp.float32)
    mixed_in = (
        (latent_ref[...][:, None, :] * amplitude[None])
        .reshape(block_samples * tones, width)
        .astype(jnp.bfloat16)
    )
    wanted = wanted_ref[...].astype(jnp.float32).reshape(block_samples * tones, width)
    filter_re = filter_ref[pl.ds(0, 1), :]
    filter_im = filter_ref[pl.ds(1, 1), :]
    spectrum = jnp.dot(mixed_in, forward_ref[...], preferred_element_type=jnp.float32)
    spec_re = spectrum[:, :half_width]
    spec_im = spectrum[:, half_width:]
    filtered = jnp.concatenate(
        [spec_re * filter_re - spec_im * filter_im, spec_re * filter_im + spec_im * filter_re], 1
    ).astype(jnp.bfloat16)
    mixed_back = jnp.dot(filtered, inverse_ref[...], preferred_element_type=jnp.float32)
    activated, activation_vjp = jax.vjp(jax.nn.gelu, mixed_back)
    hidden = (mixed_in.astype(jnp.float32) + activated).astype(jnp.bfloat16)
    rebuilt = hidden.astype(jnp.float32) + jnp.dot(
        hidden, output_weight_ref[...], preferred_element_type=jnp.float32
    )
    residual = loss_scale * (rebuilt - wanted)
    residual_half = residual.astype(jnp.bfloat16)
    grad_out_part = lax.dot_general(
        hidden, residual_half, (((0,), (0,)), ((), ())), preferred_element_type=jnp.float32
    )
    grad_hidden = residual + lax.dot_general(
        residual_half, output_weight_ref[...], _TRANSPOSED_RIGHT, preferred_element_type=jnp.float32
    )
    grad_mixed = activation_vjp(grad_hidden)[0].astype(jnp.bfloat16)
    grad_filtered = lax.dot_general(
        grad_mixed, inverse_ref[...], _TRANSPOSED_RIGHT, preferred_element_type=jnp.float32
    )
    grad_re = grad_filtered[:, :half_width]
    grad_im = grad_filtered[:, half_width:]
    filter_grad_re = jnp.sum(grad_re * spec_re + grad_im * spec_im, 0, keepdims=True)
    filter_grad_im = jnp.sum(grad_im * spec_re - grad_re * spec_im, 0, keepdims=True)
    grad_spec = jnp.concatenate(
        [grad_re * filter_re + grad_im * filter_im, grad_im * filter_re - grad_re * filter_im], 1
    ).astype(jnp.bfloat16)
    derivative_entering = grad_hidden + lax.dot_general(
        grad_spec, forward_ref[...], _TRANSPOSED_RIGHT, preferred_element_type=jnp.float32
    )
    bottleneck_ref[...] = jnp.sum(
        derivative_entering.reshape(block_samples, tones, width) * amplitude[None], 1
    )

    @pl.when(pl.program_id(0) == 0)
    def _():
        grad_out_ref[...] = jnp.zeros_like(grad_out_ref)
        grad_filter_ref[...] = jnp.zeros_like(grad_filter_ref)

    grad_out_ref[...] += grad_out_part
    grad_filter_ref[pl.ds(0, 1), :] += filter_grad_re
    grad_filter_ref[pl.ds(1, 1), :] += filter_grad_im


def decode_block(
    latent,
    frequency_amplitude,
    desired_responses,
    spectral_filter_weight,
    forward_transform,
    inverse_transform,
    output_weight,
    loss_scale,
):
    samples, tones, width = desired_responses.shape
    block_samples = 8 if samples % 8 == 0 else samples
    whole = lambda shape: pl.BlockSpec(shape, lambda i: (0,) * len(shape))
    return pl.pallas_call(
        functools.partial(_decoder_kernel, loss_scale),
        grid=(samples // block_samples,),
        in_specs=[
            pl.BlockSpec((block_samples, width), lambda i: (i, 0)),
            whole(frequency_amplitude.shape),
            pl.BlockSpec((block_samples, tones, width), lambda i: (i, 0, 0)),
            whole(spectral_filter_weight.shape),
            whole(forward_transform.shape),
            whole(inverse_transform.shape),
            whole(output_weight.shape),
        ],
        out_specs=[
            pl.BlockSpec((block_samples, width), lambda i: (i, 0)),
            whole((width, width)),
            whole(spectral_filter_weight.shape),
        ],
        out_shape=[
            jax.ShapeDtypeStruct((samples, width), jnp.float32),
            jax.ShapeDtypeStruct((width, width), jnp.float32),
            jax.ShapeDtypeStruct(spectral_filter_weight.shape, jnp.float32),
        ],
        compiler_params=pltpu.CompilerParams(dimension_semantics=("arbitrary",)),
    )(
        latent,
        frequency_amplitude,
        desired_responses,
        spectral_filter_weight,
        forward_transform,
        inverse_transform,
        output_weight,
    )


def local(
    encoder_input,
    desired_responses,
    sample_index,
    encoder_weight,
    decoder_weight,
    frequency_amplitude,
    spectral_filter_weight,
    output_weight,
):
    samples = sample_index.shape[0]
    sub_dev = desired_responses.shape[1]
    width = desired_responses.shape[2]
    forward_transform, inverse_transform = rotation_tables(width // 2)
    loss_scale = 1.0 / math.sqrt(samples * sub_dev * lax.axis_size("freq"))
    all_inputs = gather_rows(encoder_input, "freq")
    codes = jnp.tanh(
        jnp.dot(all_inputs, encoder_weight, preferred_element_type=jnp.float32)
    ).astype(jnp.bfloat16)
    selection = (
        sample_index[None, :] == jnp.arange(samples, dtype=jnp.int32)[:, None]
    ).astype(jnp.bfloat16)
    codes_by_sample = jnp.dot(selection, codes, preferred_element_type=jnp.float32).astype(
        jnp.bfloat16
    )
    latent = jnp.dot(codes_by_sample, decoder_weight, preferred_element_type=jnp.float32)
    derivative_bottleneck, grad_out, grad_filter = decode_block(
        latent,
        frequency_amplitude,
        desired_responses,
        spectral_filter_weight,
        forward_transform,
        inverse_transform,
        output_weight,
        loss_scale,
    )
    count = lax.axis_size("freq")
    packed_rows = samples + 1 + grad_out.shape[0]
    padding = -packed_rows % count
    packed = jnp.concatenate(
        [
            grad_out,
            derivative_bottleneck,
            grad_filter.reshape(1, -1),
            jnp.zeros((padding, width), jnp.float32),
        ],
        0,
    )
    packed = sum_halving(packed, "freq")
    rows_out = grad_out.shape[0]
    grad_out = packed[:rows_out].astype(jnp.float32)
    derivative_bottleneck = packed[rows_out : rows_out + samples].astype(jnp.float32)
    grad_filter = packed[rows_out + samples].astype(jnp.float32).reshape(grad_filter.shape)
    grad_enc, grad_dec = encoder_grads(
        all_inputs, codes, derivative_bottleneck[sample_index], decoder_weight
    )
    return (grad_enc, grad_dec, grad_out, grad_filter)


def solution(mesh):
    return jax.shard_map(
        local,
        mesh=mesh,
        in_specs=(
            P(("groups", "freq"), None),
            P("groups", "freq", None),
            P("groups"),
            P(),
            P(),
            P("freq", None),
            P(),
            P(),
        ),
        out_specs=(P("groups", None), P("groups", None), P("groups", None), P("groups", None)),
        check_vma=False,
    )
```

```python
import math

import jax
import ml_dtypes
import numpy as np
import jax.numpy as jnp
from jax import lax
from jax.sharding import PartitionSpec as P


def rotation_tables(antennas):
    indices = np.arange(antennas, dtype=np.int32)
    products_mod = indices[:, None] * indices[None, :] % antennas
    angle_table = products_mod.astype(np.float32) * np.float32(2.0 * math.pi / antennas)
    cosine_table = np.cos(angle_table) / np.float32(math.sqrt(antennas))
    sine_table = np.sin(angle_table) / np.float32(math.sqrt(antennas))
    forward_transform = np.concatenate(
        [
            np.concatenate([cosine_table, -sine_table], 1),
            np.concatenate([sine_table, cosine_table], 1),
        ],
        0,
    )
    inverse_transform = np.concatenate(
        [
            np.concatenate([cosine_table, sine_table], 1),
            np.concatenate([-sine_table, cosine_table], 1),
        ],
        0,
    )
    return (
        jnp.asarray(forward_transform.astype(ml_dtypes.bfloat16)),
        jnp.asarray(inverse_transform.astype(ml_dtypes.bfloat16)),
    )


def decode_rows(
    mixed_in,
    wanted_lines,
    output_weight,
    spectral_filter_weight,
    forward_transform,
    inverse_transform,
    loss_scale,
):
    filter_re = spectral_filter_weight[0]
    filter_im = spectral_filter_weight[1]
    spectrum = jnp.dot(mixed_in, forward_transform, preferred_element_type=jnp.float32)
    half_width = spectrum.shape[1] // 2
    spec_re = spectrum[:, :half_width]
    spec_im = spectrum[:, half_width:]
    filtered = jnp.concatenate(
        [spec_re * filter_re - spec_im * filter_im, spec_re * filter_im + spec_im * filter_re], 1
    ).astype(jnp.bfloat16)
    mixed_back = lax.dot_general(
        filtered, forward_transform, (((1,), (1,)), ((), ())), preferred_element_type=jnp.float32
    )
    hidden = (mixed_in.astype(jnp.float32) + jax.nn.gelu(mixed_back)).astype(jnp.bfloat16)
    rebuilt = hidden.astype(jnp.float32) + jnp.dot(
        hidden, output_weight, preferred_element_type=jnp.float32
    )
    residual = loss_scale * (rebuilt - wanted_lines.astype(jnp.float32))
    residual_half = residual.astype(jnp.bfloat16)
    grad_out = lax.dot_general(
        hidden, residual_half, (((0,), (0,)), ((), ())), preferred_element_type=jnp.float32
    )
    grad_hidden = residual + lax.dot_general(
        residual_half, output_weight, (((1,), (1,)), ((), ())), preferred_element_type=jnp.float32
    )
    grad_mixed = jax.vjp(jax.nn.gelu, mixed_back)[1](grad_hidden)[0].astype(jnp.bfloat16)
    grad_filtered = jnp.dot(grad_mixed, forward_transform, preferred_element_type=jnp.float32)
    grad_re = grad_filtered[:, :half_width]
    grad_im = grad_filtered[:, half_width:]
    grad_filter = jnp.stack(
        [
            jnp.sum(grad_re * spec_re + grad_im * spec_im, 0),
            jnp.sum(grad_im * spec_re - grad_re * spec_im, 0),
        ]
    )
    grad_spec = jnp.concatenate(
        [grad_re * filter_re + grad_im * filter_im, grad_im * filter_re - grad_re * filter_im], 1
    ).astype(jnp.bfloat16)
    derivative_entering = grad_hidden + lax.dot_general(
        grad_spec, forward_transform, (((1,), (1,)), ((), ())), preferred_element_type=jnp.float32
    )
    return (derivative_entering, grad_out, grad_filter)


def encoder_grads(inputs_rows, codewords, latent_sums, decoder_weight):
    latent_half = latent_sums.astype(jnp.bfloat16)
    grad_dec = lax.dot_general(
        codewords, latent_half, (((0,), (0,)), ((), ())), preferred_element_type=jnp.float32
    )
    grad_codes = lax.dot_general(
        latent_half, decoder_weight, (((1,), (1,)), ((), ())), preferred_element_type=jnp.float32
    )
    grad_pre = (grad_codes * (1.0 - jnp.square(codewords.astype(jnp.float32)))).astype(jnp.bfloat16)
    grad_enc = lax.dot_general(
        inputs_rows, grad_pre, (((0,), (0,)), ((), ())), preferred_element_type=jnp.float32
    )
    return (grad_enc, grad_dec)


def _exchange_pairs(count, distance):
    return [(i, i ^ distance) for i in range(count)]


def _is_power_of_two(count):
    return count > 0 and count & (count - 1) == 0


def gather_rows(block, axis_name):
    count = lax.axis_size(axis_name)
    if not _is_power_of_two(count):
        return lax.all_gather(block, axis_name, axis=0, tiled=True)
    position = lax.axis_index(axis_name)
    distance = 1
    while distance < count:
        other = lax.ppermute(block, axis_name, _exchange_pairs(count, distance))
        lower = (position // distance) % 2 == 0
        block = jnp.where(
            lower, jnp.concatenate([block, other], 0), jnp.concatenate([other, block], 0)
        )
        distance *= 2
    return block


def sum_whole(values, axis_name):
    count = lax.axis_size(axis_name)
    if not _is_power_of_two(count):
        return lax.psum(values, axis_name)
    distance = 1
    while distance < count:
        values = values + lax.ppermute(values, axis_name, _exchange_pairs(count, distance))
        distance *= 2
    return values


def sum_halving(values, axis_name, wire=jnp.bfloat16, halving_levels=2):
    count = lax.axis_size(axis_name)
    if not _is_power_of_two(count) or values.shape[0] % count != 0:
        return lax.psum(values, axis_name)
    position = lax.axis_index(axis_name)
    distance = 1
    while distance < count and distance < 2**halving_levels:
        half = values.shape[0] // 2
        lower = (position // distance) % 2 == 0
        keep = jnp.where(lower, values[:half], values[half:])
        send = jnp.where(lower, values[half:], values[:half]).astype(wire)
        arrived = lax.ppermute(send, axis_name, _exchange_pairs(count, distance))
        values = keep + arrived.astype(keep.dtype)
        distance *= 2
    top = distance
    values = values.astype(wire)
    while distance < count:
        arrived = lax.ppermute(values, axis_name, _exchange_pairs(count, distance))
        values = (values.astype(jnp.float32) + arrived.astype(jnp.float32)).astype(wire)
        distance *= 2
    distance = top // 2
    while distance >= 1:
        other = lax.ppermute(values, axis_name, _exchange_pairs(count, distance))
        lower = (position // distance) % 2 == 0
        values = jnp.where(
            lower, jnp.concatenate([values, other], 0), jnp.concatenate([other, values], 0)
        )
        distance //= 2
    return values


def local(
    encoder_input,
    desired_responses,
    sample_index,
    encoder_weight,
    decoder_weight,
    frequency_amplitude,
    spectral_filter_weight,
    output_weight,
):
    samples = sample_index.shape[0]
    sub_dev = desired_responses.shape[1]
    width = desired_responses.shape[2]
    forward_transform, inverse_transform = rotation_tables(width // 2)
    loss_scale = 1.0 / math.sqrt(samples * sub_dev * lax.axis_size("freq"))
    all_inputs = gather_rows(encoder_input, "freq")
    codes = jnp.tanh(
        jnp.dot(all_inputs, encoder_weight, preferred_element_type=jnp.float32)
    ).astype(jnp.bfloat16)
    selection = (
        sample_index[None, :] == jnp.arange(samples, dtype=jnp.int32)[:, None]
    ).astype(jnp.bfloat16)
    codes_by_sample = jnp.dot(selection, codes, preferred_element_type=jnp.float32).astype(
        jnp.bfloat16
    )
    latent = jnp.dot(codes_by_sample, decoder_weight, preferred_element_type=jnp.float32)
    gain_row_values = frequency_amplitude.astype(jnp.float32)
    mixed_in = (latent[:, None, :] * gain_row_values[None]).astype(jnp.bfloat16).reshape(-1, width)
    wanted_lines = desired_responses.reshape(-1, width)
    derivative_entering, grad_out, grad_filter = decode_rows(
        mixed_in,
        wanted_lines,
        output_weight,
        spectral_filter_weight,
        forward_transform,
        inverse_transform,
        loss_scale,
    )
    derivative_bottleneck = jnp.einsum(
        "orm,rm->om", derivative_entering.reshape(samples, sub_dev, width), gain_row_values
    )
    count = lax.axis_size("freq")
    packed_rows = samples + 1 + grad_out.shape[0]
    padding = -packed_rows % count
    packed = jnp.concatenate(
        [
            grad_out,
            derivative_bottleneck,
            grad_filter.reshape(1, -1),
            jnp.zeros((padding, width), jnp.float32),
        ],
        0,
    )
    packed = sum_halving(packed, "freq")
    rows_out = grad_out.shape[0]
    grad_out = packed[:rows_out].astype(jnp.float32)
    derivative_bottleneck = packed[rows_out : rows_out + samples].astype(jnp.float32)
    grad_filter = packed[rows_out + samples].astype(jnp.float32).reshape(grad_filter.shape)
    grad_enc, grad_dec = encoder_grads(
        all_inputs, codes, derivative_bottleneck[sample_index], decoder_weight
    )
    return (grad_enc, grad_dec, grad_out, grad_filter)


def solution(mesh):
    return jax.shard_map(
        local,
        mesh=mesh,
        in_specs=(
            P(("groups", "freq"), None),
            P("groups", "freq", None),
            P("groups"),
            P(),
            P(),
            P("freq", None),
            P(),
            P(),
        ),
        out_specs=(P("groups", None), P("groups", None), P("groups", None), P("groups", None)),
        check_vma=False,
    )
```

```python
import math

import jax
import ml_dtypes
import numpy as np
import jax.numpy as jnp
from jax import lax
from jax.sharding import PartitionSpec as P


def rotation_tables(antennas):
    indices = np.arange(antennas, dtype=np.int32)
    products_mod = indices[:, None] * indices[None, :] % antennas
    angle_table = products_mod.astype(np.float32) * np.float32(2.0 * math.pi / antennas)
    cosine_table = np.cos(angle_table) / np.float32(math.sqrt(antennas))
    sine_table = np.sin(angle_table) / np.float32(math.sqrt(antennas))
    forward_transform = np.concatenate(
        [
            np.concatenate([cosine_table, -sine_table], 1),
            np.concatenate([sine_table, cosine_table], 1),
        ],
        0,
    )
    inverse_transform = np.concatenate(
        [
            np.concatenate([cosine_table, sine_table], 1),
            np.concatenate([-sine_table, cosine_table], 1),
        ],
        0,
    )
    return (
        jnp.asarray(forward_transform.astype(ml_dtypes.bfloat16)),
        jnp.asarray(inverse_transform.astype(ml_dtypes.bfloat16)),
    )


def decode_rows(
    mixed_in,
    wanted_lines,
    output_weight,
    spectral_filter_weight,
    forward_transform,
    inverse_transform,
    loss_scale,
):
    filter_re = spectral_filter_weight[0]
    filter_im = spectral_filter_weight[1]
    spectrum = jnp.dot(mixed_in, forward_transform, preferred_element_type=jnp.float32)
    half_width = spectrum.shape[1] // 2
    spec_re = spectrum[:, :half_width]
    spec_im = spectrum[:, half_width:]
    filtered = jnp.concatenate(
        [spec_re * filter_re - spec_im * filter_im, spec_re * filter_im + spec_im * filter_re], 1
    ).astype(jnp.bfloat16)
    mixed_back = lax.dot_general(
        filtered, forward_transform, (((1,), (1,)), ((), ())), preferred_element_type=jnp.float32
    )
    hidden = (mixed_in.astype(jnp.float32) + jax.nn.gelu(mixed_back)).astype(jnp.bfloat16)
    rebuilt = hidden.astype(jnp.float32) + jnp.dot(
        hidden, output_weight, preferred_element_type=jnp.float32
    )
    residual = loss_scale * (rebuilt - wanted_lines.astype(jnp.float32))
    residual_half = residual.astype(jnp.bfloat16)
    grad_out = lax.dot_general(
        hidden, residual_half, (((0,), (0,)), ((), ())), preferred_element_type=jnp.float32
    )
    grad_hidden = residual + lax.dot_general(
        residual_half, output_weight, (((1,), (1,)), ((), ())), preferred_element_type=jnp.float32
    )
    grad_mixed = jax.vjp(jax.nn.gelu, mixed_back)[1](grad_hidden)[0].astype(jnp.bfloat16)
    grad_filtered = jnp.dot(grad_mixed, forward_transform, preferred_element_type=jnp.float32)
    grad_re = grad_filtered[:, :half_width]
    grad_im = grad_filtered[:, half_width:]
    grad_filter = jnp.stack(
        [
            jnp.sum(grad_re * spec_re + grad_im * spec_im, 0),
            jnp.sum(grad_im * spec_re - grad_re * spec_im, 0),
        ]
    )
    grad_spec = jnp.concatenate(
        [grad_re * filter_re + grad_im * filter_im, grad_im * filter_re - grad_re * filter_im], 1
    ).astype(jnp.bfloat16)
    derivative_entering = grad_hidden + lax.dot_general(
        grad_spec, forward_transform, (((1,), (1,)), ((), ())), preferred_element_type=jnp.float32
    )
    return (derivative_entering, grad_out, grad_filter)


def encoder_grads(inputs_rows, codewords, latent_sums, decoder_weight):
    latent_half = latent_sums.astype(jnp.bfloat16)
    grad_dec = lax.dot_general(
        codewords, latent_half, (((0,), (0,)), ((), ())), preferred_element_type=jnp.float32
    )
    grad_codes = lax.dot_general(
        latent_half, decoder_weight, (((1,), (1,)), ((), ())), preferred_element_type=jnp.float32
    )
    grad_pre = (grad_codes * (1.0 - jnp.square(codewords.astype(jnp.float32)))).astype(jnp.bfloat16)
    grad_enc = lax.dot_general(
        inputs_rows, grad_pre, (((0,), (0,)), ((), ())), preferred_element_type=jnp.float32
    )
    return (grad_enc, grad_dec)


def _exchange_pairs(count, distance):
    return [(i, i ^ distance) for i in range(count)]


def _is_power_of_two(count):
    return count > 0 and count & (count - 1) == 0


def gather_rows(block, axis_name):
    count = lax.axis_size(axis_name)
    if not _is_power_of_two(count):
        return lax.all_gather(block, axis_name, axis=0, tiled=True)
    position = lax.axis_index(axis_name)
    distance = 1
    while distance < count:
        other = lax.ppermute(block, axis_name, _exchange_pairs(count, distance))
        lower = (position // distance) % 2 == 0
        block = jnp.where(
            lower, jnp.concatenate([block, other], 0), jnp.concatenate([other, block], 0)
        )
        distance *= 2
    return block


def sum_whole(values, axis_name):
    count = lax.axis_size(axis_name)
    if not _is_power_of_two(count):
        return lax.psum(values, axis_name)
    distance = 1
    while distance < count:
        values = values + lax.ppermute(values, axis_name, _exchange_pairs(count, distance))
        distance *= 2
    return values


def sum_halving(values, axis_name, wire=jnp.bfloat16, halving_levels=2):
    count = lax.axis_size(axis_name)
    if not _is_power_of_two(count) or values.shape[0] % count != 0:
        return lax.psum(values, axis_name)
    position = lax.axis_index(axis_name)
    distance = 1
    while distance < count and distance < 2**halving_levels:
        half = values.shape[0] // 2
        lower = (position // distance) % 2 == 0
        keep = jnp.where(lower, values[:half], values[half:])
        send = jnp.where(lower, values[half:], values[:half]).astype(wire)
        arrived = lax.ppermute(send, axis_name, _exchange_pairs(count, distance))
        values = keep + arrived.astype(keep.dtype)
        distance *= 2
    top = distance
    values = values.astype(wire)
    while distance < count:
        arrived = lax.ppermute(values, axis_name, _exchange_pairs(count, distance))
        values = (values.astype(jnp.float32) + arrived.astype(jnp.float32)).astype(wire)
        distance *= 2
    distance = top // 2
    while distance >= 1:
        other = lax.ppermute(values, axis_name, _exchange_pairs(count, distance))
        lower = (position // distance) % 2 == 0
        values = jnp.where(
            lower, jnp.concatenate([values, other], 0), jnp.concatenate([other, values], 0)
        )
        distance //= 2
    return values


def local(
    encoder_input,
    desired_responses,
    sample_index,
    encoder_weight,
    decoder_weight,
    frequency_amplitude,
    spectral_filter_weight,
    output_weight,
):
    samples = sample_index.shape[0]
    sub_dev = desired_responses.shape[1]
    width = desired_responses.shape[2]
    forward_transform, inverse_transform = rotation_tables(width // 2)
    loss_scale = 1.0 / math.sqrt(samples * sub_dev * lax.axis_size("freq"))
    all_inputs = gather_rows(encoder_input, "freq")
    selection = (
        sample_index[None, :] == jnp.arange(samples, dtype=jnp.int32)[:, None]
    ).astype(jnp.bfloat16)
    inputs_by_sample = jnp.dot(selection, all_inputs, preferred_element_type=jnp.float32).astype(
        jnp.bfloat16
    )
    codes_by_sample = jnp.tanh(
        jnp.dot(inputs_by_sample, encoder_weight, preferred_element_type=jnp.float32)
    ).astype(jnp.bfloat16)
    latent = jnp.dot(codes_by_sample, decoder_weight, preferred_element_type=jnp.float32)
    gain_row_values = frequency_amplitude.astype(jnp.float32)
    mixed_in = (latent[:, None, :] * gain_row_values[None]).astype(jnp.bfloat16).reshape(-1, width)
    wanted_lines = desired_responses.reshape(-1, width)
    derivative_entering, grad_out, grad_filter = decode_rows(
        mixed_in,
        wanted_lines,
        output_weight,
        spectral_filter_weight,
        forward_transform,
        inverse_transform,
        loss_scale,
    )
    derivative_bottleneck = jnp.einsum(
        "orm,rm->om", derivative_entering.reshape(samples, sub_dev, width), gain_row_values
    )
    count = lax.axis_size("freq")
    half_width = grad_filter.shape[1]
    filter_rows = jnp.concatenate(
        [grad_filter, jnp.zeros((grad_filter.shape[0], width - half_width), jnp.float32)], 1
    )
    packed_rows = grad_out.shape[0] + samples + filter_rows.shape[0]
    padding = -packed_rows % count
    packed = jnp.concatenate(
        [
            grad_out,
            derivative_bottleneck,
            filter_rows,
            jnp.zeros((padding, width), jnp.float32),
        ],
        0,
    )
    packed = sum_halving(packed, "freq")
    rows_out = grad_out.shape[0]
    grad_out = packed[:rows_out].astype(jnp.float32)
    derivative_bottleneck = packed[rows_out : rows_out + samples].astype(jnp.float32)
    grad_filter = packed[
        rows_out + samples : rows_out + samples + filter_rows.shape[0], :half_width
    ].astype(jnp.float32)
    grad_enc, grad_dec = encoder_grads(
        inputs_by_sample, codes_by_sample, derivative_bottleneck, decoder_weight
    )
    return (grad_enc, grad_dec, grad_out, grad_filter)


def solution(mesh):
    return jax.shard_map(
        local,
        mesh=mesh,
        in_specs=(
            P(("groups", "freq"), None),
            P("groups", "freq", None),
            P("groups"),
            P(),
            P(),
            P("freq", None),
            P(),
            P(),
        ),
        out_specs=(P("groups", None), P("groups", None), P("groups", None), P("groups", None)),
        check_vma=False,
    )
```

```python
import math

import jax
import ml_dtypes
import numpy as np
import jax.numpy as jnp
from jax import lax
from jax.sharding import PartitionSpec as P


def rotation_tables(antennas):
    indices = np.arange(antennas, dtype=np.int32)
    products_mod = indices[:, None] * indices[None, :] % antennas
    angle_table = products_mod.astype(np.float32) * np.float32(2.0 * math.pi / antennas)
    cosine_table = np.cos(angle_table) / np.float32(math.sqrt(antennas))
    sine_table = np.sin(angle_table) / np.float32(math.sqrt(antennas))
    forward_transform = np.concatenate(
        [
            np.concatenate([cosine_table, -sine_table], 1),
            np.concatenate([sine_table, cosine_table], 1),
        ],
        0,
    )
    inverse_transform = np.concatenate(
        [
            np.concatenate([cosine_table, sine_table], 1),
            np.concatenate([-sine_table, cosine_table], 1),
        ],
        0,
    )
    return (
        jnp.asarray(forward_transform.astype(ml_dtypes.bfloat16)),
        jnp.asarray(inverse_transform.astype(ml_dtypes.bfloat16)),
    )


def decode_rows(
    mixed_in,
    wanted_lines,
    output_weight,
    spectral_filter_weight,
    forward_transform,
    inverse_transform,
    loss_scale,
):
    filter_re = spectral_filter_weight[0]
    filter_im = spectral_filter_weight[1]
    spectrum = jnp.dot(mixed_in, forward_transform, preferred_element_type=jnp.float32)
    half_width = spectrum.shape[1] // 2
    spec_re = spectrum[:, :half_width]
    spec_im = spectrum[:, half_width:]
    filtered = jnp.concatenate(
        [spec_re * filter_re - spec_im * filter_im, spec_re * filter_im + spec_im * filter_re], 1
    ).astype(jnp.bfloat16)
    mixed_back = lax.dot_general(
        filtered, forward_transform, (((1,), (1,)), ((), ())), preferred_element_type=jnp.float32
    )
    hidden = (mixed_in.astype(jnp.float32) + jax.nn.gelu(mixed_back)).astype(jnp.bfloat16)
    rebuilt = hidden.astype(jnp.float32) + jnp.dot(
        hidden, output_weight, preferred_element_type=jnp.float32
    )
    residual = loss_scale * (rebuilt - wanted_lines.astype(jnp.float32))
    residual_half = residual.astype(jnp.bfloat16)
    grad_out = lax.dot_general(
        hidden, residual_half, (((0,), (0,)), ((), ())), preferred_element_type=jnp.float32
    )
    grad_hidden = residual + lax.dot_general(
        residual_half, output_weight, (((1,), (1,)), ((), ())), preferred_element_type=jnp.float32
    )
    grad_mixed = jax.vjp(jax.nn.gelu, mixed_back)[1](grad_hidden)[0].astype(jnp.bfloat16)
    grad_filtered = jnp.dot(grad_mixed, forward_transform, preferred_element_type=jnp.float32)
    grad_re = grad_filtered[:, :half_width]
    grad_im = grad_filtered[:, half_width:]
    grad_filter = jnp.stack(
        [
            jnp.sum(grad_re * spec_re + grad_im * spec_im, 0),
            jnp.sum(grad_im * spec_re - grad_re * spec_im, 0),
        ]
    )
    grad_spec = jnp.concatenate(
        [grad_re * filter_re + grad_im * filter_im, grad_im * filter_re - grad_re * filter_im], 1
    ).astype(jnp.bfloat16)
    derivative_entering = grad_hidden + lax.dot_general(
        grad_spec, forward_transform, (((1,), (1,)), ((), ())), preferred_element_type=jnp.float32
    )
    return (derivative_entering, grad_out, grad_filter)


def encoder_grads(inputs_rows, codewords, latent_sums, decoder_weight):
    latent_half = latent_sums.astype(jnp.bfloat16)
    grad_dec = lax.dot_general(
        codewords, latent_half, (((0,), (0,)), ((), ())), preferred_element_type=jnp.float32
    )
    grad_codes = lax.dot_general(
        latent_half, decoder_weight, (((1,), (1,)), ((), ())), preferred_element_type=jnp.float32
    )
    grad_pre = (grad_codes * (1.0 - jnp.square(codewords.astype(jnp.float32)))).astype(jnp.bfloat16)
    grad_enc = lax.dot_general(
        inputs_rows, grad_pre, (((0,), (0,)), ((), ())), preferred_element_type=jnp.float32
    )
    return (grad_enc, grad_dec)


def _exchange_pairs(count, distance):
    return [(i, i ^ distance) for i in range(count)]


def _is_power_of_two(count):
    return count > 0 and count & (count - 1) == 0


def gather_rows(block, axis_name):
    count = lax.axis_size(axis_name)
    if not _is_power_of_two(count):
        return lax.all_gather(block, axis_name, axis=0, tiled=True), np.arange(count * block.shape[0])
    position = lax.axis_index(axis_name)
    distance = count // 2
    while distance >= 1:
        other = lax.ppermute(block, axis_name, _exchange_pairs(count, distance))
        lower = (position // distance) % 2 == 0
        block = jnp.where(
            lower, jnp.concatenate([block, other], 0), jnp.concatenate([other, block], 0)
        )
        distance //= 2
    bits = count.bit_length() - 1
    rows = block.shape[0] // count
    slots = np.arange(count)
    owners = np.zeros(count, np.int64)
    for bit in range(bits):
        owners |= ((slots >> bit) & 1) << (bits - 1 - bit)
    order = (owners[:, None] * rows + np.arange(rows)[None, :]).reshape(-1)
    return block, order


def sum_whole(values, axis_name):
    count = lax.axis_size(axis_name)
    if not _is_power_of_two(count):
        return lax.psum(values, axis_name)
    distance = 1
    while distance < count:
        values = values + lax.ppermute(values, axis_name, _exchange_pairs(count, distance))
        distance *= 2
    return values


def sum_halving(values, axis_name, wire=jnp.bfloat16, halving_levels=2):
    count = lax.axis_size(axis_name)
    if not _is_power_of_two(count) or values.shape[0] % count != 0:
        return lax.psum(values, axis_name)
    position = lax.axis_index(axis_name)
    distance = 1
    while distance < count and distance < 2**halving_levels:
        half = values.shape[0] // 2
        lower = (position // distance) % 2 == 0
        keep = jnp.where(lower, values[:half], values[half:])
        send = jnp.where(lower, values[half:], values[:half]).astype(wire)
        arrived = lax.ppermute(send, axis_name, _exchange_pairs(count, distance))
        values = keep + arrived.astype(keep.dtype)
        distance *= 2
    top = distance
    values = values.astype(wire)
    while distance < count:
        arrived = lax.ppermute(values, axis_name, _exchange_pairs(count, distance))
        values = (values.astype(jnp.float32) + arrived.astype(jnp.float32)).astype(wire)
        distance *= 2
    distance = top // 2
    while distance >= 1:
        other = lax.ppermute(values, axis_name, _exchange_pairs(count, distance))
        lower = (position // distance) % 2 == 0
        values = jnp.where(
            lower, jnp.concatenate([values, other], 0), jnp.concatenate([other, values], 0)
        )
        distance //= 2
    return values


def local(
    encoder_input,
    desired_responses,
    sample_index,
    encoder_weight,
    decoder_weight,
    frequency_amplitude,
    spectral_filter_weight,
    output_weight,
):
    samples = sample_index.shape[0]
    sub_dev = desired_responses.shape[1]
    width = desired_responses.shape[2]
    forward_transform, inverse_transform = rotation_tables(width // 2)
    loss_scale = 1.0 / math.sqrt(samples * sub_dev * lax.axis_size("freq"))
    all_inputs, row_order = gather_rows(encoder_input, "freq")
    selection = (
        sample_index[row_order][None, :] == jnp.arange(samples, dtype=jnp.int32)[:, None]
    ).astype(jnp.bfloat16)
    inputs_by_sample = jnp.dot(selection, all_inputs, preferred_element_type=jnp.float32).astype(
        jnp.bfloat16
    )
    codes_by_sample = jnp.tanh(
        jnp.dot(inputs_by_sample, encoder_weight, preferred_element_type=jnp.float32)
    ).astype(jnp.bfloat16)
    latent = jnp.dot(codes_by_sample, decoder_weight, preferred_element_type=jnp.float32)
    gain_row_values = frequency_amplitude.astype(jnp.float32)
    mixed_in = (latent[:, None, :] * gain_row_values[None]).astype(jnp.bfloat16).reshape(-1, width)
    wanted_lines = desired_responses.reshape(-1, width)
    derivative_entering, grad_out, grad_filter = decode_rows(
        mixed_in,
        wanted_lines,
        output_weight,
        spectral_filter_weight,
        forward_transform,
        inverse_transform,
        loss_scale,
    )
    derivative_bottleneck = jnp.einsum(
        "orm,rm->om", derivative_entering.reshape(samples, sub_dev, width), gain_row_values
    )
    count = lax.axis_size("freq")
    half_width = grad_filter.shape[1]
    filter_rows = jnp.concatenate(
        [grad_filter, jnp.zeros((grad_filter.shape[0], width - half_width), jnp.float32)], 1
    )
    packed_rows = grad_out.shape[0] + samples + filter_rows.shape[0]
    padding = -packed_rows % count
    packed = jnp.concatenate(
        [
            grad_out,
            derivative_bottleneck,
            filter_rows,
            jnp.zeros((padding, width), jnp.float32),
        ],
        0,
    )
    packed = sum_halving(packed, "freq")
    rows_out = grad_out.shape[0]
    grad_out = packed[:rows_out].astype(jnp.float32)
    derivative_bottleneck = packed[rows_out : rows_out + samples].astype(jnp.float32)
    grad_filter = packed[
        rows_out + samples : rows_out + samples + filter_rows.shape[0], :half_width
    ].astype(jnp.float32)
    grad_enc, grad_dec = encoder_grads(
        inputs_by_sample, codes_by_sample, derivative_bottleneck, decoder_weight
    )
    return (grad_enc, grad_dec, grad_out, grad_filter)


def solution(mesh):
    return jax.shard_map(
        local,
        mesh=mesh,
        in_specs=(
            P(("groups", "freq"), None),
            P("groups", "freq", None),
            P("groups"),
            P(),
            P(),
            P("freq", None),
            P(),
            P(),
        ),
        out_specs=(P("groups", None), P("groups", None), P("groups", None), P("groups", None)),
        check_vma=False,
    )
```

```python
import math

import jax
import ml_dtypes
import numpy as np
import jax.numpy as jnp
from jax import lax
from jax.sharding import PartitionSpec as P


def rotation_tables(antennas):
    indices = np.arange(antennas, dtype=np.int32)
    products_mod = indices[:, None] * indices[None, :] % antennas
    angle_table = products_mod.astype(np.float32) * np.float32(2.0 * math.pi / antennas)
    cosine_table = np.cos(angle_table) / np.float32(math.sqrt(antennas))
    sine_table = np.sin(angle_table) / np.float32(math.sqrt(antennas))
    forward_transform = np.concatenate(
        [
            np.concatenate([cosine_table, -sine_table], 1),
            np.concatenate([sine_table, cosine_table], 1),
        ],
        0,
    )
    inverse_transform = np.concatenate(
        [
            np.concatenate([cosine_table, sine_table], 1),
            np.concatenate([-sine_table, cosine_table], 1),
        ],
        0,
    )
    return (
        jnp.asarray(forward_transform.astype(ml_dtypes.bfloat16)),
        jnp.asarray(inverse_transform.astype(ml_dtypes.bfloat16)),
    )


def decode_rows(
    mixed_in,
    wanted_lines,
    output_weight,
    spectral_filter_weight,
    forward_transform,
    inverse_transform,
    loss_scale,
):
    filter_re = spectral_filter_weight[0]
    filter_im = spectral_filter_weight[1]
    spectrum = jnp.dot(mixed_in, forward_transform, preferred_element_type=jnp.float32)
    half_width = spectrum.shape[1] // 2
    spec_re = spectrum[:, :half_width]
    spec_im = spectrum[:, half_width:]
    filtered = jnp.concatenate(
        [spec_re * filter_re - spec_im * filter_im, spec_re * filter_im + spec_im * filter_re], 1
    ).astype(jnp.bfloat16)
    mixed_back = lax.dot_general(
        filtered, forward_transform, (((1,), (1,)), ((), ())), preferred_element_type=jnp.float32
    )
    hidden = (mixed_in.astype(jnp.float32) + jax.nn.gelu(mixed_back)).astype(jnp.bfloat16)
    rebuilt = hidden.astype(jnp.float32) + jnp.dot(
        hidden, output_weight, preferred_element_type=jnp.float32
    )
    residual = loss_scale * (rebuilt - wanted_lines.astype(jnp.float32))
    residual_half = residual.astype(jnp.bfloat16)
    grad_out = lax.dot_general(
        hidden, residual_half, (((0,), (0,)), ((), ())), preferred_element_type=jnp.float32
    )
    grad_hidden = residual + lax.dot_general(
        residual_half, output_weight, (((1,), (1,)), ((), ())), preferred_element_type=jnp.float32
    )
    grad_mixed = jax.vjp(jax.nn.gelu, mixed_back)[1](grad_hidden)[0].astype(jnp.bfloat16)
    grad_filtered = jnp.dot(grad_mixed, forward_transform, preferred_element_type=jnp.float32)
    grad_re = grad_filtered[:, :half_width]
    grad_im = grad_filtered[:, half_width:]
    grad_filter = jnp.stack(
        [
            jnp.sum(grad_re * spec_re + grad_im * spec_im, 0),
            jnp.sum(grad_im * spec_re - grad_re * spec_im, 0),
        ]
    )
    grad_spec = jnp.concatenate(
        [grad_re * filter_re + grad_im * filter_im, grad_im * filter_re - grad_re * filter_im], 1
    ).astype(jnp.bfloat16)
    derivative_entering = grad_hidden + lax.dot_general(
        grad_spec, forward_transform, (((1,), (1,)), ((), ())), preferred_element_type=jnp.float32
    )
    return (derivative_entering, grad_out, grad_filter)


def encoder_grads(inputs_rows, codewords, latent_sums, decoder_weight):
    latent_half = latent_sums.astype(jnp.bfloat16)
    grad_dec = lax.dot_general(
        codewords, latent_half, (((0,), (0,)), ((), ())), preferred_element_type=jnp.float32
    )
    grad_codes = lax.dot_general(
        latent_half, decoder_weight, (((1,), (1,)), ((), ())), preferred_element_type=jnp.float32
    )
    grad_pre = (grad_codes * (1.0 - jnp.square(codewords.astype(jnp.float32)))).astype(jnp.bfloat16)
    grad_enc = lax.dot_general(
        inputs_rows, grad_pre, (((0,), (0,)), ((), ())), preferred_element_type=jnp.float32
    )
    return (grad_enc, grad_dec)


def _exchange_pairs(count, distance):
    return [(i, i ^ distance) for i in range(count)]


def _is_power_of_two(count):
    return count > 0 and count & (count - 1) == 0


def gather_rows(block, axis_name):
    count = lax.axis_size(axis_name)
    if not _is_power_of_two(count):
        return lax.all_gather(block, axis_name, axis=0, tiled=True)
    position = lax.axis_index(axis_name)
    distance = count // 2
    while distance >= 1:
        other = lax.ppermute(block, axis_name, _exchange_pairs(count, distance))
        lower = (position // distance) % 2 == 0
        block = jnp.where(
            lower, jnp.concatenate([block, other], 0), jnp.concatenate([other, block], 0)
        )
        distance //= 2
    return block


def bit_reversed_blocks(values, count):
    if not _is_power_of_two(count):
        return values
    bits = count.bit_length() - 1
    blocks = values.reshape((2,) * bits + (-1,))
    return blocks.transpose(tuple(reversed(range(bits))) + (bits,)).reshape(-1)


def sum_whole(values, axis_name):
    count = lax.axis_size(axis_name)
    if not _is_power_of_two(count):
        return lax.psum(values, axis_name)
    distance = 1
    while distance < count:
        values = values + lax.ppermute(values, axis_name, _exchange_pairs(count, distance))
        distance *= 2
    return values


def sum_halving(values, axis_name, wire=jnp.bfloat16, halving_levels=2):
    count = lax.axis_size(axis_name)
    if not _is_power_of_two(count) or values.shape[0] % count != 0:
        return lax.psum(values, axis_name)
    position = lax.axis_index(axis_name)
    distance = 1
    while distance < count and distance < 2**halving_levels:
        half = values.shape[0] // 2
        lower = (position // distance) % 2 == 0
        keep = jnp.where(lower, values[:half], values[half:])
        send = jnp.where(lower, values[half:], values[:half]).astype(wire)
        arrived = lax.ppermute(send, axis_name, _exchange_pairs(count, distance))
        values = keep + arrived.astype(keep.dtype)
        distance *= 2
    top = distance
    values = values.astype(wire)
    while distance < count:
        arrived = lax.ppermute(values, axis_name, _exchange_pairs(count, distance))
        values = (values.astype(jnp.float32) + arrived.astype(jnp.float32)).astype(wire)
        distance *= 2
    distance = top // 2
    while distance >= 1:
        other = lax.ppermute(values, axis_name, _exchange_pairs(count, distance))
        lower = (position // distance) % 2 == 0
        values = jnp.where(
            lower, jnp.concatenate([values, other], 0), jnp.concatenate([other, values], 0)
        )
        distance //= 2
    return values


def local(
    encoder_input,
    desired_responses,
    sample_index,
    encoder_weight,
    decoder_weight,
    frequency_amplitude,
    spectral_filter_weight,
    output_weight,
):
    samples = sample_index.shape[0]
    sub_dev = desired_responses.shape[1]
    width = desired_responses.shape[2]
    forward_transform, inverse_transform = rotation_tables(width // 2)
    loss_scale = 1.0 / math.sqrt(samples * sub_dev * lax.axis_size("freq"))
    all_inputs = gather_rows(encoder_input, "freq")
    gathered_index = bit_reversed_blocks(sample_index, lax.axis_size("freq"))
    selection = (
        gathered_index[None, :] == jnp.arange(samples, dtype=jnp.int32)[:, None]
    ).astype(jnp.bfloat16)
    inputs_by_sample = jnp.dot(selection, all_inputs, preferred_element_type=jnp.float32).astype(
        jnp.bfloat16
    )
    codes_by_sample = jnp.tanh(
        jnp.dot(inputs_by_sample, encoder_weight, preferred_element_type=jnp.float32)
    ).astype(jnp.bfloat16)
    latent = jnp.dot(codes_by_sample, decoder_weight, preferred_element_type=jnp.float32)
    gain_row_values = frequency_amplitude.astype(jnp.float32)
    mixed_in = (latent[:, None, :] * gain_row_values[None]).astype(jnp.bfloat16).reshape(-1, width)
    wanted_lines = desired_responses.reshape(-1, width)
    derivative_entering, grad_out, grad_filter = decode_rows(
        mixed_in,
        wanted_lines,
        output_weight,
        spectral_filter_weight,
        forward_transform,
        inverse_transform,
        loss_scale,
    )
    derivative_bottleneck = jnp.einsum(
        "orm,rm->om", derivative_entering.reshape(samples, sub_dev, width), gain_row_values
    )
    count = lax.axis_size("freq")
    half_width = grad_filter.shape[1]
    filter_rows = jnp.concatenate(
        [grad_filter, jnp.zeros((grad_filter.shape[0], width - half_width), jnp.float32)], 1
    )
    packed_rows = grad_out.shape[0] + samples + filter_rows.shape[0]
    padding = -packed_rows % count
    packed = jnp.concatenate(
        [
            grad_out,
            derivative_bottleneck,
            filter_rows,
            jnp.zeros((padding, width), jnp.float32),
        ],
        0,
    )
    packed = sum_halving(packed, "freq")
    rows_out = grad_out.shape[0]
    grad_out = packed[:rows_out].astype(jnp.float32)
    derivative_bottleneck = packed[rows_out : rows_out + samples].astype(jnp.float32)
    grad_filter = packed[
        rows_out + samples : rows_out + samples + filter_rows.shape[0], :half_width
    ].astype(jnp.float32)
    grad_enc, grad_dec = encoder_grads(
        inputs_by_sample, codes_by_sample, derivative_bottleneck, decoder_weight
    )
    return (grad_enc, grad_dec, grad_out, grad_filter)


def solution(mesh):
    return jax.shard_map(
        local,
        mesh=mesh,
        in_specs=(
            P(("groups", "freq"), None),
            P("groups", "freq", None),
            P("groups"),
            P(),
            P(),
            P("freq", None),
            P(),
            P(),
        ),
        out_specs=(P("groups", None), P("groups", None), P("groups", None), P("groups", None)),
        check_vma=False,
    )
```

```python
import math

import jax
import ml_dtypes
import numpy as np
import jax.numpy as jnp
from jax import lax
from jax.sharding import PartitionSpec as P


def rotation_tables(antennas):
    indices = np.arange(antennas, dtype=np.int32)
    products_mod = indices[:, None] * indices[None, :] % antennas
    angle_table = products_mod.astype(np.float32) * np.float32(2.0 * math.pi / antennas)
    cosine_table = np.cos(angle_table) / np.float32(math.sqrt(antennas))
    sine_table = np.sin(angle_table) / np.float32(math.sqrt(antennas))
    forward_transform = np.concatenate(
        [
            np.concatenate([cosine_table, -sine_table], 1),
            np.concatenate([sine_table, cosine_table], 1),
        ],
        0,
    )
    inverse_transform = np.concatenate(
        [
            np.concatenate([cosine_table, sine_table], 1),
            np.concatenate([-sine_table, cosine_table], 1),
        ],
        0,
    )
    return (
        jnp.asarray(forward_transform.astype(ml_dtypes.bfloat16)),
        jnp.asarray(inverse_transform.astype(ml_dtypes.bfloat16)),
    )


def decode_rows(
    mixed_in,
    wanted_lines,
    output_weight,
    spectral_filter_weight,
    forward_transform,
    inverse_transform,
    loss_scale,
):
    filter_re = spectral_filter_weight[0]
    filter_im = spectral_filter_weight[1]
    spectrum = jnp.dot(mixed_in, forward_transform, preferred_element_type=jnp.float32)
    half_width = spectrum.shape[1] // 2
    spec_re = spectrum[:, :half_width]
    spec_im = spectrum[:, half_width:]
    filtered = jnp.concatenate(
        [spec_re * filter_re - spec_im * filter_im, spec_re * filter_im + spec_im * filter_re], 1
    ).astype(jnp.bfloat16)
    mixed_back = lax.dot_general(
        filtered, forward_transform, (((1,), (1,)), ((), ())), preferred_element_type=jnp.float32
    )
    hidden = (mixed_in.astype(jnp.float32) + jax.nn.gelu(mixed_back)).astype(jnp.bfloat16)
    rebuilt = hidden.astype(jnp.float32) + jnp.dot(
        hidden, output_weight, preferred_element_type=jnp.float32
    )
    residual = loss_scale * (rebuilt - wanted_lines.astype(jnp.float32))
    residual_half = residual.astype(jnp.bfloat16)
    grad_out = lax.dot_general(
        hidden, residual_half, (((0,), (0,)), ((), ())), preferred_element_type=jnp.float32
    )
    grad_hidden = residual + lax.dot_general(
        residual_half, output_weight, (((1,), (1,)), ((), ())), preferred_element_type=jnp.float32
    )
    grad_mixed = jax.vjp(jax.nn.gelu, mixed_back)[1](grad_hidden)[0].astype(jnp.bfloat16)
    grad_filtered = jnp.dot(grad_mixed, forward_transform, preferred_element_type=jnp.float32)
    grad_re = grad_filtered[:, :half_width]
    grad_im = grad_filtered[:, half_width:]
    grad_filter = jnp.stack(
        [
            jnp.sum(grad_re * spec_re + grad_im * spec_im, 0),
            jnp.sum(grad_im * spec_re - grad_re * spec_im, 0),
        ]
    )
    grad_spec = jnp.concatenate(
        [grad_re * filter_re + grad_im * filter_im, grad_im * filter_re - grad_re * filter_im], 1
    ).astype(jnp.bfloat16)
    derivative_entering = grad_hidden + lax.dot_general(
        grad_spec, forward_transform, (((1,), (1,)), ((), ())), preferred_element_type=jnp.float32
    )
    return (derivative_entering, grad_out, grad_filter)


def encoder_grads(inputs_rows, codewords, latent_sums, decoder_weight):
    latent_half = latent_sums.astype(jnp.bfloat16)
    grad_dec = lax.dot_general(
        codewords, latent_half, (((0,), (0,)), ((), ())), preferred_element_type=jnp.float32
    )
    grad_codes = lax.dot_general(
        latent_half, decoder_weight, (((1,), (1,)), ((), ())), preferred_element_type=jnp.float32
    )
    grad_pre = (grad_codes * (1.0 - jnp.square(codewords.astype(jnp.float32)))).astype(jnp.bfloat16)
    grad_enc = lax.dot_general(
        inputs_rows, grad_pre, (((0,), (0,)), ((), ())), preferred_element_type=jnp.float32
    )
    return (grad_enc, grad_dec)


def _exchange_pairs(count, distance):
    return [(i, i ^ distance) for i in range(count)]


def _is_power_of_two(count):
    return count > 0 and count & (count - 1) == 0


def gather_rows(block, axis_name):
    count = lax.axis_size(axis_name)
    if not _is_power_of_two(count):
        return lax.all_gather(block, axis_name, axis=0, tiled=True)
    position = lax.axis_index(axis_name)
    distance = count // 2
    while distance >= 1:
        other = lax.ppermute(block, axis_name, _exchange_pairs(count, distance))
        lower = (position // distance) % 2 == 0
        block = jnp.where(
            lower, jnp.concatenate([block, other], 0), jnp.concatenate([other, block], 0)
        )
        distance //= 2
    return block


def bit_reversed_blocks(values, count):
    if not _is_power_of_two(count):
        return values
    bits = count.bit_length() - 1
    blocks = values.reshape((2,) * bits + (-1,))
    return blocks.transpose(tuple(reversed(range(bits))) + (bits,)).reshape(-1)


def sum_whole(values, axis_name):
    count = lax.axis_size(axis_name)
    if not _is_power_of_two(count):
        return lax.psum(values, axis_name)
    distance = 1
    while distance < count:
        values = values + lax.ppermute(values, axis_name, _exchange_pairs(count, distance))
        distance *= 2
    return values


def sum_halving(values, axis_name, split, wire=jnp.bfloat16, halving_levels=2):
    count = lax.axis_size(axis_name)
    if not _is_power_of_two(count) or values.shape[0] % count != 0:
        values = lax.psum(values, axis_name)
        return values[:split], values[split:]
    position = lax.axis_index(axis_name)
    distance = 1
    while distance < count and distance < 2**halving_levels:
        half = values.shape[0] // 2
        lower = (position // distance) % 2 == 0
        keep = jnp.where(lower, values[:half], values[half:])
        send = jnp.where(lower, values[half:], values[:half]).astype(wire)
        arrived = lax.ppermute(send, axis_name, _exchange_pairs(count, distance))
        values = keep + arrived.astype(keep.dtype)
        distance *= 2
    top = distance
    values = values.astype(wire)
    while distance < count:
        arrived = lax.ppermute(values, axis_name, _exchange_pairs(count, distance))
        values = (values.astype(jnp.float32) + arrived.astype(jnp.float32)).astype(wire)
        distance *= 2
    distance = top // 2
    while distance >= 1:
        other = lax.ppermute(values, axis_name, _exchange_pairs(count, distance))
        lower = (position // distance) % 2 == 0
        if distance == 1 and values.shape[0] <= split < 2 * values.shape[0]:
            cut = split - values.shape[0]
            head = jnp.where(
                lower,
                jnp.concatenate([values, other[:cut]], 0),
                jnp.concatenate([other, values[:cut]], 0),
            )
            return head, jnp.where(lower, other[cut:], values[cut:])
        values = jnp.where(
            lower, jnp.concatenate([values, other], 0), jnp.concatenate([other, values], 0)
        )
        distance //= 2
    return values[:split], values[split:]


def local(
    encoder_input,
    desired_responses,
    sample_index,
    encoder_weight,
    decoder_weight,
    frequency_amplitude,
    spectral_filter_weight,
    output_weight,
):
    samples = sample_index.shape[0]
    sub_dev = desired_responses.shape[1]
    width = desired_responses.shape[2]
    forward_transform, inverse_transform = rotation_tables(width // 2)
    loss_scale = 1.0 / math.sqrt(samples * sub_dev * lax.axis_size("freq"))
    all_inputs = gather_rows(encoder_input, "freq")
    gathered_index = bit_reversed_blocks(sample_index, lax.axis_size("freq"))
    selection = (
        gathered_index[None, :] == jnp.arange(samples, dtype=jnp.int32)[:, None]
    ).astype(jnp.bfloat16)
    inputs_by_sample = jnp.dot(selection, all_inputs, preferred_element_type=jnp.float32).astype(
        jnp.bfloat16
    )
    codes_by_sample = jnp.tanh(
        jnp.dot(inputs_by_sample, encoder_weight, preferred_element_type=jnp.float32)
    ).astype(jnp.bfloat16)
    latent = jnp.dot(codes_by_sample, decoder_weight, preferred_element_type=jnp.float32)
    gain_row_values = frequency_amplitude.astype(jnp.float32)
    mixed_in = (latent[:, None, :] * gain_row_values[None]).astype(jnp.bfloat16).reshape(-1, width)
    wanted_lines = desired_responses.reshape(-1, width)
    derivative_entering, grad_out, grad_filter = decode_rows(
        mixed_in,
        wanted_lines,
        output_weight,
        spectral_filter_weight,
        forward_transform,
        inverse_transform,
        loss_scale,
    )
    derivative_bottleneck = jnp.einsum(
        "orm,rm->om", derivative_entering.reshape(samples, sub_dev, width), gain_row_values
    )
    count = lax.axis_size("freq")
    half_width = grad_filter.shape[1]
    filter_rows = jnp.concatenate(
        [grad_filter, jnp.zeros((grad_filter.shape[0], width - half_width), jnp.float32)], 1
    )
    packed_rows = grad_out.shape[0] + samples + filter_rows.shape[0]
    padding = -packed_rows % count
    packed = jnp.concatenate(
        [
            grad_out,
            derivative_bottleneck,
            filter_rows,
            jnp.zeros((padding, width), jnp.float32),
        ],
        0,
    )
    rows_out = grad_out.shape[0]
    head, rest = sum_halving(packed, "freq", rows_out)
    grad_out = head.astype(jnp.float32)
    derivative_bottleneck = rest[:samples].astype(jnp.float32)
    grad_filter = rest[samples : samples + filter_rows.shape[0], :half_width].astype(jnp.float32)
    grad_enc, grad_dec = encoder_grads(
        inputs_by_sample, codes_by_sample, derivative_bottleneck, decoder_weight
    )
    return (grad_enc, grad_dec, grad_out, grad_filter)


def solution(mesh):
    return jax.shard_map(
        local,
        mesh=mesh,
        in_specs=(
            P(("groups", "freq"), None),
            P("groups", "freq", None),
            P("groups"),
            P(),
            P(),
            P("freq", None),
            P(),
            P(),
        ),
        out_specs=(P("groups", None), P("groups", None), P("groups", None), P("groups", None)),
        check_vma=False,
    )
```

```python
import math

import jax
import ml_dtypes
import numpy as np
import jax.numpy as jnp
from jax import lax
from jax.sharding import PartitionSpec as P


def rotation_tables(antennas):
    indices = np.arange(antennas, dtype=np.int32)
    products_mod = indices[:, None] * indices[None, :] % antennas
    angle_table = products_mod.astype(np.float32) * np.float32(2.0 * math.pi / antennas)
    cosine_table = np.cos(angle_table) / np.float32(math.sqrt(antennas))
    sine_table = np.sin(angle_table) / np.float32(math.sqrt(antennas))
    forward_transform = np.concatenate(
        [
            np.concatenate([cosine_table, -sine_table], 1),
            np.concatenate([sine_table, cosine_table], 1),
        ],
        0,
    )
    inverse_transform = np.concatenate(
        [
            np.concatenate([cosine_table, sine_table], 1),
            np.concatenate([-sine_table, cosine_table], 1),
        ],
        0,
    )
    return (
        jnp.asarray(forward_transform.astype(ml_dtypes.bfloat16)),
        jnp.asarray(inverse_transform.astype(ml_dtypes.bfloat16)),
    )


def decode_rows(
    mixed_in,
    wanted_lines,
    output_weight,
    spectral_filter_weight,
    forward_transform,
    inverse_transform,
    loss_scale,
):
    filter_re = spectral_filter_weight[0]
    filter_im = spectral_filter_weight[1]
    spectrum = jnp.dot(mixed_in, forward_transform, preferred_element_type=jnp.float32)
    half_width = spectrum.shape[1] // 2
    spec_re = spectrum[:, :half_width]
    spec_im = spectrum[:, half_width:]
    filtered = jnp.concatenate(
        [spec_re * filter_re - spec_im * filter_im, spec_re * filter_im + spec_im * filter_re], 1
    ).astype(jnp.bfloat16)
    mixed_back = lax.dot_general(
        filtered, forward_transform, (((1,), (1,)), ((), ())), preferred_element_type=jnp.float32
    )
    hidden = (mixed_in.astype(jnp.float32) + jax.nn.gelu(mixed_back)).astype(jnp.bfloat16)
    rebuilt = hidden.astype(jnp.float32) + jnp.dot(
        hidden, output_weight, preferred_element_type=jnp.float32
    )
    residual = loss_scale * (rebuilt - wanted_lines.astype(jnp.float32))
    residual_half = residual.astype(jnp.bfloat16)
    grad_out = lax.dot_general(
        hidden, residual_half, (((0,), (0,)), ((), ())), preferred_element_type=jnp.float32
    )
    grad_hidden = residual + lax.dot_general(
        residual_half, output_weight, (((1,), (1,)), ((), ())), preferred_element_type=jnp.float32
    )
    grad_mixed = jax.vjp(jax.nn.gelu, mixed_back)[1](grad_hidden)[0].astype(jnp.bfloat16)
    grad_filtered = jnp.dot(grad_mixed, forward_transform, preferred_element_type=jnp.float32)
    grad_re = grad_filtered[:, :half_width]
    grad_im = grad_filtered[:, half_width:]
    grad_filter = jnp.stack(
        [
            jnp.sum(grad_re * spec_re + grad_im * spec_im, 0),
            jnp.sum(grad_im * spec_re - grad_re * spec_im, 0),
        ]
    )
    grad_spec = jnp.concatenate(
        [grad_re * filter_re + grad_im * filter_im, grad_im * filter_re - grad_re * filter_im], 1
    ).astype(jnp.bfloat16)
    derivative_entering = grad_hidden + lax.dot_general(
        grad_spec, forward_transform, (((1,), (1,)), ((), ())), preferred_element_type=jnp.float32
    )
    return (derivative_entering, grad_out, grad_filter)


def encoder_grads(inputs_rows, codewords, latent_sums, decoder_weight):
    latent_half = latent_sums.astype(jnp.bfloat16)
    grad_dec = lax.dot_general(
        codewords, latent_half, (((0,), (0,)), ((), ())), preferred_element_type=jnp.float32
    )
    grad_codes = lax.dot_general(
        latent_half, decoder_weight, (((1,), (1,)), ((), ())), preferred_element_type=jnp.float32
    )
    grad_pre = (grad_codes * (1.0 - jnp.square(codewords.astype(jnp.float32)))).astype(jnp.bfloat16)
    grad_enc = lax.dot_general(
        inputs_rows, grad_pre, (((0,), (0,)), ((), ())), preferred_element_type=jnp.float32
    )
    return (grad_enc, grad_dec)


def _exchange_pairs(count, distance):
    return [(i, i ^ distance) for i in range(count)]


def _is_power_of_two(count):
    return count > 0 and count & (count - 1) == 0


def gather_rows(block, axis_name):
    count = lax.axis_size(axis_name)
    if not _is_power_of_two(count):
        return lax.all_gather(block, axis_name, axis=0, tiled=True)
    position = lax.axis_index(axis_name)
    distance = count // 2
    while distance >= 1:
        other = lax.ppermute(block, axis_name, _exchange_pairs(count, distance))
        lower = (position // distance) % 2 == 0
        block = jnp.where(
            lower, jnp.concatenate([block, other], 0), jnp.concatenate([other, block], 0)
        )
        distance //= 2
    return block


def bit_reversed_blocks(values, count):
    if not _is_power_of_two(count):
        return values
    bits = count.bit_length() - 1
    blocks = values.reshape((2,) * bits + (-1,))
    return blocks.transpose(tuple(reversed(range(bits))) + (bits,)).reshape(-1)


def sum_whole(values, axis_name):
    count = lax.axis_size(axis_name)
    if not _is_power_of_two(count):
        return lax.psum(values, axis_name)
    distance = 1
    while distance < count:
        values = values + lax.ppermute(values, axis_name, _exchange_pairs(count, distance))
        distance *= 2
    return values


def sum_halving(values, axis_name, wire=jnp.bfloat16, halving_levels=3):
    count = lax.axis_size(axis_name)
    if not _is_power_of_two(count) or values.shape[0] % count != 0:
        return lax.psum(values, axis_name)
    position = lax.axis_index(axis_name)
    distance = 1
    while distance < count and distance < 2**halving_levels:
        half = values.shape[0] // 2
        lower = (position // distance) % 2 == 0
        keep = jnp.where(lower, values[:half], values[half:])
        send = jnp.where(lower, values[half:], values[:half]).astype(wire)
        arrived = lax.ppermute(send, axis_name, _exchange_pairs(count, distance))
        values = keep + arrived.astype(keep.dtype)
        distance *= 2
    top = distance
    values = values.astype(wire)
    while distance < count:
        arrived = lax.ppermute(values, axis_name, _exchange_pairs(count, distance))
        values = (values.astype(jnp.float32) + arrived.astype(jnp.float32)).astype(wire)
        distance *= 2
    distance = top // 2
    while distance >= 1:
        other = lax.ppermute(values, axis_name, _exchange_pairs(count, distance))
        lower = (position // distance) % 2 == 0
        values = jnp.where(
            lower, jnp.concatenate([values, other], 0), jnp.concatenate([other, values], 0)
        )
        distance //= 2
    return values


def local(
    encoder_input,
    desired_responses,
    sample_index,
    encoder_weight,
    decoder_weight,
    frequency_amplitude,
    spectral_filter_weight,
    output_weight,
):
    samples = sample_index.shape[0]
    sub_dev = desired_responses.shape[1]
    width = desired_responses.shape[2]
    forward_transform, inverse_transform = rotation_tables(width // 2)
    loss_scale = 1.0 / math.sqrt(samples * sub_dev * lax.axis_size("freq"))
    all_inputs = gather_rows(encoder_input, "freq")
    gathered_index = bit_reversed_blocks(sample_index, lax.axis_size("freq"))
    selection = (
        gathered_index[None, :] == jnp.arange(samples, dtype=jnp.int32)[:, None]
    ).astype(jnp.bfloat16)
    inputs_by_sample = jnp.dot(selection, all_inputs, preferred_element_type=jnp.float32).astype(
        jnp.bfloat16
    )
    codes_by_sample = jnp.tanh(
        jnp.dot(inputs_by_sample, encoder_weight, preferred_element_type=jnp.float32)
    ).astype(jnp.bfloat16)
    latent = jnp.dot(codes_by_sample, decoder_weight, preferred_element_type=jnp.float32)
    gain_row_values = frequency_amplitude.astype(jnp.float32)
    mixed_in = (latent[:, None, :] * gain_row_values[None]).astype(jnp.bfloat16).reshape(-1, width)
    wanted_lines = desired_responses.reshape(-1, width)
    derivative_entering, grad_out, grad_filter = decode_rows(
        mixed_in,
        wanted_lines,
        output_weight,
        spectral_filter_weight,
        forward_transform,
        inverse_transform,
        loss_scale,
    )
    derivative_bottleneck = jnp.einsum(
        "orm,rm->om", derivative_entering.reshape(samples, sub_dev, width), gain_row_values
    )
    count = lax.axis_size("freq")
    half_width = grad_filter.shape[1]
    filter_rows = jnp.concatenate(
        [grad_filter, jnp.zeros((grad_filter.shape[0], width - half_width), jnp.float32)], 1
    )
    packed_rows = grad_out.shape[0] + samples + filter_rows.shape[0]
    padding = -packed_rows % count
    packed = jnp.concatenate(
        [
            grad_out,
            derivative_bottleneck,
            filter_rows,
            jnp.zeros((padding, width), jnp.float32),
        ],
        0,
    )
    packed = sum_halving(packed, "freq")
    rows_out = grad_out.shape[0]
    grad_out = packed[:rows_out].astype(jnp.float32)
    derivative_bottleneck = packed[rows_out : rows_out + samples].astype(jnp.float32)
    grad_filter = packed[
        rows_out + samples : rows_out + samples + filter_rows.shape[0], :half_width
    ].astype(jnp.float32)
    grad_enc, grad_dec = encoder_grads(
        inputs_by_sample, codes_by_sample, derivative_bottleneck, decoder_weight
    )
    return (grad_enc, grad_dec, grad_out, grad_filter)


def solution(mesh):
    return jax.shard_map(
        local,
        mesh=mesh,
        in_specs=(
            P(("groups", "freq"), None),
            P("groups", "freq", None),
            P("groups"),
            P(),
            P(),
            P("freq", None),
            P(),
            P(),
        ),
        out_specs=(P("groups", None), P("groups", None), P("groups", None), P("groups", None)),
        check_vma=False,
    )
```

```python
import math

import jax
import ml_dtypes
import numpy as np
import jax.numpy as jnp
from jax import lax
from jax.sharding import PartitionSpec as P


def rotation_tables(antennas):
    indices = np.arange(antennas, dtype=np.int32)
    products_mod = indices[:, None] * indices[None, :] % antennas
    angle_table = products_mod.astype(np.float32) * np.float32(2.0 * math.pi / antennas)
    cosine_table = np.cos(angle_table) / np.float32(math.sqrt(antennas))
    sine_table = np.sin(angle_table) / np.float32(math.sqrt(antennas))
    forward_transform = np.concatenate(
        [
            np.concatenate([cosine_table, -sine_table], 1),
            np.concatenate([sine_table, cosine_table], 1),
        ],
        0,
    )
    inverse_transform = np.concatenate(
        [
            np.concatenate([cosine_table, sine_table], 1),
            np.concatenate([-sine_table, cosine_table], 1),
        ],
        0,
    )
    return (
        jnp.asarray(forward_transform.astype(ml_dtypes.bfloat16)),
        jnp.asarray(inverse_transform.astype(ml_dtypes.bfloat16)),
    )


def decode_rows(
    mixed_in,
    wanted_lines,
    output_weight,
    spectral_filter_weight,
    forward_transform,
    inverse_transform,
    loss_scale,
):
    filter_re = spectral_filter_weight[0]
    filter_im = spectral_filter_weight[1]
    spectrum = jnp.dot(mixed_in, forward_transform, preferred_element_type=jnp.float32)
    half_width = spectrum.shape[1] // 2
    spec_re = spectrum[:, :half_width]
    spec_im = spectrum[:, half_width:]
    filtered = jnp.concatenate(
        [spec_re * filter_re - spec_im * filter_im, spec_re * filter_im + spec_im * filter_re], 1
    ).astype(jnp.bfloat16)
    mixed_back = lax.dot_general(
        filtered, forward_transform, (((1,), (1,)), ((), ())), preferred_element_type=jnp.float32
    )
    hidden = (mixed_in.astype(jnp.float32) + jax.nn.gelu(mixed_back)).astype(jnp.bfloat16)
    rebuilt = hidden.astype(jnp.float32) + jnp.dot(
        hidden, output_weight, preferred_element_type=jnp.float32
    )
    residual = loss_scale * (rebuilt - wanted_lines.astype(jnp.float32))
    residual_half = residual.astype(jnp.bfloat16)
    grad_out = lax.dot_general(
        hidden, residual_half, (((0,), (0,)), ((), ())), preferred_element_type=jnp.float32
    )
    grad_hidden = residual + lax.dot_general(
        residual_half, output_weight, (((1,), (1,)), ((), ())), preferred_element_type=jnp.float32
    )
    grad_mixed = jax.vjp(jax.nn.gelu, mixed_back)[1](grad_hidden)[0].astype(jnp.bfloat16)
    grad_filtered = jnp.dot(grad_mixed, forward_transform, preferred_element_type=jnp.float32)
    grad_re = grad_filtered[:, :half_width]
    grad_im = grad_filtered[:, half_width:]
    grad_filter = jnp.stack(
        [
            jnp.sum(grad_re * spec_re + grad_im * spec_im, 0),
            jnp.sum(grad_im * spec_re - grad_re * spec_im, 0),
        ]
    )
    grad_spec = jnp.concatenate(
        [grad_re * filter_re + grad_im * filter_im, grad_im * filter_re - grad_re * filter_im], 1
    ).astype(jnp.bfloat16)
    derivative_entering = grad_hidden + lax.dot_general(
        grad_spec, forward_transform, (((1,), (1,)), ((), ())), preferred_element_type=jnp.float32
    )
    return (derivative_entering, grad_out, grad_filter)


def encoder_grads(inputs_rows, codewords, latent_sums, decoder_weight):
    latent_half = latent_sums.astype(jnp.bfloat16)
    grad_dec = lax.dot_general(
        codewords, latent_half, (((0,), (0,)), ((), ())), preferred_element_type=jnp.float32
    )
    grad_codes = lax.dot_general(
        latent_half, decoder_weight, (((1,), (1,)), ((), ())), preferred_element_type=jnp.float32
    )
    grad_pre = (grad_codes * (1.0 - jnp.square(codewords.astype(jnp.float32)))).astype(jnp.bfloat16)
    grad_enc = lax.dot_general(
        inputs_rows, grad_pre, (((0,), (0,)), ((), ())), preferred_element_type=jnp.float32
    )
    return (grad_enc, grad_dec)


def _exchange_pairs(count, distance):
    return [(i, i ^ distance) for i in range(count)]


def _is_power_of_two(count):
    return count > 0 and count & (count - 1) == 0


def gather_rows(block, axis_name):
    count = lax.axis_size(axis_name)
    if not _is_power_of_two(count):
        return lax.all_gather(block, axis_name, axis=0, tiled=True)
    position = lax.axis_index(axis_name)
    distance = count // 2
    while distance >= 1:
        other = lax.ppermute(block, axis_name, _exchange_pairs(count, distance))
        lower = (position // distance) % 2 == 0
        block = jnp.where(
            lower, jnp.concatenate([block, other], 0), jnp.concatenate([other, block], 0)
        )
        distance //= 2
    return block


def bit_reversed_blocks(values, count):
    if not _is_power_of_two(count):
        return values
    bits = count.bit_length() - 1
    blocks = values.reshape((2,) * bits + (-1,))
    return blocks.transpose(tuple(reversed(range(bits))) + (bits,)).reshape(-1)


def sum_whole(values, axis_name):
    count = lax.axis_size(axis_name)
    if not _is_power_of_two(count):
        return lax.psum(values, axis_name)
    distance = 1
    while distance < count:
        values = values + lax.ppermute(values, axis_name, _exchange_pairs(count, distance))
        distance *= 2
    return values


def sum_halving(values, axis_name, wire=jnp.bfloat16, halving_levels=2):
    count = lax.axis_size(axis_name)
    if not _is_power_of_two(count) or values.shape[0] % count != 0:
        return lax.psum(values, axis_name)
    position = lax.axis_index(axis_name)
    distance = 1
    while distance < count and distance < 2**halving_levels:
        half = values.shape[0] // 2
        lower = (position // distance) % 2 == 0
        keep = jnp.where(lower, values[:half], values[half:])
        send = jnp.where(lower, values[half:], values[:half]).astype(wire)
        arrived = lax.ppermute(send, axis_name, _exchange_pairs(count, distance))
        values = keep + arrived.astype(keep.dtype)
        distance *= 2
    top = distance
    values = values.astype(wire)
    while distance < count:
        arrived = lax.ppermute(values, axis_name, _exchange_pairs(count, distance))
        values = (values.astype(jnp.float32) + arrived.astype(jnp.float32)).astype(wire)
        distance *= 2
    distance = top // 2
    while distance >= 1:
        other = lax.ppermute(values, axis_name, _exchange_pairs(count, distance))
        lower = (position // distance) % 2 == 0
        values = jnp.where(
            lower, jnp.concatenate([values, other], 0), jnp.concatenate([other, values], 0)
        )
        distance //= 2
    return values


def local(
    encoder_input,
    desired_responses,
    sample_index,
    encoder_weight,
    decoder_weight,
    frequency_amplitude,
    spectral_filter_weight,
    output_weight,
):
    samples = sample_index.shape[0]
    sub_dev = desired_responses.shape[1]
    width = desired_responses.shape[2]
    forward_transform, inverse_transform = rotation_tables(width // 2)
    loss_scale = 1.0 / math.sqrt(samples * sub_dev * lax.axis_size("freq"))
    codes_own = jnp.tanh(
        jnp.dot(encoder_input, encoder_weight, preferred_element_type=jnp.float32)
    ).astype(jnp.bfloat16)
    enc_in = encoder_input.shape[1]
    gathered = gather_rows(jnp.concatenate([encoder_input, codes_own], 1), "freq")
    gathered_index = bit_reversed_blocks(sample_index, lax.axis_size("freq"))
    selection = (
        gathered_index[None, :] == jnp.arange(samples, dtype=jnp.int32)[:, None]
    ).astype(jnp.bfloat16)
    codes_by_sample = jnp.dot(
        selection, gathered[:, enc_in:], preferred_element_type=jnp.float32
    ).astype(jnp.bfloat16)
    inputs_by_sample = jnp.dot(
        selection, gathered[:, :enc_in], preferred_element_type=jnp.float32
    ).astype(jnp.bfloat16)
    latent = jnp.dot(codes_by_sample, decoder_weight, preferred_element_type=jnp.float32)
    gain_row_values = frequency_amplitude.astype(jnp.float32)
    mixed_in = (latent[:, None, :] * gain_row_values[None]).astype(jnp.bfloat16).reshape(-1, width)
    wanted_lines = desired_responses.reshape(-1, width)
    derivative_entering, grad_out, grad_filter = decode_rows(
        mixed_in,
        wanted_lines,
        output_weight,
        spectral_filter_weight,
        forward_transform,
        inverse_transform,
        loss_scale,
    )
    derivative_bottleneck = jnp.einsum(
        "orm,rm->om", derivative_entering.reshape(samples, sub_dev, width), gain_row_values
    )
    count = lax.axis_size("freq")
    half_width = grad_filter.shape[1]
    filter_rows = jnp.concatenate(
        [grad_filter, jnp.zeros((grad_filter.shape[0], width - half_width), jnp.float32)], 1
    )
    packed_rows = grad_out.shape[0] + samples + filter_rows.shape[0]
    padding = -packed_rows % count
    packed = jnp.concatenate(
        [
            grad_out,
            derivative_bottleneck,
            filter_rows,
            jnp.zeros((padding, width), jnp.float32),
        ],
        0,
    )
    packed = sum_halving(packed, "freq")
    rows_out = grad_out.shape[0]
    grad_out = packed[:rows_out].astype(jnp.float32)
    derivative_bottleneck = packed[rows_out : rows_out + samples].astype(jnp.float32)
    grad_filter = packed[
        rows_out + samples : rows_out + samples + filter_rows.shape[0], :half_width
    ].astype(jnp.float32)
    grad_enc, grad_dec = encoder_grads(
        inputs_by_sample, codes_by_sample, derivative_bottleneck, decoder_weight
    )
    return (grad_enc, grad_dec, grad_out, grad_filter)


def solution(mesh):
    return jax.shard_map(
        local,
        mesh=mesh,
        in_specs=(
            P(("groups", "freq"), None),
            P("groups", "freq", None),
            P("groups"),
            P(),
            P(),
            P("freq", None),
            P(),
            P(),
        ),
        out_specs=(P("groups", None), P("groups", None), P("groups", None), P("groups", None)),
        check_vma=False,
    )
```

```python
import math

import jax
import ml_dtypes
import numpy as np
import jax.numpy as jnp
from jax import lax
from jax.sharding import PartitionSpec as P


def rotation_tables(antennas):
    indices = np.arange(antennas, dtype=np.int32)
    products_mod = indices[:, None] * indices[None, :] % antennas
    angle_table = products_mod.astype(np.float32) * np.float32(2.0 * math.pi / antennas)
    cosine_table = np.cos(angle_table) / np.float32(math.sqrt(antennas))
    sine_table = np.sin(angle_table) / np.float32(math.sqrt(antennas))
    forward_transform = np.concatenate(
        [
            np.concatenate([cosine_table, -sine_table], 1),
            np.concatenate([sine_table, cosine_table], 1),
        ],
        0,
    )
    inverse_transform = np.concatenate(
        [
            np.concatenate([cosine_table, sine_table], 1),
            np.concatenate([-sine_table, cosine_table], 1),
        ],
        0,
    )
    return (
        jnp.asarray(forward_transform.astype(ml_dtypes.bfloat16)),
        jnp.asarray(inverse_transform.astype(ml_dtypes.bfloat16)),
    )


def decode_rows(
    mixed_in,
    wanted_lines,
    output_weight,
    spectral_filter_weight,
    forward_transform,
    inverse_transform,
    loss_scale,
):
    filter_re = spectral_filter_weight[0]
    filter_im = spectral_filter_weight[1]
    spectrum = jnp.dot(mixed_in, forward_transform, preferred_element_type=jnp.float32)
    half_width = spectrum.shape[1] // 2
    spec_re = spectrum[:, :half_width]
    spec_im = spectrum[:, half_width:]
    filtered = jnp.concatenate(
        [spec_re * filter_re - spec_im * filter_im, spec_re * filter_im + spec_im * filter_re], 1
    ).astype(jnp.bfloat16)
    mixed_back = lax.dot_general(
        filtered, forward_transform, (((1,), (1,)), ((), ())), preferred_element_type=jnp.float32
    )
    hidden = (mixed_in.astype(jnp.float32) + jax.nn.gelu(mixed_back)).astype(jnp.bfloat16)
    rebuilt = hidden.astype(jnp.float32) + jnp.dot(
        hidden, output_weight, preferred_element_type=jnp.float32
    )
    residual = loss_scale * (rebuilt - wanted_lines.astype(jnp.float32))
    residual_half = residual.astype(jnp.bfloat16)
    grad_out = lax.dot_general(
        hidden, residual_half, (((0,), (0,)), ((), ())), preferred_element_type=jnp.float32
    )
    grad_hidden = residual + lax.dot_general(
        residual_half, output_weight, (((1,), (1,)), ((), ())), preferred_element_type=jnp.float32
    )
    grad_mixed = jax.vjp(jax.nn.gelu, mixed_back)[1](grad_hidden)[0].astype(jnp.bfloat16)
    grad_filtered = jnp.dot(grad_mixed, forward_transform, preferred_element_type=jnp.float32)
    grad_re = grad_filtered[:, :half_width]
    grad_im = grad_filtered[:, half_width:]
    grad_filter = jnp.stack(
        [
            jnp.sum(grad_re * spec_re + grad_im * spec_im, 0),
            jnp.sum(grad_im * spec_re - grad_re * spec_im, 0),
        ]
    )
    grad_spec = jnp.concatenate(
        [grad_re * filter_re + grad_im * filter_im, grad_im * filter_re - grad_re * filter_im], 1
    ).astype(jnp.bfloat16)
    derivative_entering = grad_hidden + lax.dot_general(
        grad_spec, forward_transform, (((1,), (1,)), ((), ())), preferred_element_type=jnp.float32
    )
    return (derivative_entering, grad_out, grad_filter)


def encoder_grads(inputs_rows, codewords, latent_sums, decoder_weight):
    latent_half = latent_sums.astype(jnp.bfloat16)
    grad_dec = lax.dot_general(
        codewords, latent_half, (((0,), (0,)), ((), ())), preferred_element_type=jnp.float32
    )
    grad_codes = lax.dot_general(
        latent_half, decoder_weight, (((1,), (1,)), ((), ())), preferred_element_type=jnp.float32
    )
    grad_pre = (grad_codes * (1.0 - jnp.square(codewords.astype(jnp.float32)))).astype(jnp.bfloat16)
    grad_enc = lax.dot_general(
        inputs_rows, grad_pre, (((0,), (0,)), ((), ())), preferred_element_type=jnp.float32
    )
    return (grad_enc, grad_dec)


def _exchange_pairs(count, distance):
    return [(i, i ^ distance) for i in range(count)]


def _is_power_of_two(count):
    return count > 0 and count & (count - 1) == 0


def gather_rows(block, axis_name):
    count = lax.axis_size(axis_name)
    if not _is_power_of_two(count):
        return lax.all_gather(block, axis_name, axis=0, tiled=True)
    position = lax.axis_index(axis_name)
    distance = count // 2
    while distance >= 1:
        other = lax.ppermute(block, axis_name, _exchange_pairs(count, distance))
        lower = (position // distance) % 2 == 0
        block = jnp.where(
            lower, jnp.concatenate([block, other], 0), jnp.concatenate([other, block], 0)
        )
        distance //= 2
    return block


def bit_reversed_blocks(values, count):
    if not _is_power_of_two(count):
        return values
    bits = count.bit_length() - 1
    blocks = values.reshape((2,) * bits + (-1,))
    return blocks.transpose(tuple(reversed(range(bits))) + (bits,)).reshape(-1)


def sum_whole(values, axis_name):
    count = lax.axis_size(axis_name)
    if not _is_power_of_two(count):
        return lax.psum(values, axis_name)
    distance = 1
    while distance < count:
        values = values + lax.ppermute(values, axis_name, _exchange_pairs(count, distance))
        distance *= 2
    return values


def sum_halving(values, axis_name, wire=jnp.bfloat16, halving_levels=2):
    count = lax.axis_size(axis_name)
    if not _is_power_of_two(count) or values.shape[0] % count != 0:
        return lax.psum(values, axis_name)
    position = lax.axis_index(axis_name)
    distance = 1
    while distance < count and distance < 2**halving_levels:
        half = values.shape[0] // 2
        lower = (position // distance) % 2 == 0
        keep = jnp.where(lower, values[:half], values[half:])
        send = jnp.where(lower, values[half:], values[:half]).astype(wire)
        arrived = lax.ppermute(send, axis_name, _exchange_pairs(count, distance))
        values = keep + arrived.astype(keep.dtype)
        distance *= 2
    top = distance
    values = values.astype(wire)
    while distance < count:
        arrived = lax.ppermute(values, axis_name, _exchange_pairs(count, distance))
        values = (values.astype(jnp.float32) + arrived.astype(jnp.float32)).astype(wire)
        distance *= 2
    distance = top // 2
    while distance >= 1:
        other = lax.ppermute(values, axis_name, _exchange_pairs(count, distance))
        lower = (position // distance) % 2 == 0
        values = jnp.where(
            lower, jnp.concatenate([values, other], 0), jnp.concatenate([other, values], 0)
        )
        distance //= 2
    return values


def local(
    encoder_input,
    desired_responses,
    sample_index,
    encoder_weight,
    decoder_weight,
    frequency_amplitude,
    spectral_filter_weight,
    output_weight,
):
    samples = sample_index.shape[0]
    sub_dev = desired_responses.shape[1]
    width = desired_responses.shape[2]
    forward_transform, inverse_transform = rotation_tables(width // 2)
    loss_scale = 1.0 / math.sqrt(samples * sub_dev * lax.axis_size("freq"))
    all_inputs = gather_rows(encoder_input, "freq")
    gathered_index = bit_reversed_blocks(sample_index, lax.axis_size("freq"))
    selection = (
        gathered_index[None, :] == jnp.arange(samples, dtype=jnp.int32)[:, None]
    ).astype(jnp.bfloat16)
    inputs_by_sample = jnp.dot(selection, all_inputs, preferred_element_type=jnp.float32).astype(
        jnp.bfloat16
    )
    codes_by_sample = jnp.tanh(
        jnp.dot(inputs_by_sample, encoder_weight, preferred_element_type=jnp.float32)
    ).astype(jnp.bfloat16)
    latent = jnp.dot(codes_by_sample, decoder_weight, preferred_element_type=jnp.float32)
    gain_row_values = frequency_amplitude.astype(jnp.float32)
    mixed_in = (latent[:, None, :] * gain_row_values[None]).astype(jnp.bfloat16).reshape(-1, width)
    wanted_lines = desired_responses.reshape(-1, width)
    derivative_entering, grad_out, grad_filter = decode_rows(
        mixed_in,
        wanted_lines,
        output_weight,
        spectral_filter_weight,
        forward_transform,
        inverse_transform,
        loss_scale,
    )
    derivative_bottleneck = jnp.einsum(
        "orm,rm->om", derivative_entering.reshape(samples, sub_dev, width), gain_row_values
    )
    count = lax.axis_size("freq")
    half_width = grad_filter.shape[1]
    filter_rows = jnp.concatenate(
        [grad_filter, jnp.zeros((grad_filter.shape[0], width - half_width), jnp.float32)], 1
    )
    packed_rows = grad_out.shape[0] + samples + filter_rows.shape[0]
    padding = -packed_rows % count
    packed = jnp.concatenate(
        [
            grad_out,
            derivative_bottleneck,
            filter_rows,
            jnp.zeros((padding, width), jnp.float32),
        ],
        0,
    )
    columns = packed.shape[1] // 2
    packed = jnp.concatenate(
        [sum_halving(packed[:, :columns], "freq"), sum_halving(packed[:, columns:], "freq")], 1
    )
    rows_out = grad_out.shape[0]
    grad_out = packed[:rows_out].astype(jnp.float32)
    derivative_bottleneck = packed[rows_out : rows_out + samples].astype(jnp.float32)
    grad_filter = packed[
        rows_out + samples : rows_out + samples + filter_rows.shape[0], :half_width
    ].astype(jnp.float32)
    grad_enc, grad_dec = encoder_grads(
        inputs_by_sample, codes_by_sample, derivative_bottleneck, decoder_weight
    )
    return (grad_enc, grad_dec, grad_out, grad_filter)


def solution(mesh):
    return jax.shard_map(
        local,
        mesh=mesh,
        in_specs=(
            P(("groups", "freq"), None),
            P("groups", "freq", None),
            P("groups"),
            P(),
            P(),
            P("freq", None),
            P(),
            P(),
        ),
        out_specs=(P("groups", None), P("groups", None), P("groups", None), P("groups", None)),
        check_vma=False,
    )
```

```python
import math

import jax
import ml_dtypes
import numpy as np
import jax.numpy as jnp
from jax import lax
from jax.sharding import PartitionSpec as P


def rotation_tables(antennas):
    indices = np.arange(antennas, dtype=np.int32)
    products_mod = indices[:, None] * indices[None, :] % antennas
    angle_table = products_mod.astype(np.float32) * np.float32(2.0 * math.pi / antennas)
    cosine_table = np.cos(angle_table) / np.float32(math.sqrt(antennas))
    sine_table = np.sin(angle_table) / np.float32(math.sqrt(antennas))
    forward_transform = np.concatenate(
        [
            np.concatenate([cosine_table, -sine_table], 1),
            np.concatenate([sine_table, cosine_table], 1),
        ],
        0,
    )
    inverse_transform = np.concatenate(
        [
            np.concatenate([cosine_table, sine_table], 1),
            np.concatenate([-sine_table, cosine_table], 1),
        ],
        0,
    )
    return (
        jnp.asarray(forward_transform.astype(ml_dtypes.bfloat16)),
        jnp.asarray(inverse_transform.astype(ml_dtypes.bfloat16)),
    )


def decode_rows(
    mixed_in,
    wanted_lines,
    output_weight,
    spectral_filter_weight,
    forward_transform,
    inverse_transform,
    loss_scale,
):
    filter_re = spectral_filter_weight[0]
    filter_im = spectral_filter_weight[1]
    spectrum = jnp.dot(mixed_in, forward_transform, preferred_element_type=jnp.float32)
    half_width = spectrum.shape[1] // 2
    spec_re = spectrum[:, :half_width]
    spec_im = spectrum[:, half_width:]
    filtered = jnp.concatenate(
        [spec_re * filter_re - spec_im * filter_im, spec_re * filter_im + spec_im * filter_re], 1
    ).astype(jnp.bfloat16)
    mixed_back = lax.dot_general(
        filtered, forward_transform, (((1,), (1,)), ((), ())), preferred_element_type=jnp.float32
    )
    hidden = (mixed_in.astype(jnp.float32) + jax.nn.gelu(mixed_back)).astype(jnp.bfloat16)
    rebuilt = hidden.astype(jnp.float32) + jnp.dot(
        hidden, output_weight, preferred_element_type=jnp.float32
    )
    residual = loss_scale * (rebuilt - wanted_lines.astype(jnp.float32))
    residual_half = residual.astype(jnp.bfloat16)
    grad_out = lax.dot_general(
        hidden, residual_half, (((0,), (0,)), ((), ())), preferred_element_type=jnp.float32
    )
    grad_hidden = residual + lax.dot_general(
        residual_half, output_weight, (((1,), (1,)), ((), ())), preferred_element_type=jnp.float32
    )
    grad_mixed = jax.vjp(jax.nn.gelu, mixed_back)[1](grad_hidden)[0].astype(jnp.bfloat16)
    grad_filtered = jnp.dot(grad_mixed, forward_transform, preferred_element_type=jnp.float32)
    grad_re = grad_filtered[:, :half_width]
    grad_im = grad_filtered[:, half_width:]
    grad_filter = jnp.stack(
        [
            jnp.sum(grad_re * spec_re + grad_im * spec_im, 0),
            jnp.sum(grad_im * spec_re - grad_re * spec_im, 0),
        ]
    )
    grad_spec = jnp.concatenate(
        [grad_re * filter_re + grad_im * filter_im, grad_im * filter_re - grad_re * filter_im], 1
    ).astype(jnp.bfloat16)
    derivative_entering = grad_hidden + lax.dot_general(
        grad_spec, forward_transform, (((1,), (1,)), ((), ())), preferred_element_type=jnp.float32
    )
    return (derivative_entering, grad_out, grad_filter)


def encoder_grads(inputs_rows, codewords, latent_sums, decoder_weight):
    latent_half = latent_sums.astype(jnp.bfloat16)
    grad_dec = lax.dot_general(
        codewords, latent_half, (((0,), (0,)), ((), ())), preferred_element_type=jnp.float32
    )
    grad_codes = lax.dot_general(
        latent_half, decoder_weight, (((1,), (1,)), ((), ())), preferred_element_type=jnp.float32
    )
    grad_pre = (grad_codes * (1.0 - jnp.square(codewords.astype(jnp.float32)))).astype(jnp.bfloat16)
    grad_enc = lax.dot_general(
        inputs_rows, grad_pre, (((0,), (0,)), ((), ())), preferred_element_type=jnp.float32
    )
    return (grad_enc, grad_dec)


def _exchange_pairs(count, distance):
    return [(i, i ^ distance) for i in range(count)]


def _is_power_of_two(count):
    return count > 0 and count & (count - 1) == 0


def gather_rows(block, axis_name):
    count = lax.axis_size(axis_name)
    if not _is_power_of_two(count):
        return lax.all_gather(block, axis_name, axis=0, tiled=True)
    position = lax.axis_index(axis_name)
    distance = count // 2
    while distance >= 1:
        other = lax.ppermute(block, axis_name, _exchange_pairs(count, distance))
        lower = (position // distance) % 2 == 0
        block = jnp.where(
            lower, jnp.concatenate([block, other], 0), jnp.concatenate([other, block], 0)
        )
        distance //= 2
    return block


def bit_reversed_blocks(values, count):
    if not _is_power_of_two(count):
        return values
    bits = count.bit_length() - 1
    blocks = values.reshape((2,) * bits + (-1,))
    return blocks.transpose(tuple(reversed(range(bits))) + (bits,)).reshape(-1)


def sum_whole(values, axis_name):
    count = lax.axis_size(axis_name)
    if not _is_power_of_two(count):
        return lax.psum(values, axis_name)
    distance = 1
    while distance < count:
        values = values + lax.ppermute(values, axis_name, _exchange_pairs(count, distance))
        distance *= 2
    return values


def sum_halving(values, axis_name, wire=jnp.bfloat16, halving_levels=2):
    count = lax.axis_size(axis_name)
    if not _is_power_of_two(count) or values.shape[0] % count != 0:
        return lax.psum(values, axis_name)
    position = lax.axis_index(axis_name)
    distance = 1
    while distance < count and distance < 2**halving_levels:
        half = values.shape[0] // 2
        lower = (position // distance) % 2 == 0
        keep = jnp.where(lower, values[:half], values[half:])
        send = jnp.where(lower, values[half:], values[:half]).astype(wire)
        arrived = lax.ppermute(send, axis_name, _exchange_pairs(count, distance))
        values = keep + arrived.astype(keep.dtype)
        distance *= 2
    top = distance
    values = values.astype(wire)
    while distance < count:
        arrived = lax.ppermute(values, axis_name, _exchange_pairs(count, distance))
        values = (values.astype(jnp.float32) + arrived.astype(jnp.float32)).astype(wire)
        distance *= 2
    distance = top // 2
    while distance >= 1:
        other = lax.ppermute(values, axis_name, _exchange_pairs(count, distance))
        lower = (position // distance) % 2 == 0
        values = jnp.where(
            lower, jnp.concatenate([values, other], 0), jnp.concatenate([other, values], 0)
        )
        distance //= 2
    return values


def local(
    encoder_input,
    desired_responses,
    sample_index,
    encoder_weight,
    decoder_weight,
    frequency_amplitude,
    spectral_filter_weight,
    output_weight,
):
    samples = sample_index.shape[0]
    sub_dev = desired_responses.shape[1]
    width = desired_responses.shape[2]
    forward_transform, inverse_transform = rotation_tables(width // 2)
    loss_scale = 1.0 / math.sqrt(samples * sub_dev * lax.axis_size("freq"))
    all_inputs = gather_rows(encoder_input, "freq")
    gathered_index = bit_reversed_blocks(sample_index, lax.axis_size("freq"))
    selection = (
        gathered_index[None, :] == jnp.arange(samples, dtype=jnp.int32)[:, None]
    ).astype(jnp.bfloat16)
    inputs_by_sample = jnp.dot(selection, all_inputs, preferred_element_type=jnp.float32).astype(
        jnp.bfloat16
    )
    codes_by_sample = jnp.tanh(
        jnp.dot(inputs_by_sample, encoder_weight, preferred_element_type=jnp.float32)
    ).astype(jnp.bfloat16)
    latent = jnp.dot(codes_by_sample, decoder_weight, preferred_element_type=jnp.float32)
    gain_row_values = frequency_amplitude.astype(jnp.float32)
    mixed_in = (latent[:, None, :] * gain_row_values[None]).astype(jnp.bfloat16).reshape(-1, width)
    wanted_lines = desired_responses.reshape(-1, width)
    derivative_entering, grad_out, grad_filter = decode_rows(
        mixed_in,
        wanted_lines,
        output_weight,
        spectral_filter_weight,
        forward_transform,
        inverse_transform,
        loss_scale,
    )
    derivative_bottleneck = jnp.einsum(
        "orm,rm->om", derivative_entering.reshape(samples, sub_dev, width), gain_row_values
    )
    count = lax.axis_size("freq")
    half_width = grad_filter.shape[1]
    filter_rows = jnp.concatenate(
        [grad_filter, jnp.zeros((grad_filter.shape[0], width - half_width), jnp.float32)], 1
    )
    packed_rows = grad_out.shape[0] + samples + filter_rows.shape[0]
    padding = -packed_rows % count
    packed = jnp.concatenate(
        [
            grad_out,
            derivative_bottleneck,
            filter_rows,
            jnp.zeros((padding, width), jnp.float32),
        ],
        0,
    )
    pieces = 4 if width % (4 * 128) == 0 else 1
    columns = width // pieces
    packed = jnp.concatenate(
        [
            sum_halving(packed[:, piece * columns : (piece + 1) * columns], "freq")
            for piece in range(pieces)
        ],
        1,
    )
    rows_out = grad_out.shape[0]
    grad_out = packed[:rows_out].astype(jnp.float32)
    derivative_bottleneck = packed[rows_out : rows_out + samples].astype(jnp.float32)
    grad_filter = packed[
        rows_out + samples : rows_out + samples + filter_rows.shape[0], :half_width
    ].astype(jnp.float32)
    grad_enc, grad_dec = encoder_grads(
        inputs_by_sample, codes_by_sample, derivative_bottleneck, decoder_weight
    )
    return (grad_enc, grad_dec, grad_out, grad_filter)


def solution(mesh):
    return jax.shard_map(
        local,
        mesh=mesh,
        in_specs=(
            P(("groups", "freq"), None),
            P("groups", "freq", None),
            P("groups"),
            P(),
            P(),
            P("freq", None),
            P(),
            P(),
        ),
        out_specs=(P("groups", None), P("groups", None), P("groups", None), P("groups", None)),
        check_vma=False,
    )
```

```python
import math

import jax
import ml_dtypes
import numpy as np
import jax.numpy as jnp
from jax import lax
from jax.sharding import PartitionSpec as P


def rotation_tables(antennas):
    indices = np.arange(antennas, dtype=np.int32)
    products_mod = indices[:, None] * indices[None, :] % antennas
    angle_table = products_mod.astype(np.float32) * np.float32(2.0 * math.pi / antennas)
    cosine_table = np.cos(angle_table) / np.float32(math.sqrt(antennas))
    sine_table = np.sin(angle_table) / np.float32(math.sqrt(antennas))
    forward_transform = np.concatenate(
        [
            np.concatenate([cosine_table, -sine_table], 1),
            np.concatenate([sine_table, cosine_table], 1),
        ],
        0,
    )
    inverse_transform = np.concatenate(
        [
            np.concatenate([cosine_table, sine_table], 1),
            np.concatenate([-sine_table, cosine_table], 1),
        ],
        0,
    )
    return (
        jnp.asarray(forward_transform.astype(ml_dtypes.bfloat16)),
        jnp.asarray(inverse_transform.astype(ml_dtypes.bfloat16)),
    )


def decode_rows(
    mixed_in,
    wanted_lines,
    output_weight,
    spectral_filter_weight,
    forward_transform,
    inverse_transform,
    loss_scale,
):
    filter_re = spectral_filter_weight[0]
    filter_im = spectral_filter_weight[1]
    spectrum = jnp.dot(mixed_in, forward_transform, preferred_element_type=jnp.float32)
    half_width = spectrum.shape[1] // 2
    spec_re = spectrum[:, :half_width]
    spec_im = spectrum[:, half_width:]
    filtered = jnp.concatenate(
        [spec_re * filter_re - spec_im * filter_im, spec_re * filter_im + spec_im * filter_re], 1
    ).astype(jnp.bfloat16)
    mixed_back = lax.dot_general(
        filtered, forward_transform, (((1,), (1,)), ((), ())), preferred_element_type=jnp.float32
    )
    hidden = (mixed_in.astype(jnp.float32) + jax.nn.gelu(mixed_back)).astype(jnp.bfloat16)
    rebuilt = hidden.astype(jnp.float32) + jnp.dot(
        hidden, output_weight, preferred_element_type=jnp.float32
    )
    residual = loss_scale * (rebuilt - wanted_lines.astype(jnp.float32))
    residual_half = residual.astype(jnp.bfloat16)
    grad_out = lax.dot_general(
        hidden, residual_half, (((0,), (0,)), ((), ())), preferred_element_type=jnp.float32
    )
    grad_hidden = residual + lax.dot_general(
        residual_half, output_weight, (((1,), (1,)), ((), ())), preferred_element_type=jnp.float32
    )
    grad_mixed = jax.vjp(jax.nn.gelu, mixed_back)[1](grad_hidden)[0].astype(jnp.bfloat16)
    grad_filtered = jnp.dot(grad_mixed, forward_transform, preferred_element_type=jnp.float32)
    grad_re = grad_filtered[:, :half_width]
    grad_im = grad_filtered[:, half_width:]
    grad_filter = jnp.stack(
        [
            jnp.sum(grad_re * spec_re + grad_im * spec_im, 0),
            jnp.sum(grad_im * spec_re - grad_re * spec_im, 0),
        ]
    )
    grad_spec = jnp.concatenate(
        [grad_re * filter_re + grad_im * filter_im, grad_im * filter_re - grad_re * filter_im], 1
    ).astype(jnp.bfloat16)
    derivative_entering = grad_hidden + lax.dot_general(
        grad_spec, forward_transform, (((1,), (1,)), ((), ())), preferred_element_type=jnp.float32
    )
    return (derivative_entering, grad_out, grad_filter)


def encoder_grads(inputs_rows, codewords, latent_sums, decoder_weight):
    latent_half = latent_sums.astype(jnp.bfloat16)
    grad_dec = lax.dot_general(
        codewords, latent_half, (((0,), (0,)), ((), ())), preferred_element_type=jnp.float32
    )
    grad_codes = lax.dot_general(
        latent_half, decoder_weight, (((1,), (1,)), ((), ())), preferred_element_type=jnp.float32
    )
    grad_pre = (grad_codes * (1.0 - jnp.square(codewords.astype(jnp.float32)))).astype(jnp.bfloat16)
    grad_enc = lax.dot_general(
        inputs_rows, grad_pre, (((0,), (0,)), ((), ())), preferred_element_type=jnp.float32
    )
    return (grad_enc, grad_dec)


def _exchange_pairs(count, distance):
    return [(i, i ^ distance) for i in range(count)]


def _is_power_of_two(count):
    return count > 0 and count & (count - 1) == 0


def gather_rows(block, axis_name):
    count = lax.axis_size(axis_name)
    if not _is_power_of_two(count):
        return lax.all_gather(block, axis_name, axis=0, tiled=True)
    position = lax.axis_index(axis_name)
    distance = count // 2
    while distance >= 1:
        other = lax.ppermute(block, axis_name, _exchange_pairs(count, distance))
        lower = (position // distance) % 2 == 0
        block = jnp.where(
            lower, jnp.concatenate([block, other], 0), jnp.concatenate([other, block], 0)
        )
        distance //= 2
    return block


def bit_reversed_blocks(values, count):
    if not _is_power_of_two(count):
        return values
    bits = count.bit_length() - 1
    blocks = values.reshape((2,) * bits + (-1,))
    return blocks.transpose(tuple(reversed(range(bits))) + (bits,)).reshape(-1)


def sum_whole(values, axis_name):
    count = lax.axis_size(axis_name)
    if not _is_power_of_two(count):
        return lax.psum(values, axis_name)
    distance = 1
    while distance < count:
        values = values + lax.ppermute(values, axis_name, _exchange_pairs(count, distance))
        distance *= 2
    return values


def sum_halving(values, axis_name, halving=(1, 2), wire=jnp.bfloat16):
    count = lax.axis_size(axis_name)
    if not _is_power_of_two(count) or values.shape[0] % count != 0:
        return lax.psum(values, axis_name)
    halving = tuple(distance for distance in halving if distance < count)
    position = lax.axis_index(axis_name)
    for distance in halving:
        half = values.shape[0] // 2
        lower = (position // distance) % 2 == 0
        keep = jnp.where(lower, values[:half], values[half:])
        send = jnp.where(lower, values[half:], values[:half]).astype(wire)
        arrived = lax.ppermute(send, axis_name, _exchange_pairs(count, distance))
        values = keep + arrived.astype(keep.dtype)
    values = values.astype(wire)
    distance = 1
    while distance < count:
        if distance not in halving:
            arrived = lax.ppermute(values, axis_name, _exchange_pairs(count, distance))
            values = (values.astype(jnp.float32) + arrived.astype(jnp.float32)).astype(wire)
        distance *= 2
    for distance in reversed(halving):
        other = lax.ppermute(values, axis_name, _exchange_pairs(count, distance))
        lower = (position // distance) % 2 == 0
        values = jnp.where(
            lower, jnp.concatenate([values, other], 0), jnp.concatenate([other, values], 0)
        )
    return values


def local(
    encoder_input,
    desired_responses,
    sample_index,
    encoder_weight,
    decoder_weight,
    frequency_amplitude,
    spectral_filter_weight,
    output_weight,
):
    samples = sample_index.shape[0]
    sub_dev = desired_responses.shape[1]
    width = desired_responses.shape[2]
    forward_transform, inverse_transform = rotation_tables(width // 2)
    loss_scale = 1.0 / math.sqrt(samples * sub_dev * lax.axis_size("freq"))
    all_inputs = gather_rows(encoder_input, "freq")
    gathered_index = bit_reversed_blocks(sample_index, lax.axis_size("freq"))
    selection = (
        gathered_index[None, :] == jnp.arange(samples, dtype=jnp.int32)[:, None]
    ).astype(jnp.bfloat16)
    inputs_by_sample = jnp.dot(selection, all_inputs, preferred_element_type=jnp.float32).astype(
        jnp.bfloat16
    )
    codes_by_sample = jnp.tanh(
        jnp.dot(inputs_by_sample, encoder_weight, preferred_element_type=jnp.float32)
    ).astype(jnp.bfloat16)
    latent = jnp.dot(codes_by_sample, decoder_weight, preferred_element_type=jnp.float32)
    gain_row_values = frequency_amplitude.astype(jnp.float32)
    mixed_in = (latent[:, None, :] * gain_row_values[None]).astype(jnp.bfloat16).reshape(-1, width)
    wanted_lines = desired_responses.reshape(-1, width)
    derivative_entering, grad_out, grad_filter = decode_rows(
        mixed_in,
        wanted_lines,
        output_weight,
        spectral_filter_weight,
        forward_transform,
        inverse_transform,
        loss_scale,
    )
    derivative_bottleneck = jnp.einsum(
        "orm,rm->om", derivative_entering.reshape(samples, sub_dev, width), gain_row_values
    )
    count = lax.axis_size("freq")
    half_width = grad_filter.shape[1]
    filter_rows = jnp.concatenate(
        [grad_filter, jnp.zeros((grad_filter.shape[0], width - half_width), jnp.float32)], 1
    )
    packed_rows = grad_out.shape[0] + samples + filter_rows.shape[0]
    padding = -packed_rows % count
    packed = jnp.concatenate(
        [
            grad_out,
            derivative_bottleneck,
            filter_rows,
            jnp.zeros((padding, width), jnp.float32),
        ],
        0,
    )
    columns = packed.shape[1] // 2
    packed = jnp.concatenate(
        [
            sum_halving(packed[:, :columns], "freq", (1, 2)),
            sum_halving(packed[:, columns:], "freq", (1, 4)),
        ],
        1,
    )
    rows_out = grad_out.shape[0]
    grad_out = packed[:rows_out].astype(jnp.float32)
    derivative_bottleneck = packed[rows_out : rows_out + samples].astype(jnp.float32)
    grad_filter = packed[
        rows_out + samples : rows_out + samples + filter_rows.shape[0], :half_width
    ].astype(jnp.float32)
    grad_enc, grad_dec = encoder_grads(
        inputs_by_sample, codes_by_sample, derivative_bottleneck, decoder_weight
    )
    return (grad_enc, grad_dec, grad_out, grad_filter)


def solution(mesh):
    return jax.shard_map(
        local,
        mesh=mesh,
        in_specs=(
            P(("groups", "freq"), None),
            P("groups", "freq", None),
            P("groups"),
            P(),
            P(),
            P("freq", None),
            P(),
            P(),
        ),
        out_specs=(P("groups", None), P("groups", None), P("groups", None), P("groups", None)),
        check_vma=False,
    )
```

```python
import math

import jax
import ml_dtypes
import numpy as np
import jax.numpy as jnp
from jax import lax
from jax.sharding import PartitionSpec as P


def rotation_tables(antennas):
    indices = np.arange(antennas, dtype=np.int32)
    products_mod = indices[:, None] * indices[None, :] % antennas
    angle_table = products_mod.astype(np.float32) * np.float32(2.0 * math.pi / antennas)
    cosine_table = np.cos(angle_table) / np.float32(math.sqrt(antennas))
    sine_table = np.sin(angle_table) / np.float32(math.sqrt(antennas))
    forward_transform = np.concatenate(
        [
            np.concatenate([cosine_table, -sine_table], 1),
            np.concatenate([sine_table, cosine_table], 1),
        ],
        0,
    )
    inverse_transform = np.concatenate(
        [
            np.concatenate([cosine_table, sine_table], 1),
            np.concatenate([-sine_table, cosine_table], 1),
        ],
        0,
    )
    return (
        jnp.asarray(forward_transform.astype(ml_dtypes.bfloat16)),
        jnp.asarray(inverse_transform.astype(ml_dtypes.bfloat16)),
    )


def decode_rows(
    mixed_in,
    wanted_lines,
    output_weight,
    spectral_filter_weight,
    forward_transform,
    inverse_transform,
    loss_scale,
):
    filter_re = spectral_filter_weight[0]
    filter_im = spectral_filter_weight[1]
    spectrum = jnp.dot(mixed_in, forward_transform, preferred_element_type=jnp.float32)
    half_width = spectrum.shape[1] // 2
    spec_re = spectrum[:, :half_width]
    spec_im = spectrum[:, half_width:]
    filtered = jnp.concatenate(
        [spec_re * filter_re - spec_im * filter_im, spec_re * filter_im + spec_im * filter_re], 1
    ).astype(jnp.bfloat16)
    mixed_back = lax.dot_general(
        filtered, forward_transform, (((1,), (1,)), ((), ())), preferred_element_type=jnp.float32
    )
    hidden = (mixed_in.astype(jnp.float32) + jax.nn.gelu(mixed_back)).astype(jnp.bfloat16)
    rebuilt = hidden.astype(jnp.float32) + jnp.dot(
        hidden, output_weight, preferred_element_type=jnp.float32
    )
    residual = loss_scale * (rebuilt - wanted_lines.astype(jnp.float32))
    residual_half = residual.astype(jnp.bfloat16)
    grad_out = lax.dot_general(
        hidden, residual_half, (((0,), (0,)), ((), ())), preferred_element_type=jnp.float32
    )
    grad_hidden = residual + lax.dot_general(
        residual_half, output_weight, (((1,), (1,)), ((), ())), preferred_element_type=jnp.float32
    )
    grad_mixed = jax.vjp(jax.nn.gelu, mixed_back)[1](grad_hidden)[0].astype(jnp.bfloat16)
    grad_filtered = jnp.dot(grad_mixed, forward_transform, preferred_element_type=jnp.float32)
    grad_re = grad_filtered[:, :half_width]
    grad_im = grad_filtered[:, half_width:]
    grad_filter = jnp.stack(
        [
            jnp.sum(grad_re * spec_re + grad_im * spec_im, 0),
            jnp.sum(grad_im * spec_re - grad_re * spec_im, 0),
        ]
    )
    grad_spec = jnp.concatenate(
        [grad_re * filter_re + grad_im * filter_im, grad_im * filter_re - grad_re * filter_im], 1
    ).astype(jnp.bfloat16)
    derivative_entering = grad_hidden + lax.dot_general(
        grad_spec, forward_transform, (((1,), (1,)), ((), ())), preferred_element_type=jnp.float32
    )
    return (derivative_entering, grad_out, grad_filter)


def encoder_grads(inputs_rows, codewords, latent_sums, decoder_weight):
    latent_half = latent_sums.astype(jnp.bfloat16)
    grad_dec = lax.dot_general(
        codewords, latent_half, (((0,), (0,)), ((), ())), preferred_element_type=jnp.float32
    )
    grad_codes = lax.dot_general(
        latent_half, decoder_weight, (((1,), (1,)), ((), ())), preferred_element_type=jnp.float32
    )
    grad_pre = (grad_codes * (1.0 - jnp.square(codewords.astype(jnp.float32)))).astype(jnp.bfloat16)
    grad_enc = lax.dot_general(
        inputs_rows, grad_pre, (((0,), (0,)), ((), ())), preferred_element_type=jnp.float32
    )
    return (grad_enc, grad_dec)


def _exchange_pairs(count, distance):
    return [(i, i ^ distance) for i in range(count)]


def _is_power_of_two(count):
    return count > 0 and count & (count - 1) == 0


def gather_rows(block, axis_name):
    count = lax.axis_size(axis_name)
    if not _is_power_of_two(count):
        return lax.all_gather(block, axis_name, axis=0, tiled=True)
    position = lax.axis_index(axis_name)
    distance = count // 2
    while distance >= 1:
        other = lax.ppermute(block, axis_name, _exchange_pairs(count, distance))
        lower = (position // distance) % 2 == 0
        block = jnp.where(
            lower, jnp.concatenate([block, other], 0), jnp.concatenate([other, block], 0)
        )
        distance //= 2
    return block


def bit_reversed_blocks(values, count):
    if not _is_power_of_two(count):
        return values
    bits = count.bit_length() - 1
    blocks = values.reshape((2,) * bits + (-1,))
    return blocks.transpose(tuple(reversed(range(bits))) + (bits,)).reshape(-1)


def sum_whole(values, axis_name):
    count = lax.axis_size(axis_name)
    if not _is_power_of_two(count):
        return lax.psum(values, axis_name)
    distance = 1
    while distance < count:
        values = values + lax.ppermute(values, axis_name, _exchange_pairs(count, distance))
        distance *= 2
    return values


def sum_halving(values, axis_name, wire=jnp.bfloat16, halving_levels=2):
    count = lax.axis_size(axis_name)
    if not _is_power_of_two(count) or values.shape[0] % min(count, 2**halving_levels) != 0:
        return lax.psum(values, axis_name)
    position = lax.axis_index(axis_name)
    distance = 1
    while distance < count and distance < 2**halving_levels:
        half = values.shape[0] // 2
        lower = (position // distance) % 2 == 0
        keep = jnp.where(lower, values[:half], values[half:])
        send = jnp.where(lower, values[half:], values[:half]).astype(wire)
        arrived = lax.ppermute(send, axis_name, _exchange_pairs(count, distance))
        values = keep + arrived.astype(keep.dtype)
        distance *= 2
    top = distance
    values = values.astype(wire)
    while distance < count:
        arrived = lax.ppermute(values, axis_name, _exchange_pairs(count, distance))
        values = (values.astype(jnp.float32) + arrived.astype(jnp.float32)).astype(wire)
        distance *= 2
    distance = top // 2
    while distance >= 1:
        other = lax.ppermute(values, axis_name, _exchange_pairs(count, distance))
        lower = (position // distance) % 2 == 0
        values = jnp.where(
            lower, jnp.concatenate([values, other], 0), jnp.concatenate([other, values], 0)
        )
        distance //= 2
    return values


def local(
    encoder_input,
    desired_responses,
    sample_index,
    encoder_weight,
    decoder_weight,
    frequency_amplitude,
    spectral_filter_weight,
    output_weight,
):
    samples = sample_index.shape[0]
    sub_dev = desired_responses.shape[1]
    width = desired_responses.shape[2]
    forward_transform, inverse_transform = rotation_tables(width // 2)
    loss_scale = 1.0 / math.sqrt(samples * sub_dev * lax.axis_size("freq"))
    all_inputs = gather_rows(encoder_input, "freq")
    gathered_index = bit_reversed_blocks(sample_index, lax.axis_size("freq"))
    selection = (
        gathered_index[None, :] == jnp.arange(samples, dtype=jnp.int32)[:, None]
    ).astype(jnp.bfloat16)
    inputs_by_sample = jnp.dot(selection, all_inputs, preferred_element_type=jnp.float32).astype(
        jnp.bfloat16
    )
    codes_by_sample = jnp.tanh(
        jnp.dot(inputs_by_sample, encoder_weight, preferred_element_type=jnp.float32)
    ).astype(jnp.bfloat16)
    latent = jnp.dot(codes_by_sample, decoder_weight, preferred_element_type=jnp.float32)
    gain_row_values = frequency_amplitude.astype(jnp.float32)
    mixed_in = (latent[:, None, :] * gain_row_values[None]).astype(jnp.bfloat16).reshape(-1, width)
    wanted_lines = desired_responses.reshape(-1, width)
    derivative_entering, grad_out, grad_filter = decode_rows(
        mixed_in,
        wanted_lines,
        output_weight,
        spectral_filter_weight,
        forward_transform,
        inverse_transform,
        loss_scale,
    )
    derivative_bottleneck = jnp.einsum(
        "orm,rm->om", derivative_entering.reshape(samples, sub_dev, width), gain_row_values
    )
    half_width = grad_filter.shape[1]
    filter_rows = jnp.concatenate(
        [grad_filter, jnp.zeros((grad_filter.shape[0], width - half_width), jnp.float32)], 1
    )
    rows_out = grad_out.shape[0]
    small_rows = samples + filter_rows.shape[0]
    packed_rows = rows_out + small_rows
    padding = -packed_rows % 8
    packed = jnp.concatenate(
        [
            derivative_bottleneck,
            filter_rows,
            grad_out,
            jnp.zeros((padding, width), jnp.float32),
        ],
        0,
    )
    rows_each = packed.shape[0] // 2
    first = sum_halving(packed[:rows_each], "freq")
    second = sum_halving(packed[rows_each:], "freq")
    derivative_bottleneck = first[:samples].astype(jnp.float32)
    grad_filter = first[samples:small_rows, :half_width].astype(jnp.float32)
    grad_out = jnp.concatenate([first[small_rows:], second], 0)[:rows_out].astype(jnp.float32)
    grad_enc, grad_dec = encoder_grads(
        inputs_by_sample, codes_by_sample, derivative_bottleneck, decoder_weight
    )
    return (grad_enc, grad_dec, grad_out, grad_filter)


def solution(mesh):
    return jax.shard_map(
        local,
        mesh=mesh,
        in_specs=(
            P(("groups", "freq"), None),
            P("groups", "freq", None),
            P("groups"),
            P(),
            P(),
            P("freq", None),
            P(),
            P(),
        ),
        out_specs=(P("groups", None), P("groups", None), P("groups", None), P("groups", None)),
        check_vma=False,
    )
```

```python
import math

import jax
import ml_dtypes
import numpy as np
import jax.numpy as jnp
from jax import lax
from jax.sharding import PartitionSpec as P


def rotation_tables(antennas):
    indices = np.arange(antennas, dtype=np.int32)
    products_mod = indices[:, None] * indices[None, :] % antennas
    angle_table = products_mod.astype(np.float32) * np.float32(2.0 * math.pi / antennas)
    cosine_table = np.cos(angle_table) / np.float32(math.sqrt(antennas))
    sine_table = np.sin(angle_table) / np.float32(math.sqrt(antennas))
    forward_transform = np.concatenate(
        [
            np.concatenate([cosine_table, -sine_table], 1),
            np.concatenate([sine_table, cosine_table], 1),
        ],
        0,
    )
    inverse_transform = np.concatenate(
        [
            np.concatenate([cosine_table, sine_table], 1),
            np.concatenate([-sine_table, cosine_table], 1),
        ],
        0,
    )
    return (
        jnp.asarray(forward_transform.astype(ml_dtypes.bfloat16)),
        jnp.asarray(inverse_transform.astype(ml_dtypes.bfloat16)),
    )


def decode_rows(
    mixed_in,
    wanted_lines,
    output_weight,
    spectral_filter_weight,
    forward_transform,
    inverse_transform,
    loss_scale,
):
    filter_re = spectral_filter_weight[0]
    filter_im = spectral_filter_weight[1]
    spectrum = jnp.dot(mixed_in, forward_transform, preferred_element_type=jnp.float32)
    half_width = spectrum.shape[1] // 2
    spec_re = spectrum[:, :half_width]
    spec_im = spectrum[:, half_width:]
    filtered = jnp.concatenate(
        [spec_re * filter_re - spec_im * filter_im, spec_re * filter_im + spec_im * filter_re], 1
    ).astype(jnp.bfloat16)
    mixed_back = lax.dot_general(
        filtered, forward_transform, (((1,), (1,)), ((), ())), preferred_element_type=jnp.float32
    )
    hidden = (mixed_in.astype(jnp.float32) + jax.nn.gelu(mixed_back)).astype(jnp.bfloat16)
    rebuilt = hidden.astype(jnp.float32) + jnp.dot(
        hidden, output_weight, preferred_element_type=jnp.float32
    )
    residual = loss_scale * (rebuilt - wanted_lines.astype(jnp.float32))
    residual_half = residual.astype(jnp.bfloat16)
    grad_out = lax.dot_general(
        hidden, residual_half, (((0,), (0,)), ((), ())), preferred_element_type=jnp.float32
    )
    grad_hidden = residual + lax.dot_general(
        residual_half, output_weight, (((1,), (1,)), ((), ())), preferred_element_type=jnp.float32
    )
    grad_mixed = jax.vjp(jax.nn.gelu, mixed_back)[1](grad_hidden)[0].astype(jnp.bfloat16)
    grad_filtered = jnp.dot(grad_mixed, forward_transform, preferred_element_type=jnp.float32)
    grad_re = grad_filtered[:, :half_width]
    grad_im = grad_filtered[:, half_width:]
    grad_filter = jnp.stack(
        [
            jnp.sum(grad_re * spec_re + grad_im * spec_im, 0),
            jnp.sum(grad_im * spec_re - grad_re * spec_im, 0),
        ]
    )
    grad_spec = jnp.concatenate(
        [grad_re * filter_re + grad_im * filter_im, grad_im * filter_re - grad_re * filter_im], 1
    ).astype(jnp.bfloat16)
    derivative_entering = grad_hidden + lax.dot_general(
        grad_spec, forward_transform, (((1,), (1,)), ((), ())), preferred_element_type=jnp.float32
    )
    return (derivative_entering, grad_out, grad_filter)


def encoder_grads(inputs_rows, codewords, latent_sums, decoder_weight):
    latent_half = latent_sums.astype(jnp.bfloat16)
    grad_dec = lax.dot_general(
        codewords, latent_half, (((0,), (0,)), ((), ())), preferred_element_type=jnp.float32
    )
    grad_codes = lax.dot_general(
        latent_half, decoder_weight, (((1,), (1,)), ((), ())), preferred_element_type=jnp.float32
    )
    grad_pre = (grad_codes * (1.0 - jnp.square(codewords.astype(jnp.float32)))).astype(jnp.bfloat16)
    grad_enc = lax.dot_general(
        inputs_rows, grad_pre, (((0,), (0,)), ((), ())), preferred_element_type=jnp.float32
    )
    return (grad_enc, grad_dec)


def _exchange_pairs(count, distance):
    return [(i, i ^ distance) for i in range(count)]


def _is_power_of_two(count):
    return count > 0 and count & (count - 1) == 0


def gather_rows(block, axis_name):
    count = lax.axis_size(axis_name)
    if not _is_power_of_two(count):
        return lax.all_gather(block, axis_name, axis=0, tiled=True)
    position = lax.axis_index(axis_name)
    distance = count // 2
    while distance >= 1:
        other = lax.ppermute(block, axis_name, _exchange_pairs(count, distance))
        lower = (position // distance) % 2 == 0
        block = jnp.where(
            lower, jnp.concatenate([block, other], 0), jnp.concatenate([other, block], 0)
        )
        distance //= 2
    return block


def bit_reversed_blocks(values, count):
    if not _is_power_of_two(count):
        return values
    bits = count.bit_length() - 1
    blocks = values.reshape((2,) * bits + (-1,))
    return blocks.transpose(tuple(reversed(range(bits))) + (bits,)).reshape(-1)


def sum_whole(values, axis_name):
    count = lax.axis_size(axis_name)
    if not _is_power_of_two(count):
        return lax.psum(values, axis_name)
    distance = 1
    while distance < count:
        values = values + lax.ppermute(values, axis_name, _exchange_pairs(count, distance))
        distance *= 2
    return values


def sum_halving(values, axis_name, wire=jnp.bfloat16, halving_levels=2):
    count = lax.axis_size(axis_name)
    if not _is_power_of_two(count) or values.shape[0] % min(count, 2**halving_levels) != 0:
        return lax.psum(values, axis_name)
    position = lax.axis_index(axis_name)
    distance = 1
    while distance < count and distance < 2**halving_levels:
        half = values.shape[0] // 2
        lower = (position // distance) % 2 == 0
        keep = jnp.where(lower, values[:half], values[half:])
        send = jnp.where(lower, values[half:], values[:half]).astype(wire)
        arrived = lax.ppermute(send, axis_name, _exchange_pairs(count, distance))
        values = keep + arrived.astype(keep.dtype)
        distance *= 2
    top = distance
    values = values.astype(wire)
    while distance < count:
        arrived = lax.ppermute(values, axis_name, _exchange_pairs(count, distance))
        values = (values.astype(jnp.float32) + arrived.astype(jnp.float32)).astype(wire)
        distance *= 2
    distance = top // 2
    while distance >= 1:
        other = lax.ppermute(values, axis_name, _exchange_pairs(count, distance))
        lower = (position // distance) % 2 == 0
        values = jnp.where(
            lower, jnp.concatenate([values, other], 0), jnp.concatenate([other, values], 0)
        )
        distance //= 2
    return values


def local(
    encoder_input,
    desired_responses,
    sample_index,
    encoder_weight,
    decoder_weight,
    frequency_amplitude,
    spectral_filter_weight,
    output_weight,
):
    samples = sample_index.shape[0]
    sub_dev = desired_responses.shape[1]
    width = desired_responses.shape[2]
    forward_transform, inverse_transform = rotation_tables(width // 2)
    loss_scale = 1.0 / math.sqrt(samples * sub_dev * lax.axis_size("freq"))
    all_inputs = gather_rows(encoder_input, "freq")
    gathered_index = bit_reversed_blocks(sample_index, lax.axis_size("freq"))
    selection = (
        gathered_index[None, :] == jnp.arange(samples, dtype=jnp.int32)[:, None]
    ).astype(jnp.bfloat16)
    inputs_by_sample = jnp.dot(selection, all_inputs, preferred_element_type=jnp.float32).astype(
        jnp.bfloat16
    )
    codes_by_sample = jnp.tanh(
        jnp.dot(inputs_by_sample, encoder_weight, preferred_element_type=jnp.float32)
    ).astype(jnp.bfloat16)
    latent = jnp.dot(codes_by_sample, decoder_weight, preferred_element_type=jnp.float32)
    gain_row_values = frequency_amplitude.astype(jnp.float32)
    mixed_in = (latent[:, None, :] * gain_row_values[None]).astype(jnp.bfloat16).reshape(-1, width)
    wanted_lines = desired_responses.reshape(-1, width)
    derivative_entering, grad_out, grad_filter = decode_rows(
        mixed_in,
        wanted_lines,
        output_weight,
        spectral_filter_weight,
        forward_transform,
        inverse_transform,
        loss_scale,
    )
    derivative_bottleneck = jnp.einsum(
        "orm,rm->om", derivative_entering.reshape(samples, sub_dev, width), gain_row_values
    )
    half_width = grad_filter.shape[1]
    filter_rows = jnp.concatenate(
        [grad_filter, jnp.zeros((grad_filter.shape[0], width - half_width), jnp.float32)], 1
    )
    small = sum_whole(jnp.concatenate([derivative_bottleneck, filter_rows], 0), "freq")
    grad_out = sum_halving(grad_out, "freq").astype(jnp.float32)
    derivative_bottleneck = small[:samples]
    grad_filter = small[samples:, :half_width]
    grad_enc, grad_dec = encoder_grads(
        inputs_by_sample, codes_by_sample, derivative_bottleneck, decoder_weight
    )
    return (grad_enc, grad_dec, grad_out, grad_filter)


def solution(mesh):
    return jax.shard_map(
        local,
        mesh=mesh,
        in_specs=(
            P(("groups", "freq"), None),
            P("groups", "freq", None),
            P("groups"),
            P(),
            P(),
            P("freq", None),
            P(),
            P(),
        ),
        out_specs=(P("groups", None), P("groups", None), P("groups", None), P("groups", None)),
        check_vma=False,
    )
```

```python
import math

import jax
import ml_dtypes
import numpy as np
import jax.numpy as jnp
from jax import lax
from jax.sharding import PartitionSpec as P


def rotation_tables(antennas):
    indices = np.arange(antennas, dtype=np.int32)
    products_mod = indices[:, None] * indices[None, :] % antennas
    angle_table = products_mod.astype(np.float32) * np.float32(2.0 * math.pi / antennas)
    cosine_table = np.cos(angle_table) / np.float32(math.sqrt(antennas))
    sine_table = np.sin(angle_table) / np.float32(math.sqrt(antennas))
    forward_transform = np.concatenate(
        [
            np.concatenate([cosine_table, -sine_table], 1),
            np.concatenate([sine_table, cosine_table], 1),
        ],
        0,
    )
    inverse_transform = np.concatenate(
        [
            np.concatenate([cosine_table, sine_table], 1),
            np.concatenate([-sine_table, cosine_table], 1),
        ],
        0,
    )
    return (
        jnp.asarray(forward_transform.astype(ml_dtypes.bfloat16)),
        jnp.asarray(inverse_transform.astype(ml_dtypes.bfloat16)),
    )


def decode_rows(
    mixed_in,
    wanted_lines,
    output_weight,
    spectral_filter_weight,
    forward_transform,
    inverse_transform,
    loss_scale,
):
    filter_re = spectral_filter_weight[0]
    filter_im = spectral_filter_weight[1]
    spectrum = jnp.dot(mixed_in, forward_transform, preferred_element_type=jnp.float32)
    half_width = spectrum.shape[1] // 2
    spec_re = spectrum[:, :half_width]
    spec_im = spectrum[:, half_width:]
    filtered = jnp.concatenate(
        [spec_re * filter_re - spec_im * filter_im, spec_re * filter_im + spec_im * filter_re], 1
    ).astype(jnp.bfloat16)
    mixed_back = lax.dot_general(
        filtered, forward_transform, (((1,), (1,)), ((), ())), preferred_element_type=jnp.float32
    )
    hidden = (mixed_in.astype(jnp.float32) + jax.nn.gelu(mixed_back)).astype(jnp.bfloat16)
    rebuilt = hidden.astype(jnp.float32) + jnp.dot(
        hidden, output_weight, preferred_element_type=jnp.float32
    )
    residual = loss_scale * (rebuilt - wanted_lines.astype(jnp.float32))
    residual_half = residual.astype(jnp.bfloat16)
    grad_out = lax.dot_general(
        hidden, residual_half, (((0,), (0,)), ((), ())), preferred_element_type=jnp.float32
    )
    grad_hidden = residual + lax.dot_general(
        residual_half, output_weight, (((1,), (1,)), ((), ())), preferred_element_type=jnp.float32
    )
    grad_mixed = jax.vjp(jax.nn.gelu, mixed_back)[1](grad_hidden)[0].astype(jnp.bfloat16)
    grad_filtered = jnp.dot(grad_mixed, forward_transform, preferred_element_type=jnp.float32)
    grad_re = grad_filtered[:, :half_width]
    grad_im = grad_filtered[:, half_width:]
    grad_filter = jnp.stack(
        [
            jnp.sum(grad_re * spec_re + grad_im * spec_im, 0),
            jnp.sum(grad_im * spec_re - grad_re * spec_im, 0),
        ]
    )
    grad_spec = jnp.concatenate(
        [grad_re * filter_re + grad_im * filter_im, grad_im * filter_re - grad_re * filter_im], 1
    ).astype(jnp.bfloat16)
    derivative_entering = grad_hidden + lax.dot_general(
        grad_spec, forward_transform, (((1,), (1,)), ((), ())), preferred_element_type=jnp.float32
    )
    return (derivative_entering, grad_out, grad_filter)


def encoder_grads(inputs_rows, codewords, latent_sums, decoder_weight):
    latent_half = latent_sums.astype(jnp.bfloat16)
    grad_dec = lax.dot_general(
        codewords, latent_half, (((0,), (0,)), ((), ())), preferred_element_type=jnp.float32
    )
    grad_codes = lax.dot_general(
        latent_half, decoder_weight, (((1,), (1,)), ((), ())), preferred_element_type=jnp.float32
    )
    grad_pre = (grad_codes * (1.0 - jnp.square(codewords.astype(jnp.float32)))).astype(jnp.bfloat16)
    grad_enc = lax.dot_general(
        inputs_rows, grad_pre, (((0,), (0,)), ((), ())), preferred_element_type=jnp.float32
    )
    return (grad_enc, grad_dec)


def _exchange_pairs(count, distance):
    return [(i, i ^ distance) for i in range(count)]


def _is_power_of_two(count):
    return count > 0 and count & (count - 1) == 0


def gather_rows(block, axis_name):
    count = lax.axis_size(axis_name)
    if not _is_power_of_two(count):
        return lax.all_gather(block, axis_name, axis=0, tiled=True)
    position = lax.axis_index(axis_name)
    distance = count // 2
    while distance >= 1:
        other = lax.ppermute(block, axis_name, _exchange_pairs(count, distance))
        lower = (position // distance) % 2 == 0
        block = jnp.where(
            lower, jnp.concatenate([block, other], 0), jnp.concatenate([other, block], 0)
        )
        distance //= 2
    return block


def bit_reversed_blocks(values, count):
    if not _is_power_of_two(count):
        return values
    bits = count.bit_length() - 1
    blocks = values.reshape((2,) * bits + (-1,))
    return blocks.transpose(tuple(reversed(range(bits))) + (bits,)).reshape(-1)


def sum_whole(values, axis_name):
    count = lax.axis_size(axis_name)
    if not _is_power_of_two(count):
        return lax.psum(values, axis_name)
    distance = 1
    while distance < count:
        values = values + lax.ppermute(values, axis_name, _exchange_pairs(count, distance))
        distance *= 2
    return values


def sum_halving(values, axis_name, wire=jnp.bfloat16, halving_levels=2):
    count = lax.axis_size(axis_name)
    if not _is_power_of_two(count) or values.shape[0] % min(count, 2**halving_levels) != 0:
        return lax.psum(values, axis_name)
    position = lax.axis_index(axis_name)
    distance = 1
    while distance < count and distance < 2**halving_levels:
        half = values.shape[0] // 2
        lower = (position // distance) % 2 == 0
        keep = jnp.where(lower, values[:half], values[half:])
        send = jnp.where(lower, values[half:], values[:half]).astype(wire)
        arrived = lax.ppermute(send, axis_name, _exchange_pairs(count, distance))
        values = keep + arrived.astype(keep.dtype)
        distance *= 2
    top = distance
    values = values.astype(wire)
    while distance < count:
        arrived = lax.ppermute(values, axis_name, _exchange_pairs(count, distance))
        values = (values.astype(jnp.float32) + arrived.astype(jnp.float32)).astype(wire)
        distance *= 2
    distance = top // 2
    while distance >= 1:
        other = lax.ppermute(values, axis_name, _exchange_pairs(count, distance))
        lower = (position // distance) % 2 == 0
        values = jnp.where(
            lower, jnp.concatenate([values, other], 0), jnp.concatenate([other, values], 0)
        )
        distance //= 2
    return values


def local(
    encoder_input,
    desired_responses,
    sample_index,
    encoder_weight,
    decoder_weight,
    frequency_amplitude,
    spectral_filter_weight,
    output_weight,
):
    samples = sample_index.shape[0]
    sub_dev = desired_responses.shape[1]
    width = desired_responses.shape[2]
    forward_transform, inverse_transform = rotation_tables(width // 2)
    loss_scale = 1.0 / math.sqrt(samples * sub_dev * lax.axis_size("freq"))
    all_inputs = gather_rows(encoder_input, "freq")
    gathered_index = bit_reversed_blocks(sample_index, lax.axis_size("freq"))
    selection = (
        gathered_index[None, :] == jnp.arange(samples, dtype=jnp.int32)[:, None]
    ).astype(jnp.bfloat16)
    inputs_by_sample = jnp.dot(selection, all_inputs, preferred_element_type=jnp.float32).astype(
        jnp.bfloat16
    )
    codes_by_sample = jnp.tanh(
        jnp.dot(inputs_by_sample, encoder_weight, preferred_element_type=jnp.float32)
    ).astype(jnp.bfloat16)
    latent = jnp.dot(codes_by_sample, decoder_weight, preferred_element_type=jnp.float32)
    gain_row_values = frequency_amplitude.astype(jnp.float32)
    mixed_in = (latent[:, None, :] * gain_row_values[None]).astype(jnp.bfloat16).reshape(-1, width)
    wanted_lines = desired_responses.reshape(-1, width)
    derivative_entering, grad_out, grad_filter = decode_rows(
        mixed_in,
        wanted_lines,
        output_weight,
        spectral_filter_weight,
        forward_transform,
        inverse_transform,
        loss_scale,
    )
    derivative_bottleneck = jnp.einsum(
        "orm,rm->om", derivative_entering.reshape(samples, sub_dev, width), gain_row_values
    )
    count = lax.axis_size("freq")
    half_width = grad_filter.shape[1]
    filter_rows = jnp.concatenate(
        [grad_filter, jnp.zeros((grad_filter.shape[0], width - half_width), jnp.float32)], 1
    )
    packed_rows = grad_out.shape[0] + samples + filter_rows.shape[0]
    padding = -packed_rows % 8
    packed = jnp.concatenate(
        [
            grad_out,
            derivative_bottleneck,
            filter_rows,
            jnp.zeros((padding, width), jnp.float32),
        ],
        0,
    )
    columns = packed.shape[1] // 2
    packed = jnp.concatenate(
        [sum_halving(packed[:, :columns], "freq"), sum_halving(packed[:, columns:], "freq")], 1
    )
    rows_out = grad_out.shape[0]
    grad_out = packed[:rows_out].astype(jnp.float32)
    derivative_bottleneck = packed[rows_out : rows_out + samples].astype(jnp.float32)
    grad_filter = packed[
        rows_out + samples : rows_out + samples + filter_rows.shape[0], :half_width
    ].astype(jnp.float32)
    grad_enc, grad_dec = encoder_grads(
        inputs_by_sample, codes_by_sample, derivative_bottleneck, decoder_weight
    )
    return (grad_enc, grad_dec, grad_out, grad_filter)


def solution(mesh):
    return jax.shard_map(
        local,
        mesh=mesh,
        in_specs=(
            P(("groups", "freq"), None),
            P("groups", "freq", None),
            P("groups"),
            P(),
            P(),
            P("freq", None),
            P(),
            P(),
        ),
        out_specs=(P("groups", None), P("groups", None), P("groups", None), P("groups", None)),
        check_vma=False,
    )
```

```python
import math

import jax
import ml_dtypes
import numpy as np
import jax.numpy as jnp
from jax import lax
from jax.sharding import PartitionSpec as P


def rotation_tables(antennas):
    indices = np.arange(antennas, dtype=np.int32)
    products_mod = indices[:, None] * indices[None, :] % antennas
    angle_table = products_mod.astype(np.float32) * np.float32(2.0 * math.pi / antennas)
    cosine_table = np.cos(angle_table) / np.float32(math.sqrt(antennas))
    sine_table = np.sin(angle_table) / np.float32(math.sqrt(antennas))
    forward_transform = np.concatenate(
        [
            np.concatenate([cosine_table, -sine_table], 1),
            np.concatenate([sine_table, cosine_table], 1),
        ],
        0,
    )
    inverse_transform = np.concatenate(
        [
            np.concatenate([cosine_table, sine_table], 1),
            np.concatenate([-sine_table, cosine_table], 1),
        ],
        0,
    )
    return (
        jnp.asarray(forward_transform.astype(ml_dtypes.bfloat16)),
        jnp.asarray(inverse_transform.astype(ml_dtypes.bfloat16)),
    )


def decode_rows(
    mixed_in,
    wanted_lines,
    output_weight,
    spectral_filter_weight,
    forward_transform,
    inverse_transform,
    loss_scale,
):
    filter_re = spectral_filter_weight[0]
    filter_im = spectral_filter_weight[1]
    spectrum = jnp.dot(mixed_in, forward_transform, preferred_element_type=jnp.float32)
    half_width = spectrum.shape[1] // 2
    spec_re = spectrum[:, :half_width]
    spec_im = spectrum[:, half_width:]
    filtered = jnp.concatenate(
        [spec_re * filter_re - spec_im * filter_im, spec_re * filter_im + spec_im * filter_re], 1
    ).astype(jnp.bfloat16)
    mixed_back = lax.dot_general(
        filtered, forward_transform, (((1,), (1,)), ((), ())), preferred_element_type=jnp.float32
    )
    hidden = (mixed_in.astype(jnp.float32) + jax.nn.gelu(mixed_back)).astype(jnp.bfloat16)
    rebuilt = hidden.astype(jnp.float32) + jnp.dot(
        hidden, output_weight, preferred_element_type=jnp.float32
    )
    residual = loss_scale * (rebuilt - wanted_lines.astype(jnp.float32))
    residual_half = residual.astype(jnp.bfloat16)
    grad_out = lax.dot_general(
        hidden, residual_half, (((0,), (0,)), ((), ())), preferred_element_type=jnp.float32
    )
    grad_hidden = residual + lax.dot_general(
        residual_half, output_weight, (((1,), (1,)), ((), ())), preferred_element_type=jnp.float32
    )
    grad_mixed = jax.vjp(jax.nn.gelu, mixed_back)[1](grad_hidden)[0].astype(jnp.bfloat16)
    grad_filtered = jnp.dot(grad_mixed, forward_transform, preferred_element_type=jnp.float32)
    grad_re = grad_filtered[:, :half_width]
    grad_im = grad_filtered[:, half_width:]
    grad_filter = jnp.stack(
        [
            jnp.sum(grad_re * spec_re + grad_im * spec_im, 0),
            jnp.sum(grad_im * spec_re - grad_re * spec_im, 0),
        ]
    )
    grad_spec = jnp.concatenate(
        [grad_re * filter_re + grad_im * filter_im, grad_im * filter_re - grad_re * filter_im], 1
    ).astype(jnp.bfloat16)
    derivative_entering = grad_hidden + lax.dot_general(
        grad_spec, forward_transform, (((1,), (1,)), ((), ())), preferred_element_type=jnp.float32
    )
    return (derivative_entering, grad_out, grad_filter)


def encoder_grads(inputs_rows, codewords, latent_sums, decoder_weight):
    latent_half = latent_sums.astype(jnp.bfloat16)
    grad_dec = lax.dot_general(
        codewords, latent_half, (((0,), (0,)), ((), ())), preferred_element_type=jnp.float32
    )
    grad_codes = lax.dot_general(
        latent_half, decoder_weight, (((1,), (1,)), ((), ())), preferred_element_type=jnp.float32
    )
    grad_pre = (grad_codes * (1.0 - jnp.square(codewords.astype(jnp.float32)))).astype(jnp.bfloat16)
    grad_enc = lax.dot_general(
        inputs_rows, grad_pre, (((0,), (0,)), ((), ())), preferred_element_type=jnp.float32
    )
    return (grad_enc, grad_dec)


def _exchange_pairs(count, distance):
    return [(i, i ^ distance) for i in range(count)]


def _is_power_of_two(count):
    return count > 0 and count & (count - 1) == 0


def gather_rows(block, axis_name):
    count = lax.axis_size(axis_name)
    if not _is_power_of_two(count):
        return lax.all_gather(block, axis_name, axis=0, tiled=True)
    position = lax.axis_index(axis_name)
    distance = count // 2
    while distance >= 1:
        other = lax.ppermute(block, axis_name, _exchange_pairs(count, distance))
        lower = (position // distance) % 2 == 0
        block = jnp.where(
            lower, jnp.concatenate([block, other], 0), jnp.concatenate([other, block], 0)
        )
        distance //= 2
    return block


def bit_reversed_blocks(values, count):
    if not _is_power_of_two(count):
        return values
    bits = count.bit_length() - 1
    blocks = values.reshape((2,) * bits + (-1,))
    return blocks.transpose(tuple(reversed(range(bits))) + (bits,)).reshape(-1)


def sum_whole(values, axis_name):
    count = lax.axis_size(axis_name)
    if not _is_power_of_two(count):
        return lax.psum(values, axis_name)
    distance = 1
    while distance < count:
        values = values + lax.ppermute(values, axis_name, _exchange_pairs(count, distance))
        distance *= 2
    return values


def sum_halving(values, axis_name, wire=jnp.bfloat16, halving_levels=2, trailing=None):
    count = lax.axis_size(axis_name)
    if not _is_power_of_two(count) or values.shape[0] % min(count, 2**halving_levels) != 0:
        if trailing is not None:
            return lax.psum(values, axis_name), trailing
        return lax.psum(values, axis_name)
    position = lax.axis_index(axis_name)
    distance = 1
    while distance < count and distance < 2**halving_levels:
        half = values.shape[0] // 2
        lower = (position // distance) % 2 == 0
        keep = jnp.where(lower, values[:half], values[half:])
        send = jnp.where(lower, values[half:], values[:half]).astype(wire)
        arrived = lax.ppermute(send, axis_name, _exchange_pairs(count, distance))
        values = keep + arrived.astype(keep.dtype)
        if distance == 1 and trailing is not None:
            values, trailing = lax.optimization_barrier((values, trailing))
        distance *= 2
    top = distance
    values = values.astype(wire)
    while distance < count:
        arrived = lax.ppermute(values, axis_name, _exchange_pairs(count, distance))
        values = (values.astype(jnp.float32) + arrived.astype(jnp.float32)).astype(wire)
        distance *= 2
    distance = top // 2
    while distance >= 1:
        other = lax.ppermute(values, axis_name, _exchange_pairs(count, distance))
        lower = (position // distance) % 2 == 0
        values = jnp.where(
            lower, jnp.concatenate([values, other], 0), jnp.concatenate([other, values], 0)
        )
        distance //= 2
    if trailing is not None:
        return values, trailing
    return values


def local(
    encoder_input,
    desired_responses,
    sample_index,
    encoder_weight,
    decoder_weight,
    frequency_amplitude,
    spectral_filter_weight,
    output_weight,
):
    samples = sample_index.shape[0]
    sub_dev = desired_responses.shape[1]
    width = desired_responses.shape[2]
    forward_transform, inverse_transform = rotation_tables(width // 2)
    loss_scale = 1.0 / math.sqrt(samples * sub_dev * lax.axis_size("freq"))
    all_inputs = gather_rows(encoder_input, "freq")
    gathered_index = bit_reversed_blocks(sample_index, lax.axis_size("freq"))
    selection = (
        gathered_index[None, :] == jnp.arange(samples, dtype=jnp.int32)[:, None]
    ).astype(jnp.bfloat16)
    inputs_by_sample = jnp.dot(selection, all_inputs, preferred_element_type=jnp.float32).astype(
        jnp.bfloat16
    )
    codes_by_sample = jnp.tanh(
        jnp.dot(inputs_by_sample, encoder_weight, preferred_element_type=jnp.float32)
    ).astype(jnp.bfloat16)
    latent = jnp.dot(codes_by_sample, decoder_weight, preferred_element_type=jnp.float32)
    gain_row_values = frequency_amplitude.astype(jnp.float32)
    mixed_in = (latent[:, None, :] * gain_row_values[None]).astype(jnp.bfloat16).reshape(-1, width)
    wanted_lines = desired_responses.reshape(-1, width)
    derivative_entering, grad_out, grad_filter = decode_rows(
        mixed_in,
        wanted_lines,
        output_weight,
        spectral_filter_weight,
        forward_transform,
        inverse_transform,
        loss_scale,
    )
    derivative_bottleneck = jnp.einsum(
        "orm,rm->om", derivative_entering.reshape(samples, sub_dev, width), gain_row_values
    )
    half_width = grad_filter.shape[1]
    filter_rows = jnp.concatenate(
        [grad_filter, jnp.zeros((grad_filter.shape[0], width - half_width), jnp.float32)], 1
    )
    rows_out = grad_out.shape[0]
    small_rows = samples + filter_rows.shape[0]
    packed_rows = rows_out + small_rows
    padding = -packed_rows % 8
    packed = jnp.concatenate(
        [
            derivative_bottleneck,
            filter_rows,
            grad_out,
            jnp.zeros((padding, width), jnp.float32),
        ],
        0,
    )
    rows_each = packed.shape[0] // 2
    first, second_input = sum_halving(packed[:rows_each], "freq", trailing=packed[rows_each:])
    second = sum_halving(second_input, "freq")
    derivative_bottleneck = first[:samples].astype(jnp.float32)
    grad_filter = first[samples:small_rows, :half_width].astype(jnp.float32)
    grad_out = jnp.concatenate([first[small_rows:], second], 0)[:rows_out].astype(jnp.float32)
    grad_enc, grad_dec = encoder_grads(
        inputs_by_sample, codes_by_sample, derivative_bottleneck, decoder_weight
    )
    return (grad_enc, grad_dec, grad_out, grad_filter)


def solution(mesh):
    return jax.shard_map(
        local,
        mesh=mesh,
        in_specs=(
            P(("groups", "freq"), None),
            P("groups", "freq", None),
            P("groups"),
            P(),
            P(),
            P("freq", None),
            P(),
            P(),
        ),
        out_specs=(P("groups", None), P("groups", None), P("groups", None), P("groups", None)),
        check_vma=False,
    )
```

```python
import math

import jax
import ml_dtypes
import numpy as np
import jax.numpy as jnp
from jax import lax
from jax.sharding import PartitionSpec as P


def rotation_tables(antennas):
    indices = np.arange(antennas, dtype=np.int32)
    products_mod = indices[:, None] * indices[None, :] % antennas
    angle_table = products_mod.astype(np.float32) * np.float32(2.0 * math.pi / antennas)
    cosine_table = np.cos(angle_table) / np.float32(math.sqrt(antennas))
    sine_table = np.sin(angle_table) / np.float32(math.sqrt(antennas))
    forward_transform = np.concatenate(
        [
            np.concatenate([cosine_table, -sine_table], 1),
            np.concatenate([sine_table, cosine_table], 1),
        ],
        0,
    )
    inverse_transform = np.concatenate(
        [
            np.concatenate([cosine_table, sine_table], 1),
            np.concatenate([-sine_table, cosine_table], 1),
        ],
        0,
    )
    return (
        jnp.asarray(forward_transform.astype(ml_dtypes.bfloat16)),
        jnp.asarray(inverse_transform.astype(ml_dtypes.bfloat16)),
    )


def decode_rows(
    mixed_in,
    wanted_lines,
    output_weight,
    spectral_filter_weight,
    forward_transform,
    inverse_transform,
    loss_scale,
):
    filter_re = spectral_filter_weight[0]
    filter_im = spectral_filter_weight[1]
    spectrum = jnp.dot(mixed_in, forward_transform, preferred_element_type=jnp.float32)
    half_width = spectrum.shape[1] // 2
    spec_re = spectrum[:, :half_width]
    spec_im = spectrum[:, half_width:]
    filtered = jnp.concatenate(
        [spec_re * filter_re - spec_im * filter_im, spec_re * filter_im + spec_im * filter_re], 1
    ).astype(jnp.bfloat16)
    mixed_back = lax.dot_general(
        filtered, forward_transform, (((1,), (1,)), ((), ())), preferred_element_type=jnp.float32
    )
    hidden = (mixed_in.astype(jnp.float32) + jax.nn.gelu(mixed_back)).astype(jnp.bfloat16)
    rebuilt = hidden.astype(jnp.float32) + jnp.dot(
        hidden, output_weight, preferred_element_type=jnp.float32
    )
    residual = loss_scale * (rebuilt - wanted_lines.astype(jnp.float32))
    residual_half = residual.astype(jnp.bfloat16)
    grad_out = lax.dot_general(
        hidden, residual_half, (((0,), (0,)), ((), ())), preferred_element_type=jnp.float32
    )
    grad_hidden = residual + lax.dot_general(
        residual_half, output_weight, (((1,), (1,)), ((), ())), preferred_element_type=jnp.float32
    )
    grad_mixed = jax.vjp(jax.nn.gelu, mixed_back)[1](grad_hidden)[0].astype(jnp.bfloat16)
    grad_filtered = jnp.dot(grad_mixed, forward_transform, preferred_element_type=jnp.float32)
    grad_re = grad_filtered[:, :half_width]
    grad_im = grad_filtered[:, half_width:]
    grad_filter = jnp.stack(
        [
            jnp.sum(grad_re * spec_re + grad_im * spec_im, 0),
            jnp.sum(grad_im * spec_re - grad_re * spec_im, 0),
        ]
    )
    grad_spec = jnp.concatenate(
        [grad_re * filter_re + grad_im * filter_im, grad_im * filter_re - grad_re * filter_im], 1
    ).astype(jnp.bfloat16)
    derivative_entering = grad_hidden + lax.dot_general(
        grad_spec, forward_transform, (((1,), (1,)), ((), ())), preferred_element_type=jnp.float32
    )
    return (derivative_entering, grad_out, grad_filter)


def encoder_grads(inputs_rows, codewords, latent_sums, decoder_weight):
    latent_half = latent_sums.astype(jnp.bfloat16)
    grad_dec = lax.dot_general(
        codewords, latent_half, (((0,), (0,)), ((), ())), preferred_element_type=jnp.float32
    )
    grad_codes = lax.dot_general(
        latent_half, decoder_weight, (((1,), (1,)), ((), ())), preferred_element_type=jnp.float32
    )
    grad_pre = (grad_codes * (1.0 - jnp.square(codewords.astype(jnp.float32)))).astype(jnp.bfloat16)
    grad_enc = lax.dot_general(
        inputs_rows, grad_pre, (((0,), (0,)), ((), ())), preferred_element_type=jnp.float32
    )
    return (grad_enc, grad_dec)


def _exchange_pairs(count, distance):
    return [(i, i ^ distance) for i in range(count)]


def _is_power_of_two(count):
    return count > 0 and count & (count - 1) == 0


def gather_rows(block, axis_name):
    count = lax.axis_size(axis_name)
    if not _is_power_of_two(count):
        return lax.all_gather(block, axis_name, axis=0, tiled=True)
    position = lax.axis_index(axis_name)
    distance = count // 2
    while distance >= 1:
        other = lax.ppermute(block, axis_name, _exchange_pairs(count, distance))
        lower = (position // distance) % 2 == 0
        block = jnp.where(
            lower, jnp.concatenate([block, other], 0), jnp.concatenate([other, block], 0)
        )
        distance //= 2
    return block


def bit_reversed_blocks(values, count):
    if not _is_power_of_two(count):
        return values
    bits = count.bit_length() - 1
    blocks = values.reshape((2,) * bits + (-1,))
    return blocks.transpose(tuple(reversed(range(bits))) + (bits,)).reshape(-1)


def sum_whole(values, axis_name):
    count = lax.axis_size(axis_name)
    if not _is_power_of_two(count):
        return lax.psum(values, axis_name)
    distance = 1
    while distance < count:
        values = values + lax.ppermute(values, axis_name, _exchange_pairs(count, distance))
        distance *= 2
    return values


def sum_halving(values, axis_name, wire=jnp.bfloat16, halving_levels=2, trailing=None):
    count = lax.axis_size(axis_name)
    if not _is_power_of_two(count) or values.shape[0] % min(count, 2**halving_levels) != 0:
        if trailing is not None:
            return lax.psum(values, axis_name), trailing
        return lax.psum(values, axis_name)
    position = lax.axis_index(axis_name)
    distance = 1
    while distance < count and distance < 2**halving_levels:
        half = values.shape[0] // 2
        lower = (position // distance) % 2 == 0
        keep = jnp.where(lower, values[:half], values[half:])
        send = jnp.where(lower, values[half:], values[:half]).astype(wire)
        arrived = lax.ppermute(send, axis_name, _exchange_pairs(count, distance))
        values = keep + arrived.astype(keep.dtype)
        if distance == 1 and trailing is not None:
            values, trailing = lax.optimization_barrier((values, trailing))
        distance *= 2
    top = distance
    values = values.astype(wire)
    while distance < count:
        arrived = lax.ppermute(values, axis_name, _exchange_pairs(count, distance))
        values = (values.astype(jnp.float32) + arrived.astype(jnp.float32)).astype(wire)
        distance *= 2
    distance = top // 2
    while distance >= 1:
        other = lax.ppermute(values, axis_name, _exchange_pairs(count, distance))
        lower = (position // distance) % 2 == 0
        values = jnp.where(
            lower, jnp.concatenate([values, other], 0), jnp.concatenate([other, values], 0)
        )
        distance //= 2
    if trailing is not None:
        return values, trailing
    return values


def local(
    encoder_input,
    desired_responses,
    sample_index,
    encoder_weight,
    decoder_weight,
    frequency_amplitude,
    spectral_filter_weight,
    output_weight,
):
    samples = sample_index.shape[0]
    sub_dev = desired_responses.shape[1]
    width = desired_responses.shape[2]
    forward_transform, inverse_transform = rotation_tables(width // 2)
    loss_scale = 1.0 / math.sqrt(samples * sub_dev * lax.axis_size("freq"))
    all_inputs = gather_rows(encoder_input, "freq")
    gathered_index = bit_reversed_blocks(sample_index, lax.axis_size("freq"))
    selection = (
        gathered_index[None, :] == jnp.arange(samples, dtype=jnp.int32)[:, None]
    ).astype(jnp.bfloat16)
    inputs_by_sample = jnp.dot(selection, all_inputs, preferred_element_type=jnp.float32).astype(
        jnp.bfloat16
    )
    codes_by_sample = jnp.tanh(
        jnp.dot(inputs_by_sample, encoder_weight, preferred_element_type=jnp.float32)
    ).astype(jnp.bfloat16)
    latent = jnp.dot(codes_by_sample, decoder_weight, preferred_element_type=jnp.float32)
    gain_row_values = frequency_amplitude.astype(jnp.float32)
    mixed_in = (latent[:, None, :] * gain_row_values[None]).astype(jnp.bfloat16).reshape(-1, width)
    wanted_lines = desired_responses.reshape(-1, width)
    derivative_entering, grad_out, grad_filter = decode_rows(
        mixed_in,
        wanted_lines,
        output_weight,
        spectral_filter_weight,
        forward_transform,
        inverse_transform,
        loss_scale,
    )
    derivative_bottleneck = jnp.einsum(
        "orm,rm->om", derivative_entering.reshape(samples, sub_dev, width), gain_row_values
    )
    half_width = grad_filter.shape[1]
    filter_rows = jnp.concatenate(
        [grad_filter, jnp.zeros((grad_filter.shape[0], width - half_width), jnp.float32)], 1
    )
    rows_out = grad_out.shape[0]
    small_rows = samples + filter_rows.shape[0]
    packed_rows = rows_out + small_rows
    padding = -packed_rows % 8
    packed = jnp.concatenate(
        [
            derivative_bottleneck,
            filter_rows,
            grad_out,
            jnp.zeros((padding, width), jnp.float32),
        ],
        0,
    )
    rows_each = packed.shape[0] // 2 + 44 if packed.shape[0] % 8 == 0 and packed.shape[0] > 200 else packed.shape[0] // 2
    first, second_input = sum_halving(packed[:rows_each], "freq", trailing=packed[rows_each:])
    second = sum_halving(second_input, "freq")
    derivative_bottleneck = first[:samples].astype(jnp.float32)
    grad_filter = first[samples:small_rows, :half_width].astype(jnp.float32)
    grad_out = jnp.concatenate([first[small_rows:], second], 0)[:rows_out].astype(jnp.float32)
    grad_enc, grad_dec = encoder_grads(
        inputs_by_sample, codes_by_sample, derivative_bottleneck, decoder_weight
    )
    return (grad_enc, grad_dec, grad_out, grad_filter)


def solution(mesh):
    return jax.shard_map(
        local,
        mesh=mesh,
        in_specs=(
            P(("groups", "freq"), None),
            P("groups", "freq", None),
            P("groups"),
            P(),
            P(),
            P("freq", None),
            P(),
            P(),
        ),
        out_specs=(P("groups", None), P("groups", None), P("groups", None), P("groups", None)),
        check_vma=False,
    )
```

```python
import math

import jax
import ml_dtypes
import numpy as np
import jax.numpy as jnp
from jax import lax
from jax.sharding import PartitionSpec as P


def rotation_tables(antennas):
    indices = np.arange(antennas, dtype=np.int32)
    products_mod = indices[:, None] * indices[None, :] % antennas
    angle_table = products_mod.astype(np.float32) * np.float32(2.0 * math.pi / antennas)
    cosine_table = np.cos(angle_table) / np.float32(math.sqrt(antennas))
    sine_table = np.sin(angle_table) / np.float32(math.sqrt(antennas))
    forward_transform = np.concatenate(
        [
            np.concatenate([cosine_table, -sine_table], 1),
            np.concatenate([sine_table, cosine_table], 1),
        ],
        0,
    )
    inverse_transform = np.concatenate(
        [
            np.concatenate([cosine_table, sine_table], 1),
            np.concatenate([-sine_table, cosine_table], 1),
        ],
        0,
    )
    return (
        jnp.asarray(forward_transform.astype(ml_dtypes.bfloat16)),
        jnp.asarray(inverse_transform.astype(ml_dtypes.bfloat16)),
    )


def decode_rows(
    mixed_in,
    wanted_lines,
    output_weight,
    spectral_filter_weight,
    forward_transform,
    inverse_transform,
    loss_scale,
):
    filter_re = spectral_filter_weight[0]
    filter_im = spectral_filter_weight[1]
    spectrum = jnp.dot(mixed_in, forward_transform, preferred_element_type=jnp.float32)
    half_width = spectrum.shape[1] // 2
    spec_re = spectrum[:, :half_width]
    spec_im = spectrum[:, half_width:]
    filtered = jnp.concatenate(
        [spec_re * filter_re - spec_im * filter_im, spec_re * filter_im + spec_im * filter_re], 1
    ).astype(jnp.bfloat16)
    mixed_back = lax.dot_general(
        filtered, forward_transform, (((1,), (1,)), ((), ())), preferred_element_type=jnp.float32
    )
    hidden = (mixed_in.astype(jnp.float32) + jax.nn.gelu(mixed_back)).astype(jnp.bfloat16)
    rebuilt = hidden.astype(jnp.float32) + jnp.dot(
        hidden, output_weight, preferred_element_type=jnp.float32
    )
    residual = loss_scale * (rebuilt - wanted_lines.astype(jnp.float32))
    residual_half = residual.astype(jnp.bfloat16)
    grad_out = lax.dot_general(
        hidden, residual_half, (((0,), (0,)), ((), ())), preferred_element_type=jnp.float32
    )
    grad_hidden = residual + lax.dot_general(
        residual_half, output_weight, (((1,), (1,)), ((), ())), preferred_element_type=jnp.float32
    )
    grad_mixed = jax.vjp(jax.nn.gelu, mixed_back)[1](grad_hidden)[0].astype(jnp.bfloat16)
    grad_filtered = jnp.dot(grad_mixed, forward_transform, preferred_element_type=jnp.float32)
    grad_re = grad_filtered[:, :half_width]
    grad_im = grad_filtered[:, half_width:]
    grad_filter = jnp.stack(
        [
            jnp.sum(grad_re * spec_re + grad_im * spec_im, 0),
            jnp.sum(grad_im * spec_re - grad_re * spec_im, 0),
        ]
    )
    grad_spec = jnp.concatenate(
        [grad_re * filter_re + grad_im * filter_im, grad_im * filter_re - grad_re * filter_im], 1
    ).astype(jnp.bfloat16)
    derivative_entering = grad_hidden + lax.dot_general(
        grad_spec, forward_transform, (((1,), (1,)), ((), ())), preferred_element_type=jnp.float32
    )
    return (derivative_entering, grad_out, grad_filter)


def encoder_grads(inputs_rows, codewords, latent_sums, decoder_weight):
    latent_half = latent_sums.astype(jnp.bfloat16)
    grad_dec = lax.dot_general(
        codewords, latent_half, (((0,), (0,)), ((), ())), preferred_element_type=jnp.float32
    )
    grad_codes = lax.dot_general(
        latent_half, decoder_weight, (((1,), (1,)), ((), ())), preferred_element_type=jnp.float32
    )
    grad_pre = (grad_codes * (1.0 - jnp.square(codewords.astype(jnp.float32)))).astype(jnp.bfloat16)
    grad_enc = lax.dot_general(
        inputs_rows, grad_pre, (((0,), (0,)), ((), ())), preferred_element_type=jnp.float32
    )
    return (grad_enc, grad_dec)


def _exchange_pairs(count, distance):
    return [(i, i ^ distance) for i in range(count)]


def _is_power_of_two(count):
    return count > 0 and count & (count - 1) == 0


def gather_rows(block, axis_name):
    count = lax.axis_size(axis_name)
    if not _is_power_of_two(count):
        return lax.all_gather(block, axis_name, axis=0, tiled=True)
    position = lax.axis_index(axis_name)
    distance = count // 2
    while distance >= 1:
        other = lax.ppermute(block, axis_name, _exchange_pairs(count, distance))
        lower = (position // distance) % 2 == 0
        block = jnp.where(
            lower, jnp.concatenate([block, other], 0), jnp.concatenate([other, block], 0)
        )
        distance //= 2
    return block


def bit_reversed_blocks(values, count):
    if not _is_power_of_two(count):
        return values
    bits = count.bit_length() - 1
    blocks = values.reshape((2,) * bits + (-1,))
    return blocks.transpose(tuple(reversed(range(bits))) + (bits,)).reshape(-1)


def sum_whole(values, axis_name):
    count = lax.axis_size(axis_name)
    if not _is_power_of_two(count):
        return lax.psum(values, axis_name)
    distance = 1
    while distance < count:
        values = values + lax.ppermute(values, axis_name, _exchange_pairs(count, distance))
        distance *= 2
    return values


def sum_halving(values, axis_name, wire=jnp.bfloat16, halving_levels=2, trailing=None):
    count = lax.axis_size(axis_name)
    if not _is_power_of_two(count) or values.shape[0] % min(count, 2**halving_levels) != 0:
        if trailing is not None:
            return lax.psum(values, axis_name), trailing
        return lax.psum(values, axis_name)
    position = lax.axis_index(axis_name)
    distance = 1
    while distance < count and distance < 2**halving_levels:
        half = values.shape[0] // 2
        lower = (position // distance) % 2 == 0
        keep = jnp.where(lower, values[:half], values[half:])
        send = jnp.where(lower, values[half:], values[:half]).astype(wire)
        arrived = lax.ppermute(send, axis_name, _exchange_pairs(count, distance))
        values = keep + arrived.astype(keep.dtype)
        if distance == 2 and trailing is not None:
            values, trailing = lax.optimization_barrier((values, trailing))
        distance *= 2
    top = distance
    values = values.astype(wire)
    while distance < count:
        arrived = lax.ppermute(values, axis_name, _exchange_pairs(count, distance))
        values = (values.astype(jnp.float32) + arrived.astype(jnp.float32)).astype(wire)
        distance *= 2
    distance = top // 2
    while distance >= 1:
        other = lax.ppermute(values, axis_name, _exchange_pairs(count, distance))
        lower = (position // distance) % 2 == 0
        values = jnp.where(
            lower, jnp.concatenate([values, other], 0), jnp.concatenate([other, values], 0)
        )
        distance //= 2
    if trailing is not None:
        return values, trailing
    return values


def local(
    encoder_input,
    desired_responses,
    sample_index,
    encoder_weight,
    decoder_weight,
    frequency_amplitude,
    spectral_filter_weight,
    output_weight,
):
    samples = sample_index.shape[0]
    sub_dev = desired_responses.shape[1]
    width = desired_responses.shape[2]
    forward_transform, inverse_transform = rotation_tables(width // 2)
    loss_scale = 1.0 / math.sqrt(samples * sub_dev * lax.axis_size("freq"))
    all_inputs = gather_rows(encoder_input, "freq")
    gathered_index = bit_reversed_blocks(sample_index, lax.axis_size("freq"))
    selection = (
        gathered_index[None, :] == jnp.arange(samples, dtype=jnp.int32)[:, None]
    ).astype(jnp.bfloat16)
    inputs_by_sample = jnp.dot(selection, all_inputs, preferred_element_type=jnp.float32).astype(
        jnp.bfloat16
    )
    codes_by_sample = jnp.tanh(
        jnp.dot(inputs_by_sample, encoder_weight, preferred_element_type=jnp.float32)
    ).astype(jnp.bfloat16)
    latent = jnp.dot(codes_by_sample, decoder_weight, preferred_element_type=jnp.float32)
    gain_row_values = frequency_amplitude.astype(jnp.float32)
    mixed_in = (latent[:, None, :] * gain_row_values[None]).astype(jnp.bfloat16).reshape(-1, width)
    wanted_lines = desired_responses.reshape(-1, width)
    derivative_entering, grad_out, grad_filter = decode_rows(
        mixed_in,
        wanted_lines,
        output_weight,
        spectral_filter_weight,
        forward_transform,
        inverse_transform,
        loss_scale,
    )
    derivative_bottleneck = jnp.einsum(
        "orm,rm->om", derivative_entering.reshape(samples, sub_dev, width), gain_row_values
    )
    half_width = grad_filter.shape[1]
    filter_rows = jnp.concatenate(
        [grad_filter, jnp.zeros((grad_filter.shape[0], width - half_width), jnp.float32)], 1
    )
    rows_out = grad_out.shape[0]
    small_rows = samples + filter_rows.shape[0]
    packed_rows = rows_out + small_rows
    padding = -packed_rows % 8
    packed = jnp.concatenate(
        [
            derivative_bottleneck,
            filter_rows,
            grad_out,
            jnp.zeros((padding, width), jnp.float32),
        ],
        0,
    )
    rows_each = packed.shape[0] // 2
    first, second_input = sum_halving(packed[:rows_each], "freq", trailing=packed[rows_each:])
    second = sum_halving(second_input, "freq")
    derivative_bottleneck = first[:samples].astype(jnp.float32)
    grad_filter = first[samples:small_rows, :half_width].astype(jnp.float32)
    grad_out = jnp.concatenate([first[small_rows:], second], 0)[:rows_out].astype(jnp.float32)
    grad_enc, grad_dec = encoder_grads(
        inputs_by_sample, codes_by_sample, derivative_bottleneck, decoder_weight
    )
    return (grad_enc, grad_dec, grad_out, grad_filter)


def solution(mesh):
    return jax.shard_map(
        local,
        mesh=mesh,
        in_specs=(
            P(("groups", "freq"), None),
            P("groups", "freq", None),
            P("groups"),
            P(),
            P(),
            P("freq", None),
            P(),
            P(),
        ),
        out_specs=(P("groups", None), P("groups", None), P("groups", None), P("groups", None)),
        check_vma=False,
    )
```
